32 devices in a mesh: space: 16 (over z, y, x), ray: 2 (over core).
Axes of the slice: x: 2, y: 2, z: 4, core: 2. Of those that a mesh axis runs over, the one named last changes fastest.
Arguments:
- positions: float32 [3, 512, 256], P(None, ('space', 'ray')), may hold values from -1 to 1
- spacing: float32 [512, 256], P(('space', 'ray')), may hold values from 0.003 to 0.03
- assign: int32 [512, 8, 1], P(('space', 'ray')), may hold values from 0 to 15; in each aligned block of 128 rows (0 to 127, 128 to 255, ..., all dimensions but the last counted through in order) at most 12 rows name the same one
- depth_rank: int32 [512, 8], P(('space', 'ray')), may hold values from 0 to 7, each once within a row
- pixel_grad: float32 [3, 512], P(None, ('space', 'ray')), may hold values from -96 to 96
- fourier: float32 [3, 128], replicated, may hold values from -4 to 4
- first_weight: bfloat16 [16, 256, 256], P('space'), may hold values from -0.375 to 0.375
- first_bias: float32 [16, 256], P('space'), may hold values from -3 to 3
- second_weight: bfloat16 [16, 256, 256], P('space'), may hold values from -0.375 to 0.375
- second_bias: float32 [16, 256], P('space'), may hold values from -3 to 3
- head_weight: bfloat16 [16, 4, 256], P('space'), may hold values from -0.375 to 0.375
- head_bias: float32 [16, 4], P('space'), may hold values from -3 to 3
Outputs:
- grad_first: float32 [16, 256, 256], P('space', 'ray')
- grad_second: float32 [16, 256, 256], P('space', 'ray')
- grad_head: float32 [16, 4, 256], P('space')
- grad_first_bias: float32 [16, 256], P('space')
- grad_second_bias: float32 [16, 256], P('space')
- grad_head_bias: float32 [16, 4], P('space')
The draws below stay inside these ranges and needn't reach their ends.
Inputs may be any that keep to these rules, and one draw needn't show every extreme that they name: `assign`: within the segments of one device (aligned blocks of 128 rows in ray order), no partition is named more than 12 times. `depth_rank`: each ray's row names every place 0 to 7 once.
All inputs are finite; a program needn't handle non-finite values.
Results may differ from the reference program's by a relative error of at most 0.0053.
Values sent between devices are 32-bit elements; how exact they have to be, the bound alone decides.
No kernel may reach another device: no remote copies, remote signals or barrier semaphores. Data moves between devices by JAX's collectives and lax.ppermute only.
A program may use at most 64 MiB of HBM per device.

```python
import math
import jax
import jax.numpy as jnp
import numpy as np
from jax import lax

FREQS = 128
FEAT = 256
HID = 256
SEG_LEN = 32
SEGS = 8
RAY_DEV = 16
ZONES = 16
RAYS = 512
CAP = 12
SLOTS = 192
N_RAY = 2


def shard_levels(key, dims, shards, least, largest):
    loudness, own = 1.0, jax.random.fold_in(key, 6)
    for axis_at, parts in shards:
        steps = jnp.exp(jax.random.uniform(jax.random.fold_in(own, axis_at), (parts,), jnp.float32, least / len(shards), largest / len(shards)))
        loudness = loudness * jnp.repeat(steps, dims[axis_at] // parts).reshape([-1 if axis == axis_at else 1 for axis in range(len(dims))])
    return loudness


def shared_out(rng, own, number, rows, number_of, top, most, skew):
    ranking = jax.random.permutation(rng, number_of)
    crowded, usual = shares(number_of, rows * top, most, skew, True), shares(number_of, rows * top, most, skew, False)
    places = jnp.arange(number_of)

    def named(sizes, offset_by):
        used = int((sizes > 0).sum())
        fixed = max(1, used // 4)
        shifted = fixed + (places - fixed + offset_by * (used - fixed)) % max(1, number_of - fixed)
        return jnp.zeros((number_of,), jnp.int32).at[ranking[jnp.where(places < fixed, places, shifted)]].set(jnp.asarray(sizes, jnp.int32))

    sizes = jnp.where(number % 4 == 0, named(crowded, number // 4), named(usual, number - number // 4 - 1))
    mixed = jax.random.permutation(jax.random.fold_in(own, 3), number_of)
    source_of, sink = mixed[0:number_of // 2 * 2:2], mixed[1:number_of // 2 * 2:2]
    room = jnp.minimum(sizes[source_of] - 1, most - sizes[sink]) // 2
    room = jnp.where((source_of == ranking[0]) | (sink == ranking[0]) | (sizes[sink] == 0), 0, jnp.maximum(room, 0))
    shifted = jax.random.randint(jax.random.fold_in(own, 4), (number_of // 2,), 0, 1 << 20) % (room + 1)
    sizes = sizes.at[source_of].add(-shifted).at[sink].add(shifted)
    labels = jnp.searchsorted(jnp.cumsum(sizes), jnp.arange(rows * top), side="right").astype(jnp.int32)
    listing = labels.reshape(top, rows).T
    listing = listing[jax.random.permutation(jax.random.fold_in(own, 1), rows)]
    offset_by = jax.random.randint(jax.random.fold_in(own, 2), (rows, 1), 0, top)
    return jnp.take_along_axis(listing, (jnp.arange(top)[None, :] + offset_by) % top, axis=1)


def shares(number_of, total, limit, slope, full):
    loads = [(1 << 20) // math.isqrt(standing ** slope) + 1 for standing in range(1, number_of + 1)]
    largest = limit if full else min(limit, max(-(-total // number_of), total * loads[0] // sum(loads)))
    least = 1 if total - largest >= number_of - 1 else 0
    counts, rest = [largest] + [least] * (number_of - 1), total - largest - least * (number_of - 1)
    while rest > 0:
        movable = [i for i in range(1, number_of) if counts[i] < largest] or [i for i in range(1, number_of) if counts[i] < limit]
        pool, budget = sum([loads[i] for i in movable]), rest
        for i in movable:
            extra = min(limit - counts[i], max(1, budget * loads[i] // pool), rest)
            counts[i] = counts[i] + extra
            rest = rest - extra
    return np.array(counts)


def centred(key, shape, width, most, pieces=(), held_as=jnp.bfloat16):
    drawn = width * jax.random.normal(key, shape, jnp.float32)
    if pieces:
        drawn = drawn * shard_levels(key, shape, pieces, -0.22, 0.18)
    return jnp.clip(drawn, -most, most).astype(held_as)


def setup_inputs(seed: int = 0) -> dict:
    seeds = jax.random.split(jax.random.key(seed), 13)
    positions = jnp.clip(jax.random.uniform(seeds[0], (3, RAYS, SEGS * SEG_LEN), jnp.float32, -1.0, 1.0) * shard_levels(seeds[0], (3, RAYS, SEGS * SEG_LEN), ((1, 32),), -0.4, 0.0), -1.0, 1.0)
    spacing = jnp.clip(jnp.exp(math.log(0.03) - 2.3025851 * jax.random.uniform(seeds[1], (RAYS, SEGS * SEG_LEN), jnp.float32) ** shard_levels(seeds[1], (RAYS, SEGS * SEG_LEN), ((0, 32),), -0.2, 0.2)), 0.003, 0.03)
    assign_keys = jax.random.split(jax.random.fold_in(seeds[2], 1), RAYS * SEGS // (RAY_DEV * SEGS))
    assign_turns = jax.random.permutation(jax.random.fold_in(seeds[2], 3), RAYS * SEGS // (RAY_DEV * SEGS))
    assign = jax.vmap(lambda own, number: shared_out(jax.random.fold_in(seeds[2], 2), own, number, RAY_DEV * SEGS, ZONES, 1, CAP, 2))(assign_keys, assign_turns).reshape((RAYS, SEGS, 1))
    depth_rank = jax.vmap(lambda own: jax.random.permutation(own, SEGS))(jax.random.split(seeds[3], RAYS)).reshape((RAYS, SEGS)).astype(jnp.int32)
    pixel_grad = centred(seeds[4], (3, RAYS), 16.0, 96.0, ((1, 32),), jnp.float32)
    fourier = centred(seeds[5], (3, FREQS), 1.0, 4.0, (), jnp.float32)
    first_weight = centred(seeds[6], (ZONES, FEAT, HID), FEAT ** -0.5, 0.375, ((0, 16),))
    first_bias = centred(seeds[7], (ZONES, HID), 0.5, 3.0, ((0, 16),), jnp.float32)
    second_weight = centred(seeds[8], (ZONES, HID, HID), HID ** -0.5, 0.375, ((0, 16),))
    second_bias = centred(seeds[9], (ZONES, HID), 0.5, 3.0, ((0, 16),), jnp.float32)
    head_weight = centred(seeds[10], (ZONES, 4, HID), HID ** -0.5, 0.375, ((0, 16),))
    head_bias = centred(seeds[11], (ZONES, 4), 1.0, 3.0, ((0, 16),), jnp.float32)
    return dict(positions=positions, spacing=spacing, assign=assign, depth_rank=depth_rank, pixel_grad=pixel_grad, fourier=fourier, first_weight=first_weight, first_bias=first_bias, second_weight=second_weight, second_bias=second_bias, head_weight=head_weight, head_bias=head_bias)


two_pi = 6.283185307179586


def silu_slope(value):
    gate = jax.nn.sigmoid(value)
    return gate * (1.0 + value * (1.0 - gate))


def encode(samples, fourier):
    phases = two_pi * (samples[:, 0, :, None] * fourier[0] + samples[:, 1, :, None] * fourier[1] + samples[:, 2, :, None] * fourier[2])
    joined = jnp.concatenate([jnp.sin(phases), jnp.cos(phases)], axis=-1)
    return joined.astype(jnp.bfloat16).reshape(-1, joined.shape[-1])


def network(samples, fourier, params):
    first_weight, first_bias, second_weight, second_bias, head_weight, head_bias = params
    seg_count, length = samples.shape[0], samples.shape[2]
    encoded = encode(samples, fourier)
    pre_first = jnp.dot(encoded, first_weight, preferred_element_type=jnp.float32) + first_bias
    act_first = jax.nn.silu(pre_first).astype(jnp.bfloat16)
    pre_second = jnp.dot(act_first, second_weight, preferred_element_type=jnp.float32) + second_bias
    act_second = jax.nn.silu(pre_second).astype(jnp.bfloat16)
    head_raw = lax.dot_general(act_second, head_weight, (((1,), (1,)), ((), ())), preferred_element_type=jnp.float32) + head_bias
    head_raw = head_raw.reshape(seg_count, length, 4)
    density = jax.nn.softplus(head_raw[..., 0])
    colour = jax.nn.sigmoid(head_raw[..., 1:])
    optical = density * samples[:, 3, :]
    inclusive = jnp.cumsum(optical, axis=1)
    enter_light = jnp.exp(optical - inclusive)
    leave_light = jnp.exp(-inclusive)
    weight = enter_light - leave_light
    seg_colour = jnp.sum(weight[..., None] * colour, axis=1)
    seg_log = -inclusive[:, -1]
    saved = (encoded, pre_first, act_first, pre_second, act_second, head_raw, colour, weight, leave_light)
    return seg_colour, seg_log, saved


def backward(samples, fourier, params, up_colour, up_log):
    first_weight, first_bias, second_weight, second_bias, head_weight, head_bias = params
    unused_colour, unused_log, saved = network(samples, fourier, params)
    encoded, pre_first, act_first, pre_second, act_second, head_raw, colour, weight, leave_light = saved
    energy = jnp.sum(colour * up_colour[:, None, :], axis=-1)
    spent = weight * energy
    remaining = jnp.sum(spent, axis=1, keepdims=True) - jnp.cumsum(spent, axis=1)
    grad_optical = leave_light * energy - remaining - up_log[:, None]
    grad_density = grad_optical * samples[:, 3, :] * jax.nn.sigmoid(head_raw[..., 0])
    grad_tint = weight[..., None] * up_colour[:, None, :] * colour * (1.0 - colour)
    grad_raw = jnp.concatenate([grad_density[..., None], grad_tint], axis=-1).reshape(-1, 4).astype(jnp.bfloat16)
    grad_head = lax.dot_general(grad_raw, act_second, (((0,), (0,)), ((), ())), preferred_element_type=jnp.float32)
    grad_head_bias = jnp.sum(grad_raw.astype(jnp.float32), axis=0)
    back_second = jnp.dot(grad_raw, head_weight, preferred_element_type=jnp.float32)
    delta_second = (back_second * silu_slope(pre_second)).astype(jnp.bfloat16)
    grad_second = lax.dot_general(act_first, delta_second, (((0,), (0,)), ((), ())), preferred_element_type=jnp.float32)
    grad_second_bias = jnp.sum(delta_second.astype(jnp.float32), axis=0)
    back_first = lax.dot_general(delta_second, second_weight, (((1,), (1,)), ((), ())), preferred_element_type=jnp.float32)
    delta_first = (back_first * silu_slope(pre_first)).astype(jnp.bfloat16)
    grad_first = lax.dot_general(encoded, delta_first, (((0,), (0,)), ((), ())), preferred_element_type=jnp.float32)
    grad_first_bias = jnp.sum(delta_first.astype(jnp.float32), axis=0)
    return grad_first, grad_second, grad_head, grad_first_bias, grad_second_bias, grad_head_bias


def composite(seg_colour, seg_log, depth_rank, pixel_rows):
    before = (depth_rank[:, None, :] < depth_rank[:, :, None]).astype(jnp.float32)
    prefix = jnp.exp(jnp.sum(before * seg_log[:, None, :], axis=2))
    up_colour = prefix[..., None] * pixel_rows[:, None, :]
    shaded = prefix * jnp.sum(seg_colour * pixel_rows[:, None, :], axis=2)
    up_log = jnp.sum(before * shaded[:, :, None], axis=1)
    return up_colour, up_log


def reference(positions, spacing, assign, depth_rank, pixel_grad, fourier, first_weight, first_bias, second_weight, second_bias, head_weight, head_bias):
    total = RAYS * SEGS
    span = N_RAY * SLOTS
    owner = assign.reshape(total).astype(jnp.int32)
    sorted_ids = jnp.argsort(owner, stable=True).astype(jnp.int32)
    tally = jnp.zeros((ZONES,), jnp.int32).at[owner].add(1)
    starts = (jnp.cumsum(tally) - tally).astype(jnp.int32)
    column = jnp.arange(span, dtype=jnp.int32)
    place = jnp.minimum(starts[:, None] + column[None, :], total - 1).astype(jnp.int32)
    table = jnp.where(column[None, :] < tally[:, None], sorted_ids[place], total).astype(jnp.int32)
    seg_pos = jnp.transpose(positions.reshape(3, total, SEG_LEN), (1, 0, 2))
    seg_gap = spacing.reshape(total, 1, SEG_LEN)
    segments = jnp.concatenate([seg_pos, seg_gap], axis=1)
    padded = jnp.concatenate([segments, jnp.zeros((1, 4, SEG_LEN), jnp.float32)], axis=0)
    params = (first_weight, first_bias, second_weight, second_bias, head_weight, head_bias)

    def first_pass(index):
        chosen = padded[table[index]]
        weights = tuple(item[index] for item in params)
        seg_colour, seg_log, unused = network(chosen, fourier, weights)
        return seg_colour, seg_log

    part_colour, part_log = lax.map(first_pass, jnp.arange(ZONES, dtype=jnp.int32))
    flat_table = table.reshape(-1)
    all_colour = jnp.zeros((total + 1, 3), jnp.float32).at[flat_table].set(part_colour.reshape(-1, 3))[:total]
    all_log = jnp.zeros((total + 1,), jnp.float32).at[flat_table].set(part_log.reshape(-1))[:total]
    up_colour, up_log = composite(all_colour.reshape(RAYS, SEGS, 3), all_log.reshape(RAYS, SEGS), depth_rank, pixel_grad.T)
    upstream = jnp.concatenate([up_colour.reshape(total, 3), up_log.reshape(total, 1)], axis=1)
    upstream = jnp.concatenate([upstream, jnp.zeros((1, 4), jnp.float32)], axis=0)

    def second_pass(index):
        chosen = padded[table[index]]
        gathered = upstream[table[index]]
        weights = tuple(item[index] for item in params)
        return backward(chosen, fourier, weights, gathered[:, :3], gathered[:, 3])

    grads = lax.map(second_pass, jnp.arange(ZONES, dtype=jnp.int32))
    return (grads[0], grads[1], grads[2], grads[3], grads[4], grads[5])
```

```python
import jax
import jax.numpy as jnp
from jax import lax
from jax.sharding import PartitionSpec as P

SEG_LEN = 32
SEGS = 8


two_pi = 6.283185307179586


def silu_slope(value):
    gate = jax.nn.sigmoid(value)
    return gate * (1.0 + value * (1.0 - gate))


def encode(samples, fourier):
    phases = two_pi * (
        samples[:, 0, :, None] * fourier[0]
        + samples[:, 1, :, None] * fourier[1]
        + samples[:, 2, :, None] * fourier[2]
    )
    joined = jnp.concatenate([jnp.sin(phases), jnp.cos(phases)], axis=-1)
    return joined.astype(jnp.bfloat16).reshape(-1, joined.shape[-1])


def network(samples, fourier, params):
    first_weight, first_bias, second_weight, second_bias, head_weight, head_bias = params
    seg_count, length = (samples.shape[0], samples.shape[2])
    encoded = encode(samples, fourier)
    pre_first = jnp.dot(encoded, first_weight, preferred_element_type=jnp.float32) + first_bias
    act_first = jax.nn.silu(pre_first).astype(jnp.bfloat16)
    pre_second = jnp.dot(act_first, second_weight, preferred_element_type=jnp.float32) + second_bias
    act_second = jax.nn.silu(pre_second).astype(jnp.bfloat16)
    head_raw = (
        lax.dot_general(
            act_second, head_weight, (((1,), (1,)), ((), ())), preferred_element_type=jnp.float32
        )
        + head_bias
    )
    head_raw = head_raw.reshape(seg_count, length, 4)
    density = jax.nn.softplus(head_raw[..., 0])
    colour = jax.nn.sigmoid(head_raw[..., 1:])
    optical = density * samples[:, 3, :]
    inclusive = jnp.cumsum(optical, axis=1)
    enter_light = jnp.exp(optical - inclusive)
    leave_light = jnp.exp(-inclusive)
    weight = enter_light - leave_light
    seg_colour = jnp.sum(weight[..., None] * colour, axis=1)
    seg_log = -inclusive[:, -1]
    saved = (
        encoded,
        pre_first,
        act_first,
        pre_second,
        act_second,
        head_raw,
        colour,
        weight,
        leave_light,
    )
    return (seg_colour, seg_log, saved)


def backward(samples, params, saved, up_colour, up_log):
    first_weight, first_bias, second_weight, second_bias, head_weight, head_bias = params
    encoded, pre_first, act_first, pre_second, act_second, head_raw, colour, weight, leave_light = (
        saved
    )
    energy = jnp.sum(colour * up_colour[:, None, :], axis=-1)
    spent = weight * energy
    remaining = jnp.sum(spent, axis=1, keepdims=True) - jnp.cumsum(spent, axis=1)
    grad_optical = leave_light * energy - remaining - up_log[:, None]
    grad_density = grad_optical * samples[:, 3, :] * jax.nn.sigmoid(head_raw[..., 0])
    grad_tint = weight[..., None] * up_colour[:, None, :] * colour * (1.0 - colour)
    grad_raw = (
        jnp.concatenate([grad_density[..., None], grad_tint], axis=-1)
        .reshape(-1, 4)
        .astype(jnp.bfloat16)
    )
    grad_head = lax.dot_general(
        grad_raw, act_second, (((0,), (0,)), ((), ())), preferred_element_type=jnp.float32
    )
    grad_head_bias = jnp.sum(grad_raw.astype(jnp.float32), axis=0)
    back_second = jnp.dot(grad_raw, head_weight, preferred_element_type=jnp.float32)
    delta_second = (back_second * silu_slope(pre_second)).astype(jnp.bfloat16)
    grad_second = lax.dot_general(
        act_first, delta_second, (((0,), (0,)), ((), ())), preferred_element_type=jnp.float32
    )
    grad_second_bias = jnp.sum(delta_second.astype(jnp.float32), axis=0)
    back_first = lax.dot_general(
        delta_second, second_weight, (((1,), (1,)), ((), ())), preferred_element_type=jnp.float32
    )
    delta_first = (back_first * silu_slope(pre_first)).astype(jnp.bfloat16)
    grad_first = lax.dot_general(
        encoded, delta_first, (((0,), (0,)), ((), ())), preferred_element_type=jnp.float32
    )
    grad_first_bias = jnp.sum(delta_first.astype(jnp.float32), axis=0)
    return (grad_first, grad_second, grad_head, grad_first_bias, grad_second_bias, grad_head_bias)


def composite(seg_colour, seg_log, depth_rank, pixel_rows):
    before = (depth_rank[:, None, :] < depth_rank[:, :, None]).astype(jnp.float32)
    prefix = jnp.exp(jnp.sum(before * seg_log[:, None, :], axis=2))
    up_colour = prefix[..., None] * pixel_rows[:, None, :]
    shaded = prefix * jnp.sum(seg_colour * pixel_rows[:, None, :], axis=2)
    up_log = jnp.sum(before * shaded[:, :, None], axis=1)
    return (up_colour, up_log)


def per_device(
    positions,
    spacing,
    assign,
    depth_rank,
    pixel_grad,
    fourier,
    first_weight,
    first_bias,
    second_weight,
    second_bias,
    head_weight,
    head_bias,
):
    groups = lax.axis_size("space")
    ray_count = positions.shape[1]
    total = ray_count * SEGS
    capacity = 3 * total // (2 * groups)
    slot_count = capacity * groups
    owner = assign.reshape(total)
    member = (owner[:, None] == jnp.arange(groups, dtype=jnp.int32)[None, :]).astype(jnp.int32)
    earlier = jnp.cumsum(member, axis=0) - member
    within = jnp.sum(earlier * member, axis=1)
    target = owner * capacity + within
    dispatch = (target[:, None] == jnp.arange(slot_count, dtype=jnp.int32)[None, :]).astype(
        jnp.float32
    )
    seg_pos = jnp.transpose(positions.reshape(3, total, SEG_LEN), (1, 0, 2))
    seg_gap = spacing.reshape(total, 1, SEG_LEN)
    segments = jnp.concatenate([seg_pos, seg_gap], axis=1).reshape(total, 4 * SEG_LEN)
    outgoing = lax.dot_general(
        dispatch,
        segments,
        (((0,), (0,)), ((), ())),
        precision=lax.Precision.HIGHEST,
        preferred_element_type=jnp.float32,
    )
    outgoing = outgoing.reshape(groups, capacity, 4 * SEG_LEN)
    arrived = lax.all_to_all(outgoing, "space", split_axis=0, concat_axis=0, tiled=True)
    samples = arrived.reshape(slot_count, 4, SEG_LEN)
    params = tuple(
        (
            item[0]
            for item in (
                first_weight,
                first_bias,
                second_weight,
                second_bias,
                head_weight,
                head_bias,
            )
        )
    )
    seg_colour, seg_log, saved = network(samples, fourier, params)
    partials = jnp.concatenate([seg_colour.T, seg_log[None, :]], axis=0).reshape(
        4, groups, capacity
    )
    returned = lax.all_to_all(partials, "space", split_axis=1, concat_axis=1, tiled=True).reshape(
        4, slot_count
    )
    mine = lax.dot_general(
        dispatch,
        returned,
        (((1,), (1,)), ((), ())),
        precision=lax.Precision.HIGHEST,
        preferred_element_type=jnp.float32,
    )
    up_colour, up_log = composite(
        mine[:, :3].reshape(ray_count, SEGS, 3),
        mine[:, 3].reshape(ray_count, SEGS),
        depth_rank,
        pixel_grad.T,
    )
    upstream = jnp.concatenate([up_colour.reshape(total, 3), up_log.reshape(total, 1)], axis=1)
    sendback = lax.dot_general(
        upstream,
        dispatch,
        (((0,), (0,)), ((), ())),
        precision=lax.Precision.HIGHEST,
        preferred_element_type=jnp.float32,
    )
    sendback = sendback.reshape(4, groups, capacity)
    received = lax.all_to_all(sendback, "space", split_axis=1, concat_axis=1, tiled=True)
    received = received.reshape(4, slot_count).T
    totals = backward(samples, params, saved, received[:, :3], received[:, 3])
    grad_first, grad_second, grad_head, bias_first, bias_second, bias_head = totals
    small_sums = lax.psum((grad_head, bias_first, bias_second, bias_head), "ray")
    whole_first, whole_second = lax.psum((grad_first, grad_second), "ray")
    replicas = lax.axis_size("ray")
    position = lax.axis_index("ray")
    rows_first = whole_first.shape[0] // replicas
    rows_second = whole_second.shape[0] // replicas
    part_first = lax.dynamic_slice_in_dim(whole_first, position * rows_first, rows_first, 0)
    part_second = lax.dynamic_slice_in_dim(whole_second, position * rows_second, rows_second, 0)
    return (
        part_first[None],
        part_second[None],
        small_sums[0][None],
        small_sums[1][None],
        small_sums[2][None],
        small_sums[3][None],
    )


def solution(mesh):
    placed = (
        P(None, ("space", "ray"), None),
        P(("space", "ray"), None),
        P(("space", "ray"), None, None),
        P(("space", "ray"), None),
        P(None, ("space", "ray")),
        P(),
        P("space", None, None),
        P("space", None),
        P("space", None, None),
        P("space", None),
        P("space", None, None),
        P("space", None),
    )
    return jax.shard_map(
        per_device,
        mesh=mesh,
        in_specs=placed,
        out_specs=(
            P("space", "ray", None),
            P("space", "ray", None),
            P("space", None, None),
            P("space", None),
            P("space", None),
            P("space", None),
        ),
        check_vma=False,
    )
```

```python
import jax
import jax.numpy as jnp
from jax import lax
from jax.sharding import PartitionSpec as P

SEG_LEN = 32
SEGS = 8


two_pi = 6.283185307179586


def silu_slope(value):
    gate = jax.nn.sigmoid(value)
    return gate * (1.0 + value * (1.0 - gate))


def encode(samples, fourier):
    phases = two_pi * (
        samples[:, 0, :, None] * fourier[0]
        + samples[:, 1, :, None] * fourier[1]
        + samples[:, 2, :, None] * fourier[2]
    )
    joined = jnp.concatenate([jnp.sin(phases), jnp.cos(phases)], axis=-1)
    return joined.astype(jnp.bfloat16).reshape(-1, joined.shape[-1])


def network(samples, fourier, params):
    first_weight, first_bias, second_weight, second_bias, head_weight, head_bias = params
    seg_count, length = (samples.shape[0], samples.shape[2])
    encoded = encode(samples, fourier)
    pre_first = jnp.dot(encoded, first_weight, preferred_element_type=jnp.float32) + first_bias
    act_first = jax.nn.silu(pre_first).astype(jnp.bfloat16)
    pre_second = jnp.dot(act_first, second_weight, preferred_element_type=jnp.float32) + second_bias
    act_second = jax.nn.silu(pre_second).astype(jnp.bfloat16)
    head_raw = (
        lax.dot_general(
            act_second, head_weight, (((1,), (1,)), ((), ())), preferred_element_type=jnp.float32
        )
        + head_bias
    )
    head_raw = head_raw.reshape(seg_count, length, 4)
    density = jax.nn.softplus(head_raw[..., 0])
    colour = jax.nn.sigmoid(head_raw[..., 1:])
    optical = density * samples[:, 3, :]
    inclusive = jnp.cumsum(optical, axis=1)
    enter_light = jnp.exp(optical - inclusive)
    leave_light = jnp.exp(-inclusive)
    weight = enter_light - leave_light
    seg_colour = jnp.sum(weight[..., None] * colour, axis=1)
    seg_log = -inclusive[:, -1]
    saved = (
        encoded,
        pre_first,
        act_first,
        pre_second,
        act_second,
        head_raw,
        colour,
        weight,
        leave_light,
    )
    return (seg_colour, seg_log, saved)


def backward(samples, params, saved, up_colour, up_log):
    first_weight, first_bias, second_weight, second_bias, head_weight, head_bias = params
    encoded, pre_first, act_first, pre_second, act_second, head_raw, colour, weight, leave_light = (
        saved
    )
    energy = jnp.sum(colour * up_colour[:, None, :], axis=-1)
    spent = weight * energy
    remaining = jnp.sum(spent, axis=1, keepdims=True) - jnp.cumsum(spent, axis=1)
    grad_optical = leave_light * energy - remaining - up_log[:, None]
    grad_density = grad_optical * samples[:, 3, :] * jax.nn.sigmoid(head_raw[..., 0])
    grad_tint = weight[..., None] * up_colour[:, None, :] * colour * (1.0 - colour)
    grad_raw = (
        jnp.concatenate([grad_density[..., None], grad_tint], axis=-1)
        .reshape(-1, 4)
        .astype(jnp.bfloat16)
    )
    grad_head = lax.dot_general(
        grad_raw, act_second, (((0,), (0,)), ((), ())), preferred_element_type=jnp.float32
    )
    grad_head_bias = jnp.sum(grad_raw.astype(jnp.float32), axis=0)
    back_second = jnp.dot(grad_raw, head_weight, preferred_element_type=jnp.float32)
    delta_second = (back_second * silu_slope(pre_second)).astype(jnp.bfloat16)
    grad_second = lax.dot_general(
        act_first, delta_second, (((0,), (0,)), ((), ())), preferred_element_type=jnp.float32
    )
    grad_second_bias = jnp.sum(delta_second.astype(jnp.float32), axis=0)
    back_first = lax.dot_general(
        delta_second, second_weight, (((1,), (1,)), ((), ())), preferred_element_type=jnp.float32
    )
    delta_first = (back_first * silu_slope(pre_first)).astype(jnp.bfloat16)
    grad_first = lax.dot_general(
        encoded, delta_first, (((0,), (0,)), ((), ())), preferred_element_type=jnp.float32
    )
    grad_first_bias = jnp.sum(delta_first.astype(jnp.float32), axis=0)
    return (grad_first, grad_second, grad_head, grad_first_bias, grad_second_bias, grad_head_bias)


def composite(seg_colour, seg_log, depth_rank, pixel_rows):
    before = (depth_rank[:, None, :] < depth_rank[:, :, None]).astype(jnp.float32)
    prefix = jnp.exp(jnp.sum(before * seg_log[:, None, :], axis=2))
    up_colour = prefix[..., None] * pixel_rows[:, None, :]
    shaded = prefix * jnp.sum(seg_colour * pixel_rows[:, None, :], axis=2)
    up_log = jnp.sum(before * shaded[:, :, None], axis=1)
    return (up_colour, up_log)


def per_device(
    positions,
    spacing,
    assign,
    depth_rank,
    pixel_grad,
    fourier,
    first_weight,
    first_bias,
    second_weight,
    second_bias,
    head_weight,
    head_bias,
):
    groups = lax.axis_size("space")
    ray_count = positions.shape[1]
    total = ray_count * SEGS
    capacity = 3 * total // (2 * groups)
    slot_count = capacity * groups
    owner = assign.reshape(total)
    member = (owner[:, None] == jnp.arange(groups, dtype=jnp.int32)[None, :]).astype(jnp.int32)
    earlier = jnp.cumsum(member, axis=0) - member
    within = jnp.sum(earlier * member, axis=1)
    target = owner * capacity + within
    dispatch = (target[:, None] == jnp.arange(slot_count, dtype=jnp.int32)[None, :]).astype(
        jnp.float32
    )
    seg_pos = jnp.transpose(positions.reshape(3, total, SEG_LEN), (1, 0, 2))
    seg_gap = spacing.reshape(total, 1, SEG_LEN)
    segments = jnp.concatenate([seg_pos, seg_gap], axis=1).reshape(total, 4 * SEG_LEN)
    outgoing = lax.dot_general(
        dispatch,
        segments,
        (((0,), (0,)), ((), ())),
        precision=lax.Precision.HIGHEST,
        preferred_element_type=jnp.float32,
    )
    outgoing = outgoing.reshape(groups, capacity, 4 * SEG_LEN)
    arrived = lax.all_to_all(outgoing, "space", split_axis=0, concat_axis=0, tiled=True)
    samples = arrived.reshape(slot_count, 4, SEG_LEN)
    params = tuple(
        (
            item[0]
            for item in (
                first_weight,
                first_bias,
                second_weight,
                second_bias,
                head_weight,
                head_bias,
            )
        )
    )
    seg_colour, seg_log, saved = network(samples, fourier, params)
    partials = jnp.concatenate([seg_colour.T, seg_log[None, :]], axis=0).reshape(
        4, groups, capacity
    )
    returned = lax.all_to_all(partials, "space", split_axis=1, concat_axis=1, tiled=True).reshape(
        4, slot_count
    )
    mine = lax.dot_general(
        dispatch,
        returned,
        (((1,), (1,)), ((), ())),
        precision=lax.Precision.HIGHEST,
        preferred_element_type=jnp.float32,
    )
    up_colour, up_log = composite(
        mine[:, :3].reshape(ray_count, SEGS, 3),
        mine[:, 3].reshape(ray_count, SEGS),
        depth_rank,
        pixel_grad.T,
    )
    upstream = jnp.concatenate([up_colour.reshape(total, 3), up_log.reshape(total, 1)], axis=1)
    sendback = lax.dot_general(
        upstream,
        dispatch,
        (((0,), (0,)), ((), ())),
        precision=lax.Precision.HIGHEST,
        preferred_element_type=jnp.float32,
    )
    sendback = sendback.reshape(4, groups, capacity)
    received = lax.all_to_all(sendback, "space", split_axis=1, concat_axis=1, tiled=True)
    received = received.reshape(4, slot_count).T
    totals = backward(samples, params, saved, received[:, :3], received[:, 3])
    grad_first, grad_second, grad_head, bias_first, bias_second, bias_head = totals
    replicas = lax.axis_size("ray")
    small = jnp.concatenate(
        [grad_head.reshape(-1), bias_first, bias_second, bias_head], axis=0
    )
    if replicas & (replicas - 1) == 0:
        position = lax.axis_index("ray")
        part_first, part_second = grad_first, grad_second
        distance = replicas // 2
        while distance >= 1:
            pairs = [(i, i ^ distance) for i in range(replicas)]
            half = part_first.shape[0] // 2
            upper = (position // distance) % 2
            keep_first = lax.dynamic_slice_in_dim(part_first, upper * half, half, 0)
            send_first = lax.dynamic_slice_in_dim(part_first, (1 - upper) * half, half, 0)
            keep_second = lax.dynamic_slice_in_dim(part_second, upper * half, half, 0)
            send_second = lax.dynamic_slice_in_dim(part_second, (1 - upper) * half, half, 0)
            got_first, got_second, got_small = lax.ppermute(
                (send_first, send_second, small), "ray", pairs
            )
            part_first = keep_first + got_first
            part_second = keep_second + got_second
            small = small + got_small
            distance //= 2
    else:
        part_first = lax.psum_scatter(grad_first, "ray", scatter_dimension=0, tiled=True)
        part_second = lax.psum_scatter(grad_second, "ray", scatter_dimension=0, tiled=True)
        small = lax.psum(small, "ray")
    heads = grad_head.size
    hidden = bias_first.shape[0]
    small_sums = (
        small[:heads].reshape(grad_head.shape),
        small[heads : heads + hidden],
        small[heads + hidden : heads + 2 * hidden],
        small[heads + 2 * hidden :],
    )
    return (
        part_first[None],
        part_second[None],
        small_sums[0][None],
        small_sums[1][None],
        small_sums[2][None],
        small_sums[3][None],
    )


def solution(mesh):
    placed = (
        P(None, ("space", "ray"), None),
        P(("space", "ray"), None),
        P(("space", "ray"), None, None),
        P(("space", "ray"), None),
        P(None, ("space", "ray")),
        P(),
        P("space", None, None),
        P("space", None),
        P("space", None, None),
        P("space", None),
        P("space", None, None),
        P("space", None),
    )
    return jax.shard_map(
        per_device,
        mesh=mesh,
        in_specs=placed,
        out_specs=(
            P("space", "ray", None),
            P("space", "ray", None),
            P("space", None, None),
            P("space", None),
            P("space", None),
            P("space", None),
        ),
        check_vma=False,
    )
```

```python
import jax
import jax.numpy as jnp
from jax import lax
from jax.sharding import PartitionSpec as P

SEG_LEN = 32
SEGS = 8


two_pi = 6.283185307179586


def silu_slope(value):
    gate = jax.nn.sigmoid(value)
    return gate * (1.0 + value * (1.0 - gate))


def encode(samples, fourier):
    phases = two_pi * (
        samples[:, 0, :, None] * fourier[0]
        + samples[:, 1, :, None] * fourier[1]
        + samples[:, 2, :, None] * fourier[2]
    )
    joined = jnp.concatenate([jnp.sin(phases), jnp.cos(phases)], axis=-1)
    return joined.astype(jnp.bfloat16).reshape(-1, joined.shape[-1])


def network(samples, fourier, params):
    first_weight, first_bias, second_weight, second_bias, head_weight, head_bias = params
    seg_count, length = (samples.shape[0], samples.shape[2])
    encoded = encode(samples, fourier)
    pre_first = jnp.dot(encoded, first_weight, preferred_element_type=jnp.float32) + first_bias
    act_first = jax.nn.silu(pre_first).astype(jnp.bfloat16)
    pre_second = jnp.dot(act_first, second_weight, preferred_element_type=jnp.float32) + second_bias
    act_second = jax.nn.silu(pre_second).astype(jnp.bfloat16)
    head_raw = (
        lax.dot_general(
            act_second, head_weight, (((1,), (1,)), ((), ())), preferred_element_type=jnp.float32
        )
        + head_bias
    )
    head_raw = head_raw.reshape(seg_count, length, 4)
    density = jax.nn.softplus(head_raw[..., 0])
    colour = jax.nn.sigmoid(head_raw[..., 1:])
    optical = density * samples[:, 3, :]
    inclusive = jnp.cumsum(optical, axis=1)
    enter_light = jnp.exp(optical - inclusive)
    leave_light = jnp.exp(-inclusive)
    weight = enter_light - leave_light
    seg_colour = jnp.sum(weight[..., None] * colour, axis=1)
    seg_log = -inclusive[:, -1]
    saved = (
        encoded,
        pre_first,
        act_first,
        pre_second,
        act_second,
        head_raw,
        colour,
        weight,
        leave_light,
    )
    return (seg_colour, seg_log, saved)


def backward(samples, params, saved, up_colour, up_log):
    first_weight, first_bias, second_weight, second_bias, head_weight, head_bias = params
    encoded, pre_first, act_first, pre_second, act_second, head_raw, colour, weight, leave_light = (
        saved
    )
    energy = jnp.sum(colour * up_colour[:, None, :], axis=-1)
    spent = weight * energy
    remaining = jnp.sum(spent, axis=1, keepdims=True) - jnp.cumsum(spent, axis=1)
    grad_optical = leave_light * energy - remaining - up_log[:, None]
    grad_density = grad_optical * samples[:, 3, :] * jax.nn.sigmoid(head_raw[..., 0])
    grad_tint = weight[..., None] * up_colour[:, None, :] * colour * (1.0 - colour)
    grad_raw = (
        jnp.concatenate([grad_density[..., None], grad_tint], axis=-1)
        .reshape(-1, 4)
        .astype(jnp.bfloat16)
    )
    grad_head = lax.dot_general(
        grad_raw, act_second, (((0,), (0,)), ((), ())), preferred_element_type=jnp.float32
    )
    grad_head_bias = jnp.sum(grad_raw.astype(jnp.float32), axis=0)
    back_second = jnp.dot(grad_raw, head_weight, preferred_element_type=jnp.float32)
    delta_second = (back_second * silu_slope(pre_second)).astype(jnp.bfloat16)
    grad_second = lax.dot_general(
        act_first, delta_second, (((0,), (0,)), ((), ())), preferred_element_type=jnp.float32
    )
    grad_second_bias = jnp.sum(delta_second.astype(jnp.float32), axis=0)
    back_first = lax.dot_general(
        delta_second, second_weight, (((1,), (1,)), ((), ())), preferred_element_type=jnp.float32
    )
    delta_first = (back_first * silu_slope(pre_first)).astype(jnp.bfloat16)
    grad_first = lax.dot_general(
        encoded, delta_first, (((0,), (0,)), ((), ())), preferred_element_type=jnp.float32
    )
    grad_first_bias = jnp.sum(delta_first.astype(jnp.float32), axis=0)
    return (grad_first, grad_second, grad_head, grad_first_bias, grad_second_bias, grad_head_bias)


def composite(seg_colour, seg_log, depth_rank, pixel_rows):
    before = (depth_rank[:, None, :] < depth_rank[:, :, None]).astype(jnp.float32)
    prefix = jnp.exp(jnp.sum(before * seg_log[:, None, :], axis=2))
    up_colour = prefix[..., None] * pixel_rows[:, None, :]
    shaded = prefix * jnp.sum(seg_colour * pixel_rows[:, None, :], axis=2)
    up_log = jnp.sum(before * shaded[:, :, None], axis=1)
    return (up_colour, up_log)


def per_device(
    positions,
    spacing,
    assign,
    depth_rank,
    pixel_grad,
    fourier,
    first_weight,
    first_bias,
    second_weight,
    second_bias,
    head_weight,
    head_bias,
):
    groups = lax.axis_size("space")
    ray_count = positions.shape[1]
    total = ray_count * SEGS
    capacity = 3 * total // (2 * groups)
    slot_count = capacity * groups
    owner = assign.reshape(total)
    member = (owner[:, None] == jnp.arange(groups, dtype=jnp.int32)[None, :]).astype(jnp.int32)
    earlier = jnp.cumsum(member, axis=0) - member
    within = jnp.sum(earlier * member, axis=1)
    target = owner * capacity + within
    dispatch = (target[:, None] == jnp.arange(slot_count, dtype=jnp.int32)[None, :]).astype(
        jnp.float32
    )
    seg_pos = jnp.transpose(positions.reshape(3, total, SEG_LEN), (1, 0, 2))
    seg_gap = spacing.reshape(total, 1, SEG_LEN)
    segments = jnp.concatenate([seg_pos, seg_gap], axis=1).reshape(total, 4 * SEG_LEN)
    place = owner * slot_count + lax.axis_index("space") * capacity + within
    ray_place = jnp.broadcast_to(
        place.reshape(ray_count, 1, SEGS), (ray_count, SEGS, SEGS)
    ).astype(jnp.float32)
    ray_rank = jnp.broadcast_to(
        depth_rank.reshape(ray_count, 1, SEGS), (ray_count, SEGS, SEGS)
    ).astype(jnp.float32)
    ray_pixel = jnp.broadcast_to(pixel_grad.T[:, None, :], (ray_count, SEGS, 3))
    own_rank = depth_rank.reshape(ray_count, SEGS, 1).astype(jnp.float32)
    extra = jnp.concatenate([ray_place, ray_rank, ray_pixel, own_rank], axis=2)
    segments = jnp.concatenate([segments, extra.reshape(total, 2 * SEGS + 4)], axis=1)
    outgoing = lax.dot_general(
        dispatch,
        segments,
        (((0,), (0,)), ((), ())),
        precision=lax.Precision.HIGHEST,
        preferred_element_type=jnp.float32,
    )
    outgoing = outgoing.reshape(groups, capacity, 4 * SEG_LEN + 2 * SEGS + 4)
    arrived = lax.all_to_all(outgoing, "space", split_axis=0, concat_axis=0, tiled=True)
    arrived = arrived.reshape(slot_count, 4 * SEG_LEN + 2 * SEGS + 4)
    samples = arrived[:, : 4 * SEG_LEN].reshape(slot_count, 4, SEG_LEN)
    meta = arrived[:, 4 * SEG_LEN :]
    params = tuple(
        (
            item[0]
            for item in (
                first_weight,
                first_bias,
                second_weight,
                second_bias,
                head_weight,
                head_bias,
            )
        )
    )
    seg_colour, seg_log, saved = network(samples, fourier, params)
    partials = jnp.concatenate([seg_colour, seg_log[:, None]], axis=1)
    spread = jnp.broadcast_to(partials[None], (groups, slot_count, 4))
    table = lax.all_to_all(spread, "space", split_axis=0, concat_axis=0, tiled=True)
    table = jnp.transpose(table.reshape(groups, slot_count, 4), (1, 0, 2)).reshape(
        slot_count, groups * 4
    )
    index = meta[:, :SEGS].astype(jnp.int32)
    column = index % slot_count
    holder = index // slot_count
    pick_column = (column[:, :, None] == jnp.arange(slot_count, dtype=jnp.int32)).astype(
        jnp.float32
    )
    rows = lax.dot_general(
        pick_column,
        table,
        (((2,), (0,)), ((), ())),
        precision=lax.Precision.HIGHEST,
        preferred_element_type=jnp.float32,
    ).reshape(slot_count, SEGS, groups, 4)
    pick_holder = (holder[:, :, None] == jnp.arange(groups, dtype=jnp.int32)).astype(
        jnp.float32
    )
    values = jnp.sum(rows * pick_holder[..., None], axis=2)
    ranks = meta[:, SEGS : 2 * SEGS]
    pixel = meta[:, 2 * SEGS : 2 * SEGS + 3]
    own = meta[:, 2 * SEGS + 3 :]
    logs = values[..., 3]
    before = (ranks[:, None, :] < ranks[:, :, None]).astype(jnp.float32)
    prefix = jnp.exp(jnp.sum(before * logs[:, None, :], axis=2))
    shaded = prefix * jnp.sum(values[..., :3] * pixel[:, None, :], axis=2)
    own_before = (ranks < own).astype(jnp.float32)
    own_prefix = jnp.exp(jnp.sum(own_before * logs, axis=1))
    up_colour = own_prefix[:, None] * pixel
    up_log = jnp.sum((own < ranks).astype(jnp.float32) * shaded, axis=1)
    totals = backward(samples, params, saved, up_colour, up_log)
    grad_first, grad_second, grad_head, bias_first, bias_second, bias_head = totals
    replicas = lax.axis_size("ray")
    small = jnp.concatenate(
        [grad_head.reshape(-1), bias_first, bias_second, bias_head], axis=0
    )
    if replicas & (replicas - 1) == 0:
        position = lax.axis_index("ray")
        part_first, part_second = grad_first, grad_second
        distance = replicas // 2
        while distance >= 1:
            pairs = [(i, i ^ distance) for i in range(replicas)]
            half = part_first.shape[0] // 2
            upper = (position // distance) % 2
            keep_first = lax.dynamic_slice_in_dim(part_first, upper * half, half, 0)
            send_first = lax.dynamic_slice_in_dim(part_first, (1 - upper) * half, half, 0)
            keep_second = lax.dynamic_slice_in_dim(part_second, upper * half, half, 0)
            send_second = lax.dynamic_slice_in_dim(part_second, (1 - upper) * half, half, 0)
            got_first, got_second, got_small = lax.ppermute(
                (send_first, send_second, small), "ray", pairs
            )
            part_first = keep_first + got_first
            part_second = keep_second + got_second
            small = small + got_small
            distance //= 2
    else:
        part_first = lax.psum_scatter(grad_first, "ray", scatter_dimension=0, tiled=True)
        part_second = lax.psum_scatter(grad_second, "ray", scatter_dimension=0, tiled=True)
        small = lax.psum(small, "ray")
    heads = grad_head.size
    hidden = bias_first.shape[0]
    small_sums = (
        small[:heads].reshape(grad_head.shape),
        small[heads : heads + hidden],
        small[heads + hidden : heads + 2 * hidden],
        small[heads + 2 * hidden :],
    )
    return (
        part_first[None],
        part_second[None],
        small_sums[0][None],
        small_sums[1][None],
        small_sums[2][None],
        small_sums[3][None],
    )


def solution(mesh):
    placed = (
        P(None, ("space", "ray"), None),
        P(("space", "ray"), None),
        P(("space", "ray"), None, None),
        P(("space", "ray"), None),
        P(None, ("space", "ray")),
        P(),
        P("space", None, None),
        P("space", None),
        P("space", None, None),
        P("space", None),
        P("space", None, None),
        P("space", None),
    )
    return jax.shard_map(
        per_device,
        mesh=mesh,
        in_specs=placed,
        out_specs=(
            P("space", "ray", None),
            P("space", "ray", None),
            P("space", None, None),
            P("space", None),
            P("space", None),
            P("space", None),
        ),
        check_vma=False,
    )
```

```python
import jax
import jax.numpy as jnp
from jax import lax
from jax.sharding import PartitionSpec as P

SEG_LEN = 32
SEGS = 8


two_pi = 6.283185307179586


def silu_slope(value):
    gate = jax.nn.sigmoid(value)
    return gate * (1.0 + value * (1.0 - gate))


def turn_sin_cos(turns):
    quarter = jnp.round(turns * 4.0)
    angle = (turns - quarter * 0.25) * two_pi
    square = angle * angle
    sine = angle * (
        1.0
        + square
        * (
            -1.0 / 6.0
            + square * (1.0 / 120.0 + square * (-1.0 / 5040.0 + square * (1.0 / 362880.0)))
        )
    )
    cosine = 1.0 + square * (
        -0.5
        + square
        * (
            1.0 / 24.0
            + square * (-1.0 / 720.0 + square * (1.0 / 40320.0 + square * (-1.0 / 3628800.0)))
        )
    )
    step = quarter - 4.0 * jnp.floor(quarter * 0.25)
    flip = step >= 2.0
    odd = (step == 1.0) | (step == 3.0)
    sin_out = jnp.where(odd, cosine, sine)
    cos_out = jnp.where(odd, sine, cosine)
    sin_out = jnp.where(flip, -sin_out, sin_out)
    cos_out = jnp.where(flip != odd, -cos_out, cos_out)
    return sin_out, cos_out


def encode(samples, fourier):
    turns = (
        samples[:, 0, :, None] * fourier[0]
        + samples[:, 1, :, None] * fourier[1]
        + samples[:, 2, :, None] * fourier[2]
    )
    sine, cosine = turn_sin_cos(turns)
    joined = jnp.concatenate([sine, cosine], axis=-1)
    return joined.astype(jnp.bfloat16).reshape(-1, joined.shape[-1])


def network(samples, fourier, params):
    first_weight, first_bias, second_weight, second_bias, head_weight, head_bias = params
    seg_count, length = (samples.shape[0], samples.shape[2])
    encoded = encode(samples, fourier)
    pre_first = jnp.dot(encoded, first_weight, preferred_element_type=jnp.float32) + first_bias
    act_first = jax.nn.silu(pre_first).astype(jnp.bfloat16)
    pre_second = jnp.dot(act_first, second_weight, preferred_element_type=jnp.float32) + second_bias
    act_second = jax.nn.silu(pre_second).astype(jnp.bfloat16)
    head_raw = (
        lax.dot_general(
            act_second, head_weight, (((1,), (1,)), ((), ())), preferred_element_type=jnp.float32
        )
        + head_bias
    )
    head_raw = head_raw.reshape(seg_count, length, 4)
    density = jax.nn.softplus(head_raw[..., 0])
    colour = jax.nn.sigmoid(head_raw[..., 1:])
    optical = density * samples[:, 3, :]
    inclusive = jnp.cumsum(optical, axis=1)
    enter_light = jnp.exp(optical - inclusive)
    leave_light = jnp.exp(-inclusive)
    weight = enter_light - leave_light
    seg_colour = jnp.sum(weight[..., None] * colour, axis=1)
    seg_log = -inclusive[:, -1]
    saved = (
        encoded,
        pre_first,
        act_first,
        pre_second,
        act_second,
        head_raw,
        colour,
        weight,
        leave_light,
    )
    return (seg_colour, seg_log, saved)


def backward(samples, params, saved, up_colour, up_log):
    first_weight, first_bias, second_weight, second_bias, head_weight, head_bias = params
    encoded, pre_first, act_first, pre_second, act_second, head_raw, colour, weight, leave_light = (
        saved
    )
    energy = jnp.sum(colour * up_colour[:, None, :], axis=-1)
    spent = weight * energy
    remaining = jnp.sum(spent, axis=1, keepdims=True) - jnp.cumsum(spent, axis=1)
    grad_optical = leave_light * energy - remaining - up_log[:, None]
    grad_density = grad_optical * samples[:, 3, :] * jax.nn.sigmoid(head_raw[..., 0])
    grad_tint = weight[..., None] * up_colour[:, None, :] * colour * (1.0 - colour)
    grad_raw = (
        jnp.concatenate([grad_density[..., None], grad_tint], axis=-1)
        .reshape(-1, 4)
        .astype(jnp.bfloat16)
    )
    grad_head = lax.dot_general(
        grad_raw, act_second, (((0,), (0,)), ((), ())), preferred_element_type=jnp.float32
    )
    grad_head_bias = jnp.sum(grad_raw.astype(jnp.float32), axis=0)
    back_second = jnp.dot(grad_raw, head_weight, preferred_element_type=jnp.float32)
    delta_second = (back_second * silu_slope(pre_second)).astype(jnp.bfloat16)
    grad_second = lax.dot_general(
        act_first, delta_second, (((0,), (0,)), ((), ())), preferred_element_type=jnp.float32
    )
    grad_second_bias = jnp.sum(delta_second.astype(jnp.float32), axis=0)
    back_first = lax.dot_general(
        delta_second, second_weight, (((1,), (1,)), ((), ())), preferred_element_type=jnp.float32
    )
    delta_first = (back_first * silu_slope(pre_first)).astype(jnp.bfloat16)
    grad_first = lax.dot_general(
        encoded, delta_first, (((0,), (0,)), ((), ())), preferred_element_type=jnp.float32
    )
    grad_first_bias = jnp.sum(delta_first.astype(jnp.float32), axis=0)
    return (grad_first, grad_second, grad_head, grad_first_bias, grad_second_bias, grad_head_bias)


def composite(seg_colour, seg_log, depth_rank, pixel_rows):
    before = (depth_rank[:, None, :] < depth_rank[:, :, None]).astype(jnp.float32)
    prefix = jnp.exp(jnp.sum(before * seg_log[:, None, :], axis=2))
    up_colour = prefix[..., None] * pixel_rows[:, None, :]
    shaded = prefix * jnp.sum(seg_colour * pixel_rows[:, None, :], axis=2)
    up_log = jnp.sum(before * shaded[:, :, None], axis=1)
    return (up_colour, up_log)


def per_device(
    positions,
    spacing,
    assign,
    depth_rank,
    pixel_grad,
    fourier,
    first_weight,
    first_bias,
    second_weight,
    second_bias,
    head_weight,
    head_bias,
):
    groups = lax.axis_size("space")
    ray_count = positions.shape[1]
    total = ray_count * SEGS
    capacity = 3 * total // (2 * groups)
    slot_count = capacity * groups
    owner = assign.reshape(total)
    member = (owner[:, None] == jnp.arange(groups, dtype=jnp.int32)[None, :]).astype(jnp.int32)
    earlier = jnp.cumsum(member, axis=0) - member
    within = jnp.sum(earlier * member, axis=1)
    target = owner * capacity + within
    dispatch = (target[:, None] == jnp.arange(slot_count, dtype=jnp.int32)[None, :]).astype(
        jnp.float32
    )
    seg_pos = jnp.transpose(positions.reshape(3, total, SEG_LEN), (1, 0, 2))
    seg_gap = spacing.reshape(total, 1, SEG_LEN)
    segments = jnp.concatenate([seg_pos, seg_gap], axis=1).reshape(total, 4 * SEG_LEN)
    outgoing = lax.dot_general(
        dispatch,
        segments,
        (((0,), (0,)), ((), ())),
        precision=lax.Precision.HIGHEST,
        preferred_element_type=jnp.float32,
    )
    outgoing = outgoing.reshape(groups, capacity, 4 * SEG_LEN)
    arrived = lax.all_to_all(outgoing, "space", split_axis=0, concat_axis=0, tiled=True)
    samples = arrived.reshape(slot_count, 4, SEG_LEN)
    params = tuple(
        (
            item[0]
            for item in (
                first_weight,
                first_bias,
                second_weight,
                second_bias,
                head_weight,
                head_bias,
            )
        )
    )
    seg_colour, seg_log, saved = network(samples, fourier, params)
    partials = jnp.concatenate([seg_colour.T, seg_log[None, :]], axis=0).reshape(
        4, groups, capacity
    )
    returned = lax.all_to_all(partials, "space", split_axis=1, concat_axis=1, tiled=True).reshape(
        4, slot_count
    )
    mine = lax.dot_general(
        dispatch,
        returned,
        (((1,), (1,)), ((), ())),
        precision=lax.Precision.HIGHEST,
        preferred_element_type=jnp.float32,
    )
    up_colour, up_log = composite(
        mine[:, :3].reshape(ray_count, SEGS, 3),
        mine[:, 3].reshape(ray_count, SEGS),
        depth_rank,
        pixel_grad.T,
    )
    upstream = jnp.concatenate([up_colour.reshape(total, 3), up_log.reshape(total, 1)], axis=1)
    sendback = lax.dot_general(
        upstream,
        dispatch,
        (((0,), (0,)), ((), ())),
        precision=lax.Precision.HIGHEST,
        preferred_element_type=jnp.float32,
    )
    sendback = sendback.reshape(4, groups, capacity)
    received = lax.all_to_all(sendback, "space", split_axis=1, concat_axis=1, tiled=True)
    received = received.reshape(4, slot_count).T
    totals = backward(samples, params, saved, received[:, :3], received[:, 3])
    grad_first, grad_second, grad_head, bias_first, bias_second, bias_head = totals
    replicas = lax.axis_size("ray")
    small = jnp.concatenate(
        [grad_head.reshape(-1), bias_first, bias_second, bias_head], axis=0
    )
    if replicas & (replicas - 1) == 0:
        position = lax.axis_index("ray")
        part_first, part_second = grad_first, grad_second
        distance = replicas // 2
        while distance >= 1:
            pairs = [(i, i ^ distance) for i in range(replicas)]
            half = part_first.shape[0] // 2
            upper = (position // distance) % 2
            keep_first = lax.dynamic_slice_in_dim(part_first, upper * half, half, 0)
            send_first = lax.dynamic_slice_in_dim(part_first, (1 - upper) * half, half, 0)
            keep_second = lax.dynamic_slice_in_dim(part_second, upper * half, half, 0)
            send_second = lax.dynamic_slice_in_dim(part_second, (1 - upper) * half, half, 0)
            got_first, got_second, got_small = lax.ppermute(
                (send_first, send_second, small), "ray", pairs
            )
            part_first = keep_first + got_first
            part_second = keep_second + got_second
            small = small + got_small
            distance //= 2
    else:
        part_first = lax.psum_scatter(grad_first, "ray", scatter_dimension=0, tiled=True)
        part_second = lax.psum_scatter(grad_second, "ray", scatter_dimension=0, tiled=True)
        small = lax.psum(small, "ray")
    heads = grad_head.size
    hidden = bias_first.shape[0]
    small_sums = (
        small[:heads].reshape(grad_head.shape),
        small[heads : heads + hidden],
        small[heads + hidden : heads + 2 * hidden],
        small[heads + 2 * hidden :],
    )
    return (
        part_first[None],
        part_second[None],
        small_sums[0][None],
        small_sums[1][None],
        small_sums[2][None],
        small_sums[3][None],
    )


def solution(mesh):
    placed = (
        P(None, ("space", "ray"), None),
        P(("space", "ray"), None),
        P(("space", "ray"), None, None),
        P(("space", "ray"), None),
        P(None, ("space", "ray")),
        P(),
        P("space", None, None),
        P("space", None),
        P("space", None, None),
        P("space", None),
        P("space", None, None),
        P("space", None),
    )
    return jax.shard_map(
        per_device,
        mesh=mesh,
        in_specs=placed,
        out_specs=(
            P("space", "ray", None),
            P("space", "ray", None),
            P("space", None, None),
            P("space", None),
            P("space", None),
            P("space", None),
        ),
        check_vma=False,
    )
```

```python
import jax
import jax.numpy as jnp
from jax import lax
from jax.sharding import PartitionSpec as P

SEG_LEN = 32
SEGS = 8


two_pi = 6.283185307179586


def silu_slope(value):
    gate = jax.nn.sigmoid(value)
    return gate * (1.0 + value * (1.0 - gate))


def turn_sin_cos(turns):
    quarter = jnp.round(turns * 4.0)
    angle = (turns - quarter * 0.25) * two_pi
    square = angle * angle
    sine = angle * (
        1.0
        + square
        * (
            -1.0 / 6.0
            + square * (1.0 / 120.0 + square * (-1.0 / 5040.0 + square * (1.0 / 362880.0)))
        )
    )
    cosine = 1.0 + square * (
        -0.5
        + square
        * (
            1.0 / 24.0
            + square * (-1.0 / 720.0 + square * (1.0 / 40320.0 + square * (-1.0 / 3628800.0)))
        )
    )
    step = quarter - 4.0 * jnp.floor(quarter * 0.25)
    flip = step >= 2.0
    odd = (step == 1.0) | (step == 3.0)
    sin_out = jnp.where(odd, cosine, sine)
    cos_out = jnp.where(odd, sine, cosine)
    sin_out = jnp.where(flip, -sin_out, sin_out)
    cos_out = jnp.where(flip != odd, -cos_out, cos_out)
    return sin_out, cos_out


def encode(samples, fourier):
    turns = (
        samples[:, 0, :, None] * fourier[0]
        + samples[:, 1, :, None] * fourier[1]
        + samples[:, 2, :, None] * fourier[2]
    )
    sine, cosine = turn_sin_cos(turns)
    joined = jnp.concatenate([sine, cosine], axis=-1)
    return joined.astype(jnp.bfloat16).reshape(-1, joined.shape[-1])


def network(samples, fourier, params):
    first_weight, first_bias, second_weight, second_bias, head_weight, head_bias = params
    seg_count, length = (samples.shape[0], samples.shape[2])
    encoded = encode(samples, fourier)
    pre_first = jnp.dot(encoded, first_weight, preferred_element_type=jnp.float32) + first_bias
    act_first = jax.nn.silu(pre_first).astype(jnp.bfloat16)
    pre_second = jnp.dot(act_first, second_weight, preferred_element_type=jnp.float32) + second_bias
    act_second = jax.nn.silu(pre_second).astype(jnp.bfloat16)
    head_raw = (
        lax.dot_general(
            act_second, head_weight, (((1,), (1,)), ((), ())), preferred_element_type=jnp.float32
        )
        + head_bias
    )
    head_raw = head_raw.reshape(seg_count, length, 4)
    density = jax.nn.softplus(head_raw[..., 0])
    colour = jax.nn.sigmoid(head_raw[..., 1:])
    optical = density * samples[:, 3, :]
    inclusive = jnp.cumsum(optical, axis=1)
    enter_light = jnp.exp(optical - inclusive)
    leave_light = jnp.exp(-inclusive)
    weight = enter_light - leave_light
    seg_colour = jnp.sum(weight[..., None] * colour, axis=1)
    seg_log = -inclusive[:, -1]
    saved = (
        encoded,
        pre_first,
        act_first,
        pre_second,
        act_second,
        head_raw,
        colour,
        weight,
        leave_light,
    )
    return (seg_colour, seg_log, saved)


def backward(samples, params, saved, up_colour, up_log):
    first_weight, first_bias, second_weight, second_bias, head_weight, head_bias = params
    encoded, pre_first, act_first, pre_second, act_second, head_raw, colour, weight, leave_light = (
        saved
    )
    energy = jnp.sum(colour * up_colour[:, None, :], axis=-1)
    spent = weight * energy
    remaining = jnp.sum(spent, axis=1, keepdims=True) - jnp.cumsum(spent, axis=1)
    grad_optical = leave_light * energy - remaining - up_log[:, None]
    grad_density = grad_optical * samples[:, 3, :] * jax.nn.sigmoid(head_raw[..., 0])
    grad_tint = weight[..., None] * up_colour[:, None, :] * colour * (1.0 - colour)
    grad_raw = (
        jnp.concatenate([grad_density[..., None], grad_tint], axis=-1)
        .reshape(-1, 4)
        .astype(jnp.bfloat16)
    )
    grad_head = lax.dot_general(
        grad_raw, act_second, (((0,), (0,)), ((), ())), preferred_element_type=jnp.float32
    )
    grad_head_bias = jnp.sum(grad_raw.astype(jnp.float32), axis=0)
    back_second = jnp.dot(grad_raw, head_weight, preferred_element_type=jnp.float32)
    delta_second = (back_second * silu_slope(pre_second)).astype(jnp.bfloat16)
    grad_second = lax.dot_general(
        act_first, delta_second, (((0,), (0,)), ((), ())), preferred_element_type=jnp.float32
    )
    grad_second_bias = jnp.sum(delta_second.astype(jnp.float32), axis=0)
    back_first = lax.dot_general(
        delta_second, second_weight, (((1,), (1,)), ((), ())), preferred_element_type=jnp.float32
    )
    delta_first = (back_first * silu_slope(pre_first)).astype(jnp.bfloat16)
    grad_first = lax.dot_general(
        encoded, delta_first, (((0,), (0,)), ((), ())), preferred_element_type=jnp.float32
    )
    grad_first_bias = jnp.sum(delta_first.astype(jnp.float32), axis=0)
    return (grad_first, grad_second, grad_head, grad_first_bias, grad_second_bias, grad_head_bias)


def composite(seg_colour, seg_log, depth_rank, pixel_rows):
    before = (depth_rank[:, None, :] < depth_rank[:, :, None]).astype(jnp.float32)
    prefix = jnp.exp(jnp.sum(before * seg_log[:, None, :], axis=2))
    up_colour = prefix[..., None] * pixel_rows[:, None, :]
    shaded = prefix * jnp.sum(seg_colour * pixel_rows[:, None, :], axis=2)
    up_log = jnp.sum(before * shaded[:, :, None], axis=1)
    return (up_colour, up_log)


def shift_exchange(blocks, axis, direction):
    count = blocks.shape[axis]
    parts = [lax.index_in_dim(blocks, 0, axis, keepdims=False)]
    for shift in range(1, count):
        pairs = [(i, (i + direction * shift) % count) for i in range(count)]
        piece = lax.index_in_dim(blocks, shift, axis, keepdims=False)
        parts.append(lax.ppermute(piece, "space", pairs))
    return jnp.stack(parts, axis=axis)


def per_device(
    positions,
    spacing,
    assign,
    depth_rank,
    pixel_grad,
    fourier,
    first_weight,
    first_bias,
    second_weight,
    second_bias,
    head_weight,
    head_bias,
):
    groups = lax.axis_size("space")
    ray_count = positions.shape[1]
    total = ray_count * SEGS
    capacity = 3 * total // (2 * groups)
    slot_count = capacity * groups
    owner = assign.reshape(total)
    member = (owner[:, None] == jnp.arange(groups, dtype=jnp.int32)[None, :]).astype(jnp.int32)
    earlier = jnp.cumsum(member, axis=0) - member
    within = jnp.sum(earlier * member, axis=1)
    target = ((owner - lax.axis_index("space")) % groups) * capacity + within
    dispatch = (target[:, None] == jnp.arange(slot_count, dtype=jnp.int32)[None, :]).astype(
        jnp.float32
    )
    seg_pos = jnp.transpose(positions.reshape(3, total, SEG_LEN), (1, 0, 2))
    seg_gap = spacing.reshape(total, 1, SEG_LEN)
    segments = jnp.concatenate([seg_pos, seg_gap], axis=1).reshape(total, 4 * SEG_LEN)
    outgoing = lax.dot_general(
        dispatch,
        segments,
        (((0,), (0,)), ((), ())),
        precision=lax.Precision.HIGHEST,
        preferred_element_type=jnp.float32,
    )
    outgoing = outgoing.reshape(groups, capacity, 4 * SEG_LEN)
    arrived = shift_exchange(outgoing, 0, 1)
    samples = arrived.reshape(slot_count, 4, SEG_LEN)
    params = tuple(
        (
            item[0]
            for item in (
                first_weight,
                first_bias,
                second_weight,
                second_bias,
                head_weight,
                head_bias,
            )
        )
    )
    seg_colour, seg_log, saved = network(samples, fourier, params)
    partials = jnp.concatenate([seg_colour.T, seg_log[None, :]], axis=0).reshape(
        4, groups, capacity
    )
    returned = shift_exchange(partials, 1, -1).reshape(
        4, slot_count
    )
    mine = lax.dot_general(
        dispatch,
        returned,
        (((1,), (1,)), ((), ())),
        precision=lax.Precision.HIGHEST,
        preferred_element_type=jnp.float32,
    )
    up_colour, up_log = composite(
        mine[:, :3].reshape(ray_count, SEGS, 3),
        mine[:, 3].reshape(ray_count, SEGS),
        depth_rank,
        pixel_grad.T,
    )
    upstream = jnp.concatenate([up_colour.reshape(total, 3), up_log.reshape(total, 1)], axis=1)
    sendback = lax.dot_general(
        upstream,
        dispatch,
        (((0,), (0,)), ((), ())),
        precision=lax.Precision.HIGHEST,
        preferred_element_type=jnp.float32,
    )
    sendback = sendback.reshape(4, groups, capacity)
    received = shift_exchange(sendback, 1, 1)
    received = received.reshape(4, slot_count).T
    totals = backward(samples, params, saved, received[:, :3], received[:, 3])
    grad_first, grad_second, grad_head, bias_first, bias_second, bias_head = totals
    replicas = lax.axis_size("ray")
    small = jnp.concatenate(
        [grad_head.reshape(-1), bias_first, bias_second, bias_head], axis=0
    )
    if replicas & (replicas - 1) == 0:
        position = lax.axis_index("ray")
        part_first, part_second = grad_first, grad_second
        distance = replicas // 2
        while distance >= 1:
            pairs = [(i, i ^ distance) for i in range(replicas)]
            half = part_first.shape[0] // 2
            upper = (position // distance) % 2
            keep_first = lax.dynamic_slice_in_dim(part_first, upper * half, half, 0)
            send_first = lax.dynamic_slice_in_dim(part_first, (1 - upper) * half, half, 0)
            keep_second = lax.dynamic_slice_in_dim(part_second, upper * half, half, 0)
            send_second = lax.dynamic_slice_in_dim(part_second, (1 - upper) * half, half, 0)
            got_first, got_second, got_small = lax.ppermute(
                (send_first, send_second, small), "ray", pairs
            )
            part_first = keep_first + got_first
            part_second = keep_second + got_second
            small = small + got_small
            distance //= 2
    else:
        part_first = lax.psum_scatter(grad_first, "ray", scatter_dimension=0, tiled=True)
        part_second = lax.psum_scatter(grad_second, "ray", scatter_dimension=0, tiled=True)
        small = lax.psum(small, "ray")
    heads = grad_head.size
    hidden = bias_first.shape[0]
    small_sums = (
        small[:heads].reshape(grad_head.shape),
        small[heads : heads + hidden],
        small[heads + hidden : heads + 2 * hidden],
        small[heads + 2 * hidden :],
    )
    return (
        part_first[None],
        part_second[None],
        small_sums[0][None],
        small_sums[1][None],
        small_sums[2][None],
        small_sums[3][None],
    )


def solution(mesh):
    placed = (
        P(None, ("space", "ray"), None),
        P(("space", "ray"), None),
        P(("space", "ray"), None, None),
        P(("space", "ray"), None),
        P(None, ("space", "ray")),
        P(),
        P("space", None, None),
        P("space", None),
        P("space", None, None),
        P("space", None),
        P("space", None, None),
        P("space", None),
    )
    return jax.shard_map(
        per_device,
        mesh=mesh,
        in_specs=placed,
        out_specs=(
            P("space", "ray", None),
            P("space", "ray", None),
            P("space", None, None),
            P("space", None),
            P("space", None),
            P("space", None),
        ),
        check_vma=False,
    )
```

```python
import jax
import jax.numpy as jnp
from jax import lax
from jax.sharding import PartitionSpec as P

SEG_LEN = 32
SEGS = 8


two_pi = 6.283185307179586


def gate_of(value):
    return 0.5 * jnp.tanh(0.5 * value) + 0.5


def silu_slope(value):
    gate = gate_of(value)
    return gate * (1.0 + value * (1.0 - gate))


def turn_sin_cos(turns):
    quarter = jnp.round(turns * 4.0)
    angle = (turns - quarter * 0.25) * two_pi
    square = angle * angle
    sine = angle * (
        1.0
        + square
        * (
            -1.0 / 6.0
            + square * (1.0 / 120.0 + square * (-1.0 / 5040.0 + square * (1.0 / 362880.0)))
        )
    )
    cosine = 1.0 + square * (
        -0.5
        + square
        * (
            1.0 / 24.0
            + square * (-1.0 / 720.0 + square * (1.0 / 40320.0 + square * (-1.0 / 3628800.0)))
        )
    )
    step = quarter - 4.0 * jnp.floor(quarter * 0.25)
    flip = step >= 2.0
    odd = (step == 1.0) | (step == 3.0)
    sin_out = jnp.where(odd, cosine, sine)
    cos_out = jnp.where(odd, sine, cosine)
    sin_out = jnp.where(flip, -sin_out, sin_out)
    cos_out = jnp.where(flip != odd, -cos_out, cos_out)
    return sin_out, cos_out


def encode(samples, fourier):
    turns = (
        samples[:, 0, :, None] * fourier[0]
        + samples[:, 1, :, None] * fourier[1]
        + samples[:, 2, :, None] * fourier[2]
    )
    sine, cosine = turn_sin_cos(turns)
    joined = jnp.concatenate([sine, cosine], axis=-1)
    return joined.astype(jnp.bfloat16).reshape(-1, joined.shape[-1])


def network(samples, fourier, params):
    first_weight, first_bias, second_weight, second_bias, head_weight, head_bias = params
    seg_count, length = (samples.shape[0], samples.shape[2])
    encoded = encode(samples, fourier)
    pre_first = jnp.dot(encoded, first_weight, preferred_element_type=jnp.float32) + first_bias
    act_first = (pre_first * gate_of(pre_first)).astype(jnp.bfloat16)
    pre_second = jnp.dot(act_first, second_weight, preferred_element_type=jnp.float32) + second_bias
    act_second = (pre_second * gate_of(pre_second)).astype(jnp.bfloat16)
    head_raw = (
        lax.dot_general(
            act_second, head_weight, (((1,), (1,)), ((), ())), preferred_element_type=jnp.float32
        )
        + head_bias
    )
    head_raw = head_raw.reshape(seg_count, length, 4)
    density = jax.nn.softplus(head_raw[..., 0])
    colour = jax.nn.sigmoid(head_raw[..., 1:])
    optical = density * samples[:, 3, :]
    inclusive = jnp.cumsum(optical, axis=1)
    enter_light = jnp.exp(optical - inclusive)
    leave_light = jnp.exp(-inclusive)
    weight = enter_light - leave_light
    seg_colour = jnp.sum(weight[..., None] * colour, axis=1)
    seg_log = -inclusive[:, -1]
    saved = (
        encoded,
        pre_first,
        act_first,
        pre_second,
        act_second,
        head_raw,
        colour,
        weight,
        leave_light,
    )
    return (seg_colour, seg_log, saved)


def backward(samples, params, saved, up_colour, up_log):
    first_weight, first_bias, second_weight, second_bias, head_weight, head_bias = params
    encoded, pre_first, act_first, pre_second, act_second, head_raw, colour, weight, leave_light = (
        saved
    )
    energy = jnp.sum(colour * up_colour[:, None, :], axis=-1)
    spent = weight * energy
    remaining = jnp.sum(spent, axis=1, keepdims=True) - jnp.cumsum(spent, axis=1)
    grad_optical = leave_light * energy - remaining - up_log[:, None]
    grad_density = grad_optical * samples[:, 3, :] * jax.nn.sigmoid(head_raw[..., 0])
    grad_tint = weight[..., None] * up_colour[:, None, :] * colour * (1.0 - colour)
    grad_raw = (
        jnp.concatenate([grad_density[..., None], grad_tint], axis=-1)
        .reshape(-1, 4)
        .astype(jnp.bfloat16)
    )
    grad_head = lax.dot_general(
        grad_raw, act_second, (((0,), (0,)), ((), ())), preferred_element_type=jnp.float32
    )
    grad_head_bias = jnp.sum(grad_raw.astype(jnp.float32), axis=0)
    back_second = jnp.dot(grad_raw, head_weight, preferred_element_type=jnp.float32)
    delta_second = (back_second * silu_slope(pre_second)).astype(jnp.bfloat16)
    grad_second = lax.dot_general(
        act_first, delta_second, (((0,), (0,)), ((), ())), preferred_element_type=jnp.float32
    )
    grad_second_bias = jnp.sum(delta_second.astype(jnp.float32), axis=0)
    back_first = lax.dot_general(
        delta_second, second_weight, (((1,), (1,)), ((), ())), preferred_element_type=jnp.float32
    )
    delta_first = (back_first * silu_slope(pre_first)).astype(jnp.bfloat16)
    grad_first = lax.dot_general(
        encoded, delta_first, (((0,), (0,)), ((), ())), preferred_element_type=jnp.float32
    )
    grad_first_bias = jnp.sum(delta_first.astype(jnp.float32), axis=0)
    return (grad_first, grad_second, grad_head, grad_first_bias, grad_second_bias, grad_head_bias)


def composite(seg_colour, seg_log, depth_rank, pixel_rows):
    before = (depth_rank[:, None, :] < depth_rank[:, :, None]).astype(jnp.float32)
    prefix = jnp.exp(jnp.sum(before * seg_log[:, None, :], axis=2))
    up_colour = prefix[..., None] * pixel_rows[:, None, :]
    shaded = prefix * jnp.sum(seg_colour * pixel_rows[:, None, :], axis=2)
    up_log = jnp.sum(before * shaded[:, :, None], axis=1)
    return (up_colour, up_log)


def per_device(
    positions,
    spacing,
    assign,
    depth_rank,
    pixel_grad,
    fourier,
    first_weight,
    first_bias,
    second_weight,
    second_bias,
    head_weight,
    head_bias,
):
    groups = lax.axis_size("space")
    ray_count = positions.shape[1]
    total = ray_count * SEGS
    capacity = 3 * total // (2 * groups)
    slot_count = capacity * groups
    owner = assign.reshape(total)
    member = (owner[:, None] == jnp.arange(groups, dtype=jnp.int32)[None, :]).astype(jnp.int32)
    earlier = jnp.cumsum(member, axis=0) - member
    within = jnp.sum(earlier * member, axis=1)
    target = owner * capacity + within
    dispatch = (target[:, None] == jnp.arange(slot_count, dtype=jnp.int32)[None, :]).astype(
        jnp.float32
    )
    seg_pos = jnp.transpose(positions.reshape(3, total, SEG_LEN), (1, 0, 2))
    seg_gap = spacing.reshape(total, 1, SEG_LEN)
    segments = jnp.concatenate([seg_pos, seg_gap], axis=1).reshape(total, 4 * SEG_LEN)
    outgoing = lax.dot_general(
        dispatch,
        segments,
        (((0,), (0,)), ((), ())),
        precision=lax.Precision.HIGHEST,
        preferred_element_type=jnp.float32,
    )
    outgoing = outgoing.reshape(groups, capacity, 4 * SEG_LEN)
    arrived = lax.all_to_all(outgoing, "space", split_axis=0, concat_axis=0, tiled=True)
    samples = arrived.reshape(slot_count, 4, SEG_LEN)
    params = tuple(
        (
            item[0]
            for item in (
                first_weight,
                first_bias,
                second_weight,
                second_bias,
                head_weight,
                head_bias,
            )
        )
    )
    seg_colour, seg_log, saved = network(samples, fourier, params)
    partials = jnp.concatenate([seg_colour.T, seg_log[None, :]], axis=0).reshape(
        4, groups, capacity
    )
    returned = lax.all_to_all(partials, "space", split_axis=1, concat_axis=1, tiled=True).reshape(
        4, slot_count
    )
    mine = lax.dot_general(
        dispatch,
        returned,
        (((1,), (1,)), ((), ())),
        precision=lax.Precision.HIGHEST,
        preferred_element_type=jnp.float32,
    )
    up_colour, up_log = composite(
        mine[:, :3].reshape(ray_count, SEGS, 3),
        mine[:, 3].reshape(ray_count, SEGS),
        depth_rank,
        pixel_grad.T,
    )
    upstream = jnp.concatenate([up_colour.reshape(total, 3), up_log.reshape(total, 1)], axis=1)
    sendback = lax.dot_general(
        upstream,
        dispatch,
        (((0,), (0,)), ((), ())),
        precision=lax.Precision.HIGHEST,
        preferred_element_type=jnp.float32,
    )
    sendback = sendback.reshape(4, groups, capacity)
    received = lax.all_to_all(sendback, "space", split_axis=1, concat_axis=1, tiled=True)
    received = received.reshape(4, slot_count).T
    totals = backward(samples, params, saved, received[:, :3], received[:, 3])
    grad_first, grad_second, grad_head, bias_first, bias_second, bias_head = totals
    replicas = lax.axis_size("ray")
    small = jnp.concatenate(
        [grad_head.reshape(-1), bias_first, bias_second, bias_head], axis=0
    )
    if replicas & (replicas - 1) == 0:
        position = lax.axis_index("ray")
        part_first, part_second = grad_first, grad_second
        distance = replicas // 2
        while distance >= 1:
            pairs = [(i, i ^ distance) for i in range(replicas)]
            half = part_first.shape[0] // 2
            upper = (position // distance) % 2
            keep_first = lax.dynamic_slice_in_dim(part_first, upper * half, half, 0)
            send_first = lax.dynamic_slice_in_dim(part_first, (1 - upper) * half, half, 0)
            keep_second = lax.dynamic_slice_in_dim(part_second, upper * half, half, 0)
            send_second = lax.dynamic_slice_in_dim(part_second, (1 - upper) * half, half, 0)
            got_first, got_second, got_small = lax.ppermute(
                (send_first, send_second, small), "ray", pairs
            )
            part_first = keep_first + got_first
            part_second = keep_second + got_second
            small = small + got_small
            distance //= 2
    else:
        part_first = lax.psum_scatter(grad_first, "ray", scatter_dimension=0, tiled=True)
        part_second = lax.psum_scatter(grad_second, "ray", scatter_dimension=0, tiled=True)
        small = lax.psum(small, "ray")
    heads = grad_head.size
    hidden = bias_first.shape[0]
    small_sums = (
        small[:heads].reshape(grad_head.shape),
        small[heads : heads + hidden],
        small[heads + hidden : heads + 2 * hidden],
        small[heads + 2 * hidden :],
    )
    return (
        part_first[None],
        part_second[None],
        small_sums[0][None],
        small_sums[1][None],
        small_sums[2][None],
        small_sums[3][None],
    )


def solution(mesh):
    placed = (
        P(None, ("space", "ray"), None),
        P(("space", "ray"), None),
        P(("space", "ray"), None, None),
        P(("space", "ray"), None),
        P(None, ("space", "ray")),
        P(),
        P("space", None, None),
        P("space", None),
        P("space", None, None),
        P("space", None),
        P("space", None, None),
        P("space", None),
    )
    return jax.shard_map(
        per_device,
        mesh=mesh,
        in_specs=placed,
        out_specs=(
            P("space", "ray", None),
            P("space", "ray", None),
            P("space", None, None),
            P("space", None),
            P("space", None),
            P("space", None),
        ),
        check_vma=False,
    )
```

```python
import jax
import jax.numpy as jnp
from jax import lax
from jax.sharding import PartitionSpec as P

SEG_LEN = 32
SEGS = 8


two_pi = 6.283185307179586


def gate_of(value):
    return 0.5 * jnp.tanh(0.5 * value) + 0.5


def silu_slope(value):
    gate = gate_of(value)
    return gate * (1.0 + value * (1.0 - gate))


def turn_sin_cos(turns):
    quarter = jnp.round(turns * 4.0)
    angle = (turns - quarter * 0.25) * two_pi
    square = angle * angle
    sine = angle * (
        1.0
        + square
        * (
            -1.0 / 6.0
            + square * (1.0 / 120.0 + square * (-1.0 / 5040.0 + square * (1.0 / 362880.0)))
        )
    )
    cosine = 1.0 + square * (
        -0.5
        + square
        * (
            1.0 / 24.0
            + square * (-1.0 / 720.0 + square * (1.0 / 40320.0 + square * (-1.0 / 3628800.0)))
        )
    )
    step = quarter - 4.0 * jnp.floor(quarter * 0.25)
    flip = step >= 2.0
    odd = (step == 1.0) | (step == 3.0)
    sin_out = jnp.where(odd, cosine, sine)
    cos_out = jnp.where(odd, sine, cosine)
    sin_out = jnp.where(flip, -sin_out, sin_out)
    cos_out = jnp.where(flip != odd, -cos_out, cos_out)
    return sin_out, cos_out


def encode(samples, fourier):
    turns = (
        samples[:, 0, :, None] * fourier[0]
        + samples[:, 1, :, None] * fourier[1]
        + samples[:, 2, :, None] * fourier[2]
    )
    sine, cosine = turn_sin_cos(turns)
    joined = jnp.concatenate([sine, cosine], axis=-1)
    return joined.astype(jnp.bfloat16).reshape(-1, joined.shape[-1])


def network(samples, fourier, params):
    first_weight, first_bias, second_weight, second_bias, head_weight, head_bias = params
    seg_count, length = (samples.shape[0], samples.shape[2])
    encoded = encode(samples, fourier)
    pre_first = jnp.dot(encoded, first_weight, preferred_element_type=jnp.float32) + first_bias
    act_first = (pre_first * gate_of(pre_first)).astype(jnp.bfloat16)
    pre_second = jnp.dot(act_first, second_weight, preferred_element_type=jnp.float32) + second_bias
    act_second = (pre_second * gate_of(pre_second)).astype(jnp.bfloat16)
    head_raw = (
        lax.dot_general(
            act_second, head_weight, (((1,), (1,)), ((), ())), preferred_element_type=jnp.float32
        )
        + head_bias
    )
    head_raw = head_raw.reshape(seg_count, length, 4)
    density = jax.nn.softplus(head_raw[..., 0])
    colour = jax.nn.sigmoid(head_raw[..., 1:])
    optical = density * samples[:, 3, :]
    inclusive = jnp.cumsum(optical, axis=1)
    enter_light = jnp.exp(optical - inclusive)
    leave_light = jnp.exp(-inclusive)
    weight = enter_light - leave_light
    seg_colour = jnp.sum(weight[..., None] * colour, axis=1)
    seg_log = -inclusive[:, -1]
    saved = (
        encoded,
        pre_first,
        act_first,
        pre_second,
        act_second,
        head_raw,
        colour,
        weight,
        leave_light,
    )
    return (seg_colour, seg_log, saved)


def backward(samples, params, saved, up_colour, up_log):
    first_weight, first_bias, second_weight, second_bias, head_weight, head_bias = params
    encoded, pre_first, act_first, pre_second, act_second, head_raw, colour, weight, leave_light = (
        saved
    )
    energy = jnp.sum(colour * up_colour[:, None, :], axis=-1)
    spent = weight * energy
    remaining = jnp.sum(spent, axis=1, keepdims=True) - jnp.cumsum(spent, axis=1)
    grad_optical = leave_light * energy - remaining - up_log[:, None]
    grad_density = grad_optical * samples[:, 3, :] * jax.nn.sigmoid(head_raw[..., 0])
    grad_tint = weight[..., None] * up_colour[:, None, :] * colour * (1.0 - colour)
    grad_raw = (
        jnp.concatenate([grad_density[..., None], grad_tint], axis=-1)
        .reshape(-1, 4)
        .astype(jnp.bfloat16)
    )
    grad_head = lax.dot_general(
        grad_raw, act_second, (((0,), (0,)), ((), ())), preferred_element_type=jnp.float32
    )
    grad_head_bias = jnp.sum(grad_raw.astype(jnp.float32), axis=0)
    back_second = jnp.dot(grad_raw, head_weight, preferred_element_type=jnp.float32)
    delta_second = (back_second * silu_slope(pre_second)).astype(jnp.bfloat16)
    grad_second = lax.dot_general(
        act_first, delta_second, (((0,), (0,)), ((), ())), preferred_element_type=jnp.float32
    )
    grad_second_bias = jnp.sum(delta_second.astype(jnp.float32), axis=0)
    back_first = lax.dot_general(
        delta_second, second_weight, (((1,), (1,)), ((), ())), preferred_element_type=jnp.float32
    )
    delta_first = (back_first * silu_slope(pre_first)).astype(jnp.bfloat16)
    grad_first = lax.dot_general(
        encoded, delta_first, (((0,), (0,)), ((), ())), preferred_element_type=jnp.float32
    )
    grad_first_bias = jnp.sum(delta_first.astype(jnp.float32), axis=0)
    return (grad_first, grad_second, grad_head, grad_first_bias, grad_second_bias, grad_head_bias)


def composite(seg_colour, seg_log, depth_rank, pixel_rows):
    before = (depth_rank[:, None, :] < depth_rank[:, :, None]).astype(jnp.float32)
    prefix = jnp.exp(jnp.sum(before * seg_log[:, None, :], axis=2))
    up_colour = prefix[..., None] * pixel_rows[:, None, :]
    shaded = prefix * jnp.sum(seg_colour * pixel_rows[:, None, :], axis=2)
    up_log = jnp.sum(before * shaded[:, :, None], axis=1)
    return (up_colour, up_log)


def per_device(
    positions,
    spacing,
    assign,
    depth_rank,
    pixel_grad,
    fourier,
    first_weight,
    first_bias,
    second_weight,
    second_bias,
    head_weight,
    head_bias,
):
    groups = lax.axis_size("space")
    ray_count = positions.shape[1]
    total = ray_count * SEGS
    capacity = 3 * total // (2 * groups)
    slot_count = capacity * groups
    owner = assign.reshape(total)
    member = (owner[:, None] == jnp.arange(groups, dtype=jnp.int32)[None, :]).astype(jnp.int32)
    earlier = jnp.cumsum(member, axis=0) - member
    within = jnp.sum(earlier * member, axis=1)
    target = owner * capacity + within
    dispatch = (target[:, None] == jnp.arange(slot_count, dtype=jnp.int32)[None, :]).astype(
        jnp.float32
    )
    seg_pos = jnp.transpose(positions.reshape(3, total, SEG_LEN), (1, 0, 2))
    seg_gap = spacing.reshape(total, 1, SEG_LEN)
    segments = jnp.concatenate([seg_pos, seg_gap], axis=1).reshape(total, 4 * SEG_LEN)
    outgoing = lax.dot_general(
        dispatch,
        segments,
        (((0,), (0,)), ((), ())),
        precision=lax.Precision.HIGHEST,
        preferred_element_type=jnp.float32,
    )
    outgoing = outgoing.reshape(groups, capacity, 4 * SEG_LEN)
    arrived = lax.all_to_all(outgoing, "space", split_axis=0, concat_axis=0, tiled=True)
    samples = arrived.reshape(slot_count, 4, SEG_LEN)
    params = tuple(
        (
            item[0]
            for item in (
                first_weight,
                first_bias,
                second_weight,
                second_bias,
                head_weight,
                head_bias,
            )
        )
    )
    seg_colour, seg_log, saved = network(samples, fourier, params)
    saved = lax.optimization_barrier(saved)
    partials = jnp.concatenate([seg_colour.T, seg_log[None, :]], axis=0).reshape(
        4, groups, capacity
    )
    returned = lax.all_to_all(partials, "space", split_axis=1, concat_axis=1, tiled=True).reshape(
        4, slot_count
    )
    mine = lax.dot_general(
        dispatch,
        returned,
        (((1,), (1,)), ((), ())),
        precision=lax.Precision.HIGHEST,
        preferred_element_type=jnp.float32,
    )
    up_colour, up_log = composite(
        mine[:, :3].reshape(ray_count, SEGS, 3),
        mine[:, 3].reshape(ray_count, SEGS),
        depth_rank,
        pixel_grad.T,
    )
    upstream = jnp.concatenate([up_colour.reshape(total, 3), up_log.reshape(total, 1)], axis=1)
    sendback = lax.dot_general(
        upstream,
        dispatch,
        (((0,), (0,)), ((), ())),
        precision=lax.Precision.HIGHEST,
        preferred_element_type=jnp.float32,
    )
    sendback = sendback.reshape(4, groups, capacity)
    received = lax.all_to_all(sendback, "space", split_axis=1, concat_axis=1, tiled=True)
    received = received.reshape(4, slot_count).T
    totals = backward(samples, params, saved, received[:, :3], received[:, 3])
    grad_first, grad_second, grad_head, bias_first, bias_second, bias_head = totals
    replicas = lax.axis_size("ray")
    small = jnp.concatenate(
        [grad_head.reshape(-1), bias_first, bias_second, bias_head], axis=0
    )
    if replicas & (replicas - 1) == 0:
        position = lax.axis_index("ray")
        part_first, part_second = grad_first, grad_second
        distance = replicas // 2
        while distance >= 1:
            pairs = [(i, i ^ distance) for i in range(replicas)]
            half = part_first.shape[0] // 2
            upper = (position // distance) % 2
            keep_first = lax.dynamic_slice_in_dim(part_first, upper * half, half, 0)
            send_first = lax.dynamic_slice_in_dim(part_first, (1 - upper) * half, half, 0)
            keep_second = lax.dynamic_slice_in_dim(part_second, upper * half, half, 0)
            send_second = lax.dynamic_slice_in_dim(part_second, (1 - upper) * half, half, 0)
            got_first, got_second, got_small = lax.ppermute(
                (send_first, send_second, small), "ray", pairs
            )
            part_first = keep_first + got_first
            part_second = keep_second + got_second
            small = small + got_small
            distance //= 2
    else:
        part_first = lax.psum_scatter(grad_first, "ray", scatter_dimension=0, tiled=True)
        part_second = lax.psum_scatter(grad_second, "ray", scatter_dimension=0, tiled=True)
        small = lax.psum(small, "ray")
    heads = grad_head.size
    hidden = bias_first.shape[0]
    small_sums = (
        small[:heads].reshape(grad_head.shape),
        small[heads : heads + hidden],
        small[heads + hidden : heads + 2 * hidden],
        small[heads + 2 * hidden :],
    )
    return (
        part_first[None],
        part_second[None],
        small_sums[0][None],
        small_sums[1][None],
        small_sums[2][None],
        small_sums[3][None],
    )


def solution(mesh):
    placed = (
        P(None, ("space", "ray"), None),
        P(("space", "ray"), None),
        P(("space", "ray"), None, None),
        P(("space", "ray"), None),
        P(None, ("space", "ray")),
        P(),
        P("space", None, None),
        P("space", None),
        P("space", None, None),
        P("space", None),
        P("space", None, None),
        P("space", None),
    )
    return jax.shard_map(
        per_device,
        mesh=mesh,
        in_specs=placed,
        out_specs=(
            P("space", "ray", None),
            P("space", "ray", None),
            P("space", None, None),
            P("space", None),
            P("space", None),
            P("space", None),
        ),
        check_vma=False,
    )
```

```python
import jax
import jax.numpy as jnp
from jax import lax
from jax.sharding import PartitionSpec as P
from jax.experimental import pallas as pl
from jax.experimental.pallas import tpu as pltpu

SEG_LEN = 32
SEGS = 8


two_pi = 6.283185307179586


def gate_of(value):
    return 0.5 * jnp.tanh(0.5 * value) + 0.5


def silu_slope(value):
    gate = gate_of(value)
    return gate * (1.0 + value * (1.0 - gate))


def turn_sin_cos(turns):
    quarter = jnp.floor(turns * 4.0 + 0.5)
    angle = (turns - quarter * 0.25) * two_pi
    square = angle * angle
    sine = angle * (
        1.0
        + square
        * (
            -1.0 / 6.0
            + square * (1.0 / 120.0 + square * (-1.0 / 5040.0 + square * (1.0 / 362880.0)))
        )
    )
    cosine = 1.0 + square * (
        -0.5
        + square
        * (
            1.0 / 24.0
            + square * (-1.0 / 720.0 + square * (1.0 / 40320.0 + square * (-1.0 / 3628800.0)))
        )
    )
    step = quarter - 4.0 * jnp.floor(quarter * 0.25)
    flip = step >= 2.0
    odd = (step == 1.0) | (step == 3.0)
    sin_out = jnp.where(odd, cosine, sine)
    cos_out = jnp.where(odd, sine, cosine)
    sin_out = jnp.where(flip, -sin_out, sin_out)
    cos_out = jnp.where(flip != odd, -cos_out, cos_out)
    return sin_out, cos_out


def encode(samples, fourier):
    turns = (
        samples[:, 0, :, None] * fourier[0]
        + samples[:, 1, :, None] * fourier[1]
        + samples[:, 2, :, None] * fourier[2]
    )
    sine, cosine = turn_sin_cos(turns)
    joined = jnp.concatenate([sine, cosine], axis=-1)
    return joined.astype(jnp.bfloat16).reshape(-1, joined.shape[-1])


def network(samples, fourier, params):
    first_weight, first_bias, second_weight, second_bias, head_weight, head_bias = params
    seg_count, length = (samples.shape[0], samples.shape[2])
    encoded = encode(samples, fourier)
    pre_first = jnp.dot(encoded, first_weight, preferred_element_type=jnp.float32) + first_bias
    act_first = (pre_first * gate_of(pre_first)).astype(jnp.bfloat16)
    pre_second = jnp.dot(act_first, second_weight, preferred_element_type=jnp.float32) + second_bias
    act_second = (pre_second * gate_of(pre_second)).astype(jnp.bfloat16)
    head_raw = (
        lax.dot_general(
            act_second, head_weight, (((1,), (1,)), ((), ())), preferred_element_type=jnp.float32
        )
        + head_bias
    )
    head_raw = head_raw.reshape(seg_count, length, 4)
    density = jax.nn.softplus(head_raw[..., 0])
    colour = jax.nn.sigmoid(head_raw[..., 1:])
    optical = density * samples[:, 3, :]
    inclusive = jnp.cumsum(optical, axis=1)
    enter_light = jnp.exp(optical - inclusive)
    leave_light = jnp.exp(-inclusive)
    weight = enter_light - leave_light
    seg_colour = jnp.sum(weight[..., None] * colour, axis=1)
    seg_log = -inclusive[:, -1]
    saved = (head_raw, colour, weight, leave_light)
    return (seg_colour, seg_log, saved)


def backward_kernel(
    place_ref, fourier_ref, w1_ref, b1_ref, w2_ref, b2_ref, wh_ref, raw_ref,
    g1_ref, gb1_ref, g2_ref, gb2_ref, gh_ref,
):
    @pl.when(pl.program_id(0) == 0)
    def _():
        g1_ref[...] = jnp.zeros_like(g1_ref)
        gb1_ref[...] = jnp.zeros_like(gb1_ref)
        g2_ref[...] = jnp.zeros_like(g2_ref)
        gb2_ref[...] = jnp.zeros_like(gb2_ref)
        gh_ref[...] = jnp.zeros_like(gh_ref)

    place = place_ref[...]
    fourier = fourier_ref[...]
    turns = (
        place[:, 0:1] * fourier[0:1, :]
        + place[:, 1:2] * fourier[1:2, :]
        + place[:, 2:3] * fourier[2:3, :]
    )
    sine, cosine = turn_sin_cos(turns)
    encoded = jnp.concatenate([sine, cosine], axis=1).astype(jnp.bfloat16)
    pre_first = jnp.dot(encoded, w1_ref[...], preferred_element_type=jnp.float32) + b1_ref[...]
    gate_first = gate_of(pre_first)
    act_first = (pre_first * gate_first).astype(jnp.bfloat16)
    pre_second = jnp.dot(act_first, w2_ref[...], preferred_element_type=jnp.float32) + b2_ref[...]
    gate_second = gate_of(pre_second)
    act_second = (pre_second * gate_second).astype(jnp.bfloat16).astype(jnp.float32)
    raw = raw_ref[...].astype(jnp.float32)
    head = wh_ref[...].astype(jnp.float32)
    back_second = (
        raw[:, 0:1] * head[0:1, :]
        + raw[:, 1:2] * head[1:2, :]
        + raw[:, 2:3] * head[2:3, :]
        + raw[:, 3:4] * head[3:4, :]
    )
    slope_second = gate_second * (1.0 + pre_second * (1.0 - gate_second))
    delta_second = (back_second * slope_second).astype(jnp.bfloat16)
    g2_ref[...] += lax.dot_general(
        act_first, delta_second, (((0,), (0,)), ((), ())), preferred_element_type=jnp.float32
    )
    gb2_ref[...] += jnp.sum(delta_second.astype(jnp.float32), axis=0, keepdims=True)
    back_first = lax.dot_general(
        delta_second, w2_ref[...], (((1,), (1,)), ((), ())), preferred_element_type=jnp.float32
    )
    slope_first = gate_first * (1.0 + pre_first * (1.0 - gate_first))
    delta_first = (back_first * slope_first).astype(jnp.bfloat16)
    g1_ref[...] += lax.dot_general(
        encoded, delta_first, (((0,), (0,)), ((), ())), preferred_element_type=jnp.float32
    )
    gb1_ref[...] += jnp.sum(delta_first.astype(jnp.float32), axis=0, keepdims=True)
    gh_ref[...] += jnp.concatenate(
        [jnp.sum(raw[:, c : c + 1] * act_second, axis=0, keepdims=True) for c in range(4)],
        axis=0,
    )


def backward(samples, fourier, params, saved, up_colour, up_log):
    first_weight, first_bias, second_weight, second_bias, head_weight, head_bias = params
    head_raw, colour, weight, leave_light = saved
    energy = jnp.sum(colour * up_colour[:, None, :], axis=-1)
    spent = weight * energy
    remaining = jnp.sum(spent, axis=1, keepdims=True) - jnp.cumsum(spent, axis=1)
    grad_optical = leave_light * energy - remaining - up_log[:, None]
    grad_density = grad_optical * samples[:, 3, :] * jax.nn.sigmoid(head_raw[..., 0])
    grad_tint = weight[..., None] * up_colour[:, None, :] * colour * (1.0 - colour)
    grad_raw = (
        jnp.concatenate([grad_density[..., None], grad_tint], axis=-1)
        .reshape(-1, 4)
        .astype(jnp.bfloat16)
    )
    grad_head_bias = jnp.sum(grad_raw.astype(jnp.float32), axis=0)
    rows = grad_raw.shape[0]
    block = 512
    place = jnp.transpose(samples[:, :3, :], (0, 2, 1)).reshape(rows, 3)
    features = first_weight.shape[0]
    hidden = first_weight.shape[1]
    whole = lambda i: (0, 0)
    outs = pl.pallas_call(
        backward_kernel,
        grid=(rows // block,),
        in_specs=[
            pl.BlockSpec((block, 3), lambda i: (i, 0)),
            pl.BlockSpec(fourier.shape, whole),
            pl.BlockSpec(first_weight.shape, whole),
            pl.BlockSpec((1, hidden), whole),
            pl.BlockSpec(second_weight.shape, whole),
            pl.BlockSpec((1, hidden), whole),
            pl.BlockSpec(head_weight.shape, whole),
            pl.BlockSpec((block, 4), lambda i: (i, 0)),
        ],
        out_specs=[
            pl.BlockSpec((features, hidden), whole),
            pl.BlockSpec((1, hidden), whole),
            pl.BlockSpec((hidden, hidden), whole),
            pl.BlockSpec((1, hidden), whole),
            pl.BlockSpec((4, hidden), whole),
        ],
        out_shape=[
            jax.ShapeDtypeStruct((features, hidden), jnp.float32),
            jax.ShapeDtypeStruct((1, hidden), jnp.float32),
            jax.ShapeDtypeStruct((hidden, hidden), jnp.float32),
            jax.ShapeDtypeStruct((1, hidden), jnp.float32),
            jax.ShapeDtypeStruct((4, hidden), jnp.float32),
        ],
        compiler_params=pltpu.CompilerParams(dimension_semantics=("arbitrary",)),
    )(
        place,
        fourier,
        first_weight,
        first_bias.reshape(1, hidden),
        second_weight,
        second_bias.reshape(1, hidden),
        head_weight,
        grad_raw,
    )
    grad_first, bias_first, grad_second, bias_second, grad_head = outs
    return (grad_first, grad_second, grad_head, bias_first[0], bias_second[0], grad_head_bias)


def composite(seg_colour, seg_log, depth_rank, pixel_rows):
    before = (depth_rank[:, None, :] < depth_rank[:, :, None]).astype(jnp.float32)
    prefix = jnp.exp(jnp.sum(before * seg_log[:, None, :], axis=2))
    up_colour = prefix[..., None] * pixel_rows[:, None, :]
    shaded = prefix * jnp.sum(seg_colour * pixel_rows[:, None, :], axis=2)
    up_log = jnp.sum(before * shaded[:, :, None], axis=1)
    return (up_colour, up_log)


def per_device(
    positions,
    spacing,
    assign,
    depth_rank,
    pixel_grad,
    fourier,
    first_weight,
    first_bias,
    second_weight,
    second_bias,
    head_weight,
    head_bias,
):
    groups = lax.axis_size("space")
    ray_count = positions.shape[1]
    total = ray_count * SEGS
    capacity = 3 * total // (2 * groups)
    slot_count = capacity * groups
    owner = assign.reshape(total)
    member = (owner[:, None] == jnp.arange(groups, dtype=jnp.int32)[None, :]).astype(jnp.int32)
    earlier = jnp.cumsum(member, axis=0) - member
    within = jnp.sum(earlier * member, axis=1)
    target = owner * capacity + within
    dispatch = (target[:, None] == jnp.arange(slot_count, dtype=jnp.int32)[None, :]).astype(
        jnp.float32
    )
    seg_pos = jnp.transpose(positions.reshape(3, total, SEG_LEN), (1, 0, 2))
    seg_gap = spacing.reshape(total, 1, SEG_LEN)
    segments = jnp.concatenate([seg_pos, seg_gap], axis=1).reshape(total, 4 * SEG_LEN)
    outgoing = lax.dot_general(
        dispatch,
        segments,
        (((0,), (0,)), ((), ())),
        precision=lax.Precision.HIGHEST,
        preferred_element_type=jnp.float32,
    )
    outgoing = outgoing.reshape(groups, capacity, 4 * SEG_LEN)
    arrived = lax.all_to_all(outgoing, "space", split_axis=0, concat_axis=0, tiled=True)
    samples = arrived.reshape(slot_count, 4, SEG_LEN)
    params = tuple(
        (
            item[0]
            for item in (
                first_weight,
                first_bias,
                second_weight,
                second_bias,
                head_weight,
                head_bias,
            )
        )
    )
    seg_colour, seg_log, saved = network(samples, fourier, params)
    partials = jnp.concatenate([seg_colour.T, seg_log[None, :]], axis=0).reshape(
        4, groups, capacity
    )
    returned = lax.all_to_all(partials, "space", split_axis=1, concat_axis=1, tiled=True).reshape(
        4, slot_count
    )
    mine = lax.dot_general(
        dispatch,
        returned,
        (((1,), (1,)), ((), ())),
        precision=lax.Precision.HIGHEST,
        preferred_element_type=jnp.float32,
    )
    up_colour, up_log = composite(
        mine[:, :3].reshape(ray_count, SEGS, 3),
        mine[:, 3].reshape(ray_count, SEGS),
        depth_rank,
        pixel_grad.T,
    )
    upstream = jnp.concatenate([up_colour.reshape(total, 3), up_log.reshape(total, 1)], axis=1)
    sendback = lax.dot_general(
        upstream,
        dispatch,
        (((0,), (0,)), ((), ())),
        precision=lax.Precision.HIGHEST,
        preferred_element_type=jnp.float32,
    )
    sendback = sendback.reshape(4, groups, capacity)
    received = lax.all_to_all(sendback, "space", split_axis=1, concat_axis=1, tiled=True)
    received = received.reshape(4, slot_count).T
    totals = backward(samples, fourier, params, saved, received[:, :3], received[:, 3])
    grad_first, grad_second, grad_head, bias_first, bias_second, bias_head = totals
    replicas = lax.axis_size("ray")
    small = jnp.concatenate(
        [grad_head.reshape(-1), bias_first, bias_second, bias_head], axis=0
    )
    if replicas & (replicas - 1) == 0:
        position = lax.axis_index("ray")
        part_first, part_second = grad_first, grad_second
        distance = replicas // 2
        while distance >= 1:
            pairs = [(i, i ^ distance) for i in range(replicas)]
            half = part_first.shape[0] // 2
            upper = (position // distance) % 2
            keep_first = lax.dynamic_slice_in_dim(part_first, upper * half, half, 0)
            send_first = lax.dynamic_slice_in_dim(part_first, (1 - upper) * half, half, 0)
            keep_second = lax.dynamic_slice_in_dim(part_second, upper * half, half, 0)
            send_second = lax.dynamic_slice_in_dim(part_second, (1 - upper) * half, half, 0)
            got_first, got_second, got_small = lax.ppermute(
                (send_first, send_second, small), "ray", pairs
            )
            part_first = keep_first + got_first
            part_second = keep_second + got_second
            small = small + got_small
            distance //= 2
    else:
        part_first = lax.psum_scatter(grad_first, "ray", scatter_dimension=0, tiled=True)
        part_second = lax.psum_scatter(grad_second, "ray", scatter_dimension=0, tiled=True)
        small = lax.psum(small, "ray")
    heads = grad_head.size
    hidden = bias_first.shape[0]
    small_sums = (
        small[:heads].reshape(grad_head.shape),
        small[heads : heads + hidden],
        small[heads + hidden : heads + 2 * hidden],
        small[heads + 2 * hidden :],
    )
    return (
        part_first[None],
        part_second[None],
        small_sums[0][None],
        small_sums[1][None],
        small_sums[2][None],
        small_sums[3][None],
    )


def solution(mesh):
    placed = (
        P(None, ("space", "ray"), None),
        P(("space", "ray"), None),
        P(("space", "ray"), None, None),
        P(("space", "ray"), None),
        P(None, ("space", "ray")),
        P(),
        P("space", None, None),
        P("space", None),
        P("space", None, None),
        P("space", None),
        P("space", None, None),
        P("space", None),
    )
    return jax.shard_map(
        per_device,
        mesh=mesh,
        in_specs=placed,
        out_specs=(
            P("space", "ray", None),
            P("space", "ray", None),
            P("space", None, None),
            P("space", None),
            P("space", None),
            P("space", None),
        ),
        check_vma=False,
    )
```

```python
import jax
import jax.numpy as jnp
from jax import lax
from jax.sharding import PartitionSpec as P
from jax.experimental import pallas as pl
from jax.experimental.pallas import tpu as pltpu

SEG_LEN = 32
SEGS = 8


two_pi = 6.283185307179586


def gate_of(value):
    return 0.5 * jnp.tanh(0.5 * value) + 0.5


def silu_slope(value):
    gate = gate_of(value)
    return gate * (1.0 + value * (1.0 - gate))


def turn_sin_cos(turns):
    quarter = jnp.floor(turns * 4.0 + 0.5)
    angle = (turns - quarter * 0.25) * two_pi
    square = angle * angle
    sine = angle * (
        1.0
        + square
        * (
            -1.0 / 6.0
            + square * (1.0 / 120.0 + square * (-1.0 / 5040.0 + square * (1.0 / 362880.0)))
        )
    )
    cosine = 1.0 + square * (
        -0.5
        + square
        * (
            1.0 / 24.0
            + square * (-1.0 / 720.0 + square * (1.0 / 40320.0 + square * (-1.0 / 3628800.0)))
        )
    )
    step = quarter - 4.0 * jnp.floor(quarter * 0.25)
    flip = step >= 2.0
    odd = (step == 1.0) | (step == 3.0)
    sin_out = jnp.where(odd, cosine, sine)
    cos_out = jnp.where(odd, sine, cosine)
    sin_out = jnp.where(flip, -sin_out, sin_out)
    cos_out = jnp.where(flip != odd, -cos_out, cos_out)
    return sin_out, cos_out


def encode(samples, fourier):
    turns = (
        samples[:, 0, :, None] * fourier[0]
        + samples[:, 1, :, None] * fourier[1]
        + samples[:, 2, :, None] * fourier[2]
    )
    sine, cosine = turn_sin_cos(turns)
    joined = jnp.concatenate([sine, cosine], axis=-1)
    return joined.astype(jnp.bfloat16).reshape(-1, joined.shape[-1])


def network(samples, fourier, params):
    first_weight, first_bias, second_weight, second_bias, head_weight, head_bias = params
    seg_count, length = (samples.shape[0], samples.shape[2])
    encoded = encode(samples, fourier)
    pre_first = jnp.dot(encoded, first_weight, preferred_element_type=jnp.float32) + first_bias
    act_first = (pre_first * gate_of(pre_first)).astype(jnp.bfloat16)
    pre_second = jnp.dot(act_first, second_weight, preferred_element_type=jnp.float32) + second_bias
    act_second = (pre_second * gate_of(pre_second)).astype(jnp.bfloat16)
    head_raw = (
        lax.dot_general(
            act_second, head_weight, (((1,), (1,)), ((), ())), preferred_element_type=jnp.float32
        )
        + head_bias
    )
    head_raw = head_raw.reshape(seg_count, length, 4)
    density = jax.nn.softplus(head_raw[..., 0])
    colour = jax.nn.sigmoid(head_raw[..., 1:])
    optical = density * samples[:, 3, :]
    inclusive = jnp.cumsum(optical, axis=1)
    enter_light = jnp.exp(optical - inclusive)
    leave_light = jnp.exp(-inclusive)
    weight = enter_light - leave_light
    seg_colour = jnp.sum(weight[..., None] * colour, axis=1)
    seg_log = -inclusive[:, -1]
    saved = (head_raw, colour, weight, leave_light)
    return (seg_colour, seg_log, saved)


def backward_kernel(
    place_ref, fourier_ref, w1_ref, b1_ref, w2_ref, b2_ref, wh_ref, raw_ref,
    g1_ref, gb1_ref, g2_ref, gb2_ref, gh_ref,
):
    @pl.when(pl.program_id(0) == 0)
    def _():
        g1_ref[...] = jnp.zeros_like(g1_ref)
        gb1_ref[...] = jnp.zeros_like(gb1_ref)
        g2_ref[...] = jnp.zeros_like(g2_ref)
        gb2_ref[...] = jnp.zeros_like(gb2_ref)
        gh_ref[...] = jnp.zeros_like(gh_ref)

    place = place_ref[...]
    fourier = fourier_ref[...]
    turns = (
        place[:, 0:1] * fourier[0:1, :]
        + place[:, 1:2] * fourier[1:2, :]
        + place[:, 2:3] * fourier[2:3, :]
    )
    sine, cosine = turn_sin_cos(turns)
    encoded = jnp.concatenate([sine, cosine], axis=1).astype(jnp.bfloat16)
    pre_first = jnp.dot(encoded, w1_ref[...], preferred_element_type=jnp.float32) + b1_ref[...]
    gate_first = gate_of(pre_first)
    act_first = (pre_first * gate_first).astype(jnp.bfloat16)
    pre_second = jnp.dot(act_first, w2_ref[...], preferred_element_type=jnp.float32) + b2_ref[...]
    gate_second = gate_of(pre_second)
    act_second = (pre_second * gate_second).astype(jnp.bfloat16)
    raw = raw_ref[...]
    back_second = jnp.dot(raw, wh_ref[...], preferred_element_type=jnp.float32)
    slope_second = gate_second * (1.0 + pre_second * (1.0 - gate_second))
    delta_second = (back_second * slope_second).astype(jnp.bfloat16)
    g2_ref[...] += lax.dot_general(
        act_first, delta_second, (((0,), (0,)), ((), ())), preferred_element_type=jnp.float32
    )
    gb2_ref[...] += jnp.sum(delta_second.astype(jnp.float32), axis=0, keepdims=True)
    back_first = lax.dot_general(
        delta_second, w2_ref[...], (((1,), (1,)), ((), ())), preferred_element_type=jnp.float32
    )
    slope_first = gate_first * (1.0 + pre_first * (1.0 - gate_first))
    delta_first = (back_first * slope_first).astype(jnp.bfloat16)
    g1_ref[...] += lax.dot_general(
        encoded, delta_first, (((0,), (0,)), ((), ())), preferred_element_type=jnp.float32
    )
    gb1_ref[...] += jnp.sum(delta_first.astype(jnp.float32), axis=0, keepdims=True)
    gh_ref[...] += lax.dot_general(
        raw, act_second, (((0,), (0,)), ((), ())), preferred_element_type=jnp.float32
    )


def backward(samples, fourier, params, saved, up_colour, up_log):
    first_weight, first_bias, second_weight, second_bias, head_weight, head_bias = params
    head_raw, colour, weight, leave_light = saved
    energy = jnp.sum(colour * up_colour[:, None, :], axis=-1)
    spent = weight * energy
    remaining = jnp.sum(spent, axis=1, keepdims=True) - jnp.cumsum(spent, axis=1)
    grad_optical = leave_light * energy - remaining - up_log[:, None]
    grad_density = grad_optical * samples[:, 3, :] * jax.nn.sigmoid(head_raw[..., 0])
    grad_tint = weight[..., None] * up_colour[:, None, :] * colour * (1.0 - colour)
    grad_raw = (
        jnp.concatenate([grad_density[..., None], grad_tint], axis=-1)
        .reshape(-1, 4)
        .astype(jnp.bfloat16)
    )
    grad_head_bias = jnp.sum(grad_raw.astype(jnp.float32), axis=0)
    rows = grad_raw.shape[0]
    block = 1024
    place = jnp.transpose(samples[:, :3, :], (0, 2, 1)).reshape(rows, 3)
    features = first_weight.shape[0]
    hidden = first_weight.shape[1]
    whole = lambda i: (0, 0)
    outs = pl.pallas_call(
        backward_kernel,
        grid=(rows // block,),
        in_specs=[
            pl.BlockSpec((block, 3), lambda i: (i, 0)),
            pl.BlockSpec(fourier.shape, whole),
            pl.BlockSpec(first_weight.shape, whole),
            pl.BlockSpec((1, hidden), whole),
            pl.BlockSpec(second_weight.shape, whole),
            pl.BlockSpec((1, hidden), whole),
            pl.BlockSpec(head_weight.shape, whole),
            pl.BlockSpec((block, 4), lambda i: (i, 0)),
        ],
        out_specs=[
            pl.BlockSpec((features, hidden), whole),
            pl.BlockSpec((1, hidden), whole),
            pl.BlockSpec((hidden, hidden), whole),
            pl.BlockSpec((1, hidden), whole),
            pl.BlockSpec((4, hidden), whole),
        ],
        out_shape=[
            jax.ShapeDtypeStruct((features, hidden), jnp.float32),
            jax.ShapeDtypeStruct((1, hidden), jnp.float32),
            jax.ShapeDtypeStruct((hidden, hidden), jnp.float32),
            jax.ShapeDtypeStruct((1, hidden), jnp.float32),
            jax.ShapeDtypeStruct((4, hidden), jnp.float32),
        ],
        compiler_params=pltpu.CompilerParams(dimension_semantics=("arbitrary",)),
    )(
        place,
        fourier,
        first_weight,
        first_bias.reshape(1, hidden),
        second_weight,
        second_bias.reshape(1, hidden),
        head_weight,
        grad_raw,
    )
    grad_first, bias_first, grad_second, bias_second, grad_head = outs
    return (grad_first, grad_second, grad_head, bias_first[0], bias_second[0], grad_head_bias)


def composite(seg_colour, seg_log, depth_rank, pixel_rows):
    before = (depth_rank[:, None, :] < depth_rank[:, :, None]).astype(jnp.float32)
    prefix = jnp.exp(jnp.sum(before * seg_log[:, None, :], axis=2))
    up_colour = prefix[..., None] * pixel_rows[:, None, :]
    shaded = prefix * jnp.sum(seg_colour * pixel_rows[:, None, :], axis=2)
    up_log = jnp.sum(before * shaded[:, :, None], axis=1)
    return (up_colour, up_log)


def per_device(
    positions,
    spacing,
    assign,
    depth_rank,
    pixel_grad,
    fourier,
    first_weight,
    first_bias,
    second_weight,
    second_bias,
    head_weight,
    head_bias,
):
    groups = lax.axis_size("space")
    ray_count = positions.shape[1]
    total = ray_count * SEGS
    capacity = 3 * total // (2 * groups)
    slot_count = capacity * groups
    owner = assign.reshape(total)
    member = (owner[:, None] == jnp.arange(groups, dtype=jnp.int32)[None, :]).astype(jnp.int32)
    earlier = jnp.cumsum(member, axis=0) - member
    within = jnp.sum(earlier * member, axis=1)
    target = owner * capacity + within
    dispatch = (target[:, None] == jnp.arange(slot_count, dtype=jnp.int32)[None, :]).astype(
        jnp.float32
    )
    seg_pos = jnp.transpose(positions.reshape(3, total, SEG_LEN), (1, 0, 2))
    seg_gap = spacing.reshape(total, 1, SEG_LEN)
    segments = jnp.concatenate([seg_pos, seg_gap], axis=1).reshape(total, 4 * SEG_LEN)
    outgoing = lax.dot_general(
        dispatch,
        segments,
        (((0,), (0,)), ((), ())),
        precision=lax.Precision.HIGHEST,
        preferred_element_type=jnp.float32,
    )
    outgoing = outgoing.reshape(groups, capacity, 4 * SEG_LEN)
    arrived = lax.all_to_all(outgoing, "space", split_axis=0, concat_axis=0, tiled=True)
    samples = arrived.reshape(slot_count, 4, SEG_LEN)
    params = tuple(
        (
            item[0]
            for item in (
                first_weight,
                first_bias,
                second_weight,
                second_bias,
                head_weight,
                head_bias,
            )
        )
    )
    seg_colour, seg_log, saved = network(samples, fourier, params)
    partials = jnp.concatenate([seg_colour.T, seg_log[None, :]], axis=0).reshape(
        4, groups, capacity
    )
    returned = lax.all_to_all(partials, "space", split_axis=1, concat_axis=1, tiled=True).reshape(
        4, slot_count
    )
    mine = lax.dot_general(
        dispatch,
        returned,
        (((1,), (1,)), ((), ())),
        precision=lax.Precision.HIGHEST,
        preferred_element_type=jnp.float32,
    )
    up_colour, up_log = composite(
        mine[:, :3].reshape(ray_count, SEGS, 3),
        mine[:, 3].reshape(ray_count, SEGS),
        depth_rank,
        pixel_grad.T,
    )
    upstream = jnp.concatenate([up_colour.reshape(total, 3), up_log.reshape(total, 1)], axis=1)
    sendback = lax.dot_general(
        upstream,
        dispatch,
        (((0,), (0,)), ((), ())),
        precision=lax.Precision.HIGHEST,
        preferred_element_type=jnp.float32,
    )
    sendback = sendback.reshape(4, groups, capacity)
    received = lax.all_to_all(sendback, "space", split_axis=1, concat_axis=1, tiled=True)
    received = received.reshape(4, slot_count).T
    totals = backward(samples, fourier, params, saved, received[:, :3], received[:, 3])
    grad_first, grad_second, grad_head, bias_first, bias_second, bias_head = totals
    replicas = lax.axis_size("ray")
    small = jnp.concatenate(
        [grad_head.reshape(-1), bias_first, bias_second, bias_head], axis=0
    )
    if replicas & (replicas - 1) == 0:
        position = lax.axis_index("ray")
        part_first, part_second = grad_first, grad_second
        distance = replicas // 2
        while distance >= 1:
            pairs = [(i, i ^ distance) for i in range(replicas)]
            half = part_first.shape[0] // 2
            upper = (position // distance) % 2
            keep_first = lax.dynamic_slice_in_dim(part_first, upper * half, half, 0)
            send_first = lax.dynamic_slice_in_dim(part_first, (1 - upper) * half, half, 0)
            keep_second = lax.dynamic_slice_in_dim(part_second, upper * half, half, 0)
            send_second = lax.dynamic_slice_in_dim(part_second, (1 - upper) * half, half, 0)
            got_first, got_second, got_small = lax.ppermute(
                (send_first, send_second, small), "ray", pairs
            )
            part_first = keep_first + got_first
            part_second = keep_second + got_second
            small = small + got_small
            distance //= 2
    else:
        part_first = lax.psum_scatter(grad_first, "ray", scatter_dimension=0, tiled=True)
        part_second = lax.psum_scatter(grad_second, "ray", scatter_dimension=0, tiled=True)
        small = lax.psum(small, "ray")
    heads = grad_head.size
    hidden = bias_first.shape[0]
    small_sums = (
        small[:heads].reshape(grad_head.shape),
        small[heads : heads + hidden],
        small[heads + hidden : heads + 2 * hidden],
        small[heads + 2 * hidden :],
    )
    return (
        part_first[None],
        part_second[None],
        small_sums[0][None],
        small_sums[1][None],
        small_sums[2][None],
        small_sums[3][None],
    )


def solution(mesh):
    placed = (
        P(None, ("space", "ray"), None),
        P(("space", "ray"), None),
        P(("space", "ray"), None, None),
        P(("space", "ray"), None),
        P(None, ("space", "ray")),
        P(),
        P("space", None, None),
        P("space", None),
        P("space", None, None),
        P("space", None),
        P("space", None, None),
        P("space", None),
    )
    return jax.shard_map(
        per_device,
        mesh=mesh,
        in_specs=placed,
        out_specs=(
            P("space", "ray", None),
            P("space", "ray", None),
            P("space", None, None),
            P("space", None),
            P("space", None),
            P("space", None),
        ),
        check_vma=False,
    )
```

```python
import jax
import jax.numpy as jnp
from jax import lax
from jax.sharding import PartitionSpec as P
from jax.experimental import pallas as pl
from jax.experimental.pallas import tpu as pltpu

SEG_LEN = 32
SEGS = 8


two_pi = 6.283185307179586


def gate_of(value):
    return 0.5 * jnp.tanh(0.5 * value) + 0.5


def silu_slope(value):
    gate = gate_of(value)
    return gate * (1.0 + value * (1.0 - gate))


def turn_sin_cos(turns):
    quarter = jnp.floor(turns * 4.0 + 0.5)
    angle = (turns - quarter * 0.25) * two_pi
    square = angle * angle
    sine = angle * (
        1.0
        + square
        * (
            -1.0 / 6.0
            + square * (1.0 / 120.0 + square * (-1.0 / 5040.0 + square * (1.0 / 362880.0)))
        )
    )
    cosine = 1.0 + square * (
        -0.5
        + square
        * (
            1.0 / 24.0
            + square * (-1.0 / 720.0 + square * (1.0 / 40320.0 + square * (-1.0 / 3628800.0)))
        )
    )
    step = quarter - 4.0 * jnp.floor(quarter * 0.25)
    flip = step >= 2.0
    odd = (step == 1.0) | (step == 3.0)
    sin_out = jnp.where(odd, cosine, sine)
    cos_out = jnp.where(odd, sine, cosine)
    sin_out = jnp.where(flip, -sin_out, sin_out)
    cos_out = jnp.where(flip != odd, -cos_out, cos_out)
    return sin_out, cos_out


def encode(samples, fourier):
    turns = (
        samples[:, 0, :, None] * fourier[0]
        + samples[:, 1, :, None] * fourier[1]
        + samples[:, 2, :, None] * fourier[2]
    )
    sine, cosine = turn_sin_cos(turns)
    joined = jnp.concatenate([sine, cosine], axis=-1)
    return joined.astype(jnp.bfloat16).reshape(-1, joined.shape[-1])


def network(samples, fourier, params):
    first_weight, first_bias, second_weight, second_bias, head_weight, head_bias = params
    seg_count, length = (samples.shape[0], samples.shape[2])
    encoded = encode(samples, fourier)
    pre_first = jnp.dot(encoded, first_weight, preferred_element_type=jnp.float32) + first_bias
    act_first = (pre_first * gate_of(pre_first)).astype(jnp.bfloat16)
    pre_second = jnp.dot(act_first, second_weight, preferred_element_type=jnp.float32) + second_bias
    act_second = (pre_second * gate_of(pre_second)).astype(jnp.bfloat16)
    head_raw = (
        lax.dot_general(
            act_second, head_weight, (((1,), (1,)), ((), ())), preferred_element_type=jnp.float32
        )
        + head_bias
    )
    head_raw = head_raw.reshape(seg_count, length, 4)
    density = jax.nn.softplus(head_raw[..., 0])
    colour = jax.nn.sigmoid(head_raw[..., 1:])
    optical = density * samples[:, 3, :]
    inclusive = jnp.cumsum(optical, axis=1)
    enter_light = jnp.exp(optical - inclusive)
    leave_light = jnp.exp(-inclusive)
    weight = enter_light - leave_light
    seg_colour = jnp.sum(weight[..., None] * colour, axis=1)
    seg_log = -inclusive[:, -1]
    saved = (head_raw, colour, weight, leave_light)
    return (seg_colour, seg_log, saved)


def backward_kernel(
    place_ref, fourier_ref, w1_ref, b1_ref, w2_ref, b2_ref, wh_ref, raw_ref,
    g1_ref, gb1_ref, g2_ref, gb2_ref, gh_ref,
):
    @pl.when(pl.program_id(0) == 0)
    def _():
        g1_ref[...] = jnp.zeros_like(g1_ref)
        gb1_ref[...] = jnp.zeros_like(gb1_ref)
        g2_ref[...] = jnp.zeros_like(g2_ref)
        gb2_ref[...] = jnp.zeros_like(gb2_ref)
        gh_ref[...] = jnp.zeros_like(gh_ref)

    place = place_ref[...]
    fourier = fourier_ref[...]
    turns = (
        place[:, 0:1] * fourier[0:1, :]
        + place[:, 1:2] * fourier[1:2, :]
        + place[:, 2:3] * fourier[2:3, :]
    )
    sine, cosine = turn_sin_cos(turns)
    encoded = jnp.concatenate([sine, cosine], axis=1).astype(jnp.bfloat16)
    pre_first = jnp.dot(encoded, w1_ref[...], preferred_element_type=jnp.float32) + b1_ref[...]
    gate_first = gate_of(pre_first)
    act_first = (pre_first * gate_first).astype(jnp.bfloat16)
    pre_second = jnp.dot(act_first, w2_ref[...], preferred_element_type=jnp.float32) + b2_ref[...]
    gate_second = gate_of(pre_second)
    act_second = (pre_second * gate_second).astype(jnp.bfloat16)
    raw = raw_ref[...]
    back_second = jnp.dot(raw, wh_ref[...], preferred_element_type=jnp.float32)
    slope_second = gate_second * (1.0 + pre_second * (1.0 - gate_second))
    delta_second = (back_second * slope_second).astype(jnp.bfloat16)
    g2_ref[...] += lax.dot_general(
        act_first, delta_second, (((0,), (0,)), ((), ())), preferred_element_type=jnp.float32
    )
    gb2_ref[...] += jnp.sum(delta_second.astype(jnp.float32), axis=0, keepdims=True)
    back_first = lax.dot_general(
        delta_second, w2_ref[...], (((1,), (1,)), ((), ())), preferred_element_type=jnp.float32
    )
    slope_first = gate_first * (1.0 + pre_first * (1.0 - gate_first))
    delta_first = (back_first * slope_first).astype(jnp.bfloat16)
    g1_ref[...] += lax.dot_general(
        encoded, delta_first, (((0,), (0,)), ((), ())), preferred_element_type=jnp.float32
    )
    gb1_ref[...] += jnp.sum(delta_first.astype(jnp.float32), axis=0, keepdims=True)
    gh_ref[...] += lax.dot_general(
        raw, act_second, (((0,), (0,)), ((), ())), preferred_element_type=jnp.float32
    )


def backward(samples, fourier, params, saved, up_colour, up_log):
    first_weight, first_bias, second_weight, second_bias, head_weight, head_bias = params
    head_raw, colour, weight, leave_light = saved
    energy = jnp.sum(colour * up_colour[:, None, :], axis=-1)
    spent = weight * energy
    remaining = jnp.sum(spent, axis=1, keepdims=True) - jnp.cumsum(spent, axis=1)
    grad_optical = leave_light * energy - remaining - up_log[:, None]
    grad_density = grad_optical * samples[:, 3, :] * jax.nn.sigmoid(head_raw[..., 0])
    grad_tint = weight[..., None] * up_colour[:, None, :] * colour * (1.0 - colour)
    grad_raw = (
        jnp.concatenate([grad_density[..., None], grad_tint], axis=-1)
        .reshape(-1, 4)
        .astype(jnp.bfloat16)
    )
    grad_head_bias = jnp.sum(grad_raw.astype(jnp.float32), axis=0)
    rows = grad_raw.shape[0]
    block = 1024
    place = jnp.transpose(samples[:, :3, :], (0, 2, 1)).reshape(rows, 3)
    features = first_weight.shape[0]
    hidden = first_weight.shape[1]
    whole = lambda i: (0, 0)
    outs = pl.pallas_call(
        backward_kernel,
        grid=(rows // block,),
        in_specs=[
            pl.BlockSpec((block, 3), lambda i: (i, 0)),
            pl.BlockSpec(fourier.shape, whole),
            pl.BlockSpec(first_weight.shape, whole),
            pl.BlockSpec((1, hidden), whole),
            pl.BlockSpec(second_weight.shape, whole),
            pl.BlockSpec((1, hidden), whole),
            pl.BlockSpec(head_weight.shape, whole),
            pl.BlockSpec((block, 4), lambda i: (i, 0)),
        ],
        out_specs=[
            pl.BlockSpec((features, hidden), whole),
            pl.BlockSpec((1, hidden), whole),
            pl.BlockSpec((hidden, hidden), whole),
            pl.BlockSpec((1, hidden), whole),
            pl.BlockSpec((4, hidden), whole),
        ],
        out_shape=[
            jax.ShapeDtypeStruct((features, hidden), jnp.float32),
            jax.ShapeDtypeStruct((1, hidden), jnp.float32),
            jax.ShapeDtypeStruct((hidden, hidden), jnp.float32),
            jax.ShapeDtypeStruct((1, hidden), jnp.float32),
            jax.ShapeDtypeStruct((4, hidden), jnp.float32),
        ],
        compiler_params=pltpu.CompilerParams(dimension_semantics=("arbitrary",)),
    )(
        place,
        fourier,
        first_weight,
        first_bias.reshape(1, hidden),
        second_weight,
        second_bias.reshape(1, hidden),
        head_weight,
        grad_raw,
    )
    grad_first, bias_first, grad_second, bias_second, grad_head = outs
    return (grad_first, grad_second, grad_head, bias_first[0], bias_second[0], grad_head_bias)


def composite(seg_colour, seg_log, depth_rank, pixel_rows):
    before = (depth_rank[:, None, :] < depth_rank[:, :, None]).astype(jnp.float32)
    prefix = jnp.exp(jnp.sum(before * seg_log[:, None, :], axis=2))
    up_colour = prefix[..., None] * pixel_rows[:, None, :]
    shaded = prefix * jnp.sum(seg_colour * pixel_rows[:, None, :], axis=2)
    up_log = jnp.sum(before * shaded[:, :, None], axis=1)
    return (up_colour, up_log)


def per_device(
    positions,
    spacing,
    assign,
    depth_rank,
    pixel_grad,
    fourier,
    first_weight,
    first_bias,
    second_weight,
    second_bias,
    head_weight,
    head_bias,
):
    groups = lax.axis_size("space")
    ray_count = positions.shape[1]
    total = ray_count * SEGS
    capacity = 3 * total // (2 * groups)
    slot_count = capacity * groups
    owner = assign.reshape(total)
    member = (owner[:, None] == jnp.arange(groups, dtype=jnp.int32)[None, :]).astype(jnp.int32)
    earlier = jnp.cumsum(member, axis=0) - member
    within = jnp.sum(earlier * member, axis=1)
    target = owner * capacity + within
    dispatch = (target[:, None] == jnp.arange(slot_count, dtype=jnp.int32)[None, :]).astype(
        jnp.float32
    )
    seg_pos = jnp.transpose(positions.reshape(3, total, SEG_LEN), (1, 0, 2))
    seg_gap = spacing.reshape(total, 1, SEG_LEN)
    segments = jnp.concatenate([seg_pos, seg_gap], axis=1).reshape(total, 4 * SEG_LEN)
    outgoing = lax.dot_general(
        dispatch,
        segments,
        (((0,), (0,)), ((), ())),
        precision=lax.Precision.HIGHEST,
        preferred_element_type=jnp.float32,
    )
    outgoing = outgoing.reshape(groups, capacity, 4 * SEG_LEN)
    arrived = lax.all_to_all(outgoing, "space", split_axis=0, concat_axis=0, tiled=True)
    samples = arrived.reshape(slot_count, 4, SEG_LEN)
    params = tuple(
        (
            item[0]
            for item in (
                first_weight,
                first_bias,
                second_weight,
                second_bias,
                head_weight,
                head_bias,
            )
        )
    )
    seg_colour, seg_log, saved = network(samples, fourier, params)
    partials = jnp.concatenate([seg_colour.T, seg_log[None, :]], axis=0).reshape(
        4, groups, capacity
    )
    returned = lax.all_to_all(partials, "space", split_axis=1, concat_axis=1, tiled=True).reshape(
        4, slot_count
    )
    mine = lax.dot_general(
        dispatch,
        returned,
        (((1,), (1,)), ((), ())),
        precision=lax.Precision.HIGHEST,
        preferred_element_type=jnp.float32,
    )
    up_colour, up_log = composite(
        mine[:, :3].reshape(ray_count, SEGS, 3),
        mine[:, 3].reshape(ray_count, SEGS),
        depth_rank,
        pixel_grad.T,
    )
    upstream = jnp.concatenate([up_colour.reshape(total, 3), up_log.reshape(total, 1)], axis=1)
    sendback = lax.dot_general(
        upstream,
        dispatch,
        (((0,), (0,)), ((), ())),
        precision=lax.Precision.HIGHEST,
        preferred_element_type=jnp.float32,
    )
    sendback = sendback.reshape(4, groups, capacity)
    received = lax.all_to_all(sendback, "space", split_axis=1, concat_axis=1, tiled=True)
    received = received.reshape(4, slot_count).T
    totals = backward(samples, fourier, params, saved, received[:, :3], received[:, 3])
    grad_first, grad_second, grad_head, bias_first, bias_second, bias_head = totals
    replicas = lax.axis_size("ray")
    small = jnp.concatenate(
        [grad_head.reshape(-1), bias_first, bias_second, bias_head], axis=0
    )
    if replicas == 2:
        position = lax.axis_index("ray")
        got_first, got_second, got_small = lax.ppermute(
            (grad_first, grad_second, small), "ray", [(0, 1), (1, 0)]
        )
        rows_first = grad_first.shape[0] // 2
        rows_second = grad_second.shape[0] // 2
        part_first = lax.dynamic_slice_in_dim(
            grad_first + got_first, position * rows_first, rows_first, 0
        )
        part_second = lax.dynamic_slice_in_dim(
            grad_second + got_second, position * rows_second, rows_second, 0
        )
        small = small + got_small
    elif replicas & (replicas - 1) == 0:
        position = lax.axis_index("ray")
        part_first, part_second = grad_first, grad_second
        distance = replicas // 2
        while distance >= 1:
            pairs = [(i, i ^ distance) for i in range(replicas)]
            half = part_first.shape[0] // 2
            upper = (position // distance) % 2
            keep_first = lax.dynamic_slice_in_dim(part_first, upper * half, half, 0)
            send_first = lax.dynamic_slice_in_dim(part_first, (1 - upper) * half, half, 0)
            keep_second = lax.dynamic_slice_in_dim(part_second, upper * half, half, 0)
            send_second = lax.dynamic_slice_in_dim(part_second, (1 - upper) * half, half, 0)
            got_first, got_second, got_small = lax.ppermute(
                (send_first, send_second, small), "ray", pairs
            )
            part_first = keep_first + got_first
            part_second = keep_second + got_second
            small = small + got_small
            distance //= 2
    else:
        part_first = lax.psum_scatter(grad_first, "ray", scatter_dimension=0, tiled=True)
        part_second = lax.psum_scatter(grad_second, "ray", scatter_dimension=0, tiled=True)
        small = lax.psum(small, "ray")
    heads = grad_head.size
    hidden = bias_first.shape[0]
    small_sums = (
        small[:heads].reshape(grad_head.shape),
        small[heads : heads + hidden],
        small[heads + hidden : heads + 2 * hidden],
        small[heads + 2 * hidden :],
    )
    return (
        part_first[None],
        part_second[None],
        small_sums[0][None],
        small_sums[1][None],
        small_sums[2][None],
        small_sums[3][None],
    )


def solution(mesh):
    placed = (
        P(None, ("space", "ray"), None),
        P(("space", "ray"), None),
        P(("space", "ray"), None, None),
        P(("space", "ray"), None),
        P(None, ("space", "ray")),
        P(),
        P("space", None, None),
        P("space", None),
        P("space", None, None),
        P("space", None),
        P("space", None, None),
        P("space", None),
    )
    return jax.shard_map(
        per_device,
        mesh=mesh,
        in_specs=placed,
        out_specs=(
            P("space", "ray", None),
            P("space", "ray", None),
            P("space", None, None),
            P("space", None),
            P("space", None),
            P("space", None),
        ),
        check_vma=False,
    )
```

```python
import jax
import jax.numpy as jnp
from jax import lax
from jax.sharding import PartitionSpec as P
from jax.experimental import pallas as pl
from jax.experimental.pallas import tpu as pltpu

SEG_LEN = 32
SEGS = 8


two_pi = 6.283185307179586


def gate_of(value):
    return 0.5 * jnp.tanh(0.5 * value) + 0.5


def silu_slope(value):
    gate = gate_of(value)
    return gate * (1.0 + value * (1.0 - gate))


def turn_sin_cos(turns):
    quarter = jnp.floor(turns * 4.0 + 0.5)
    angle = (turns - quarter * 0.25) * two_pi
    square = angle * angle
    sine = angle * (
        1.0
        + square
        * (
            -1.0 / 6.0
            + square * (1.0 / 120.0 + square * (-1.0 / 5040.0 + square * (1.0 / 362880.0)))
        )
    )
    cosine = 1.0 + square * (
        -0.5
        + square
        * (
            1.0 / 24.0
            + square * (-1.0 / 720.0 + square * (1.0 / 40320.0 + square * (-1.0 / 3628800.0)))
        )
    )
    step = quarter - 4.0 * jnp.floor(quarter * 0.25)
    flip = step >= 2.0
    odd = (step == 1.0) | (step == 3.0)
    sin_out = jnp.where(odd, cosine, sine)
    cos_out = jnp.where(odd, sine, cosine)
    sin_out = jnp.where(flip, -sin_out, sin_out)
    cos_out = jnp.where(flip != odd, -cos_out, cos_out)
    return sin_out, cos_out


def encode(samples, fourier):
    turns = (
        samples[:, 0, :, None] * fourier[0]
        + samples[:, 1, :, None] * fourier[1]
        + samples[:, 2, :, None] * fourier[2]
    )
    sine, cosine = turn_sin_cos(turns)
    joined = jnp.concatenate([sine, cosine], axis=-1)
    return joined.astype(jnp.bfloat16).reshape(-1, joined.shape[-1])


def forward_kernel(
    place_ref, fourier_ref, w1_ref, b1_ref, w2_ref, b2_ref, wh_ref, bh_ref,
    enc_ref, a1_ref, a2_ref, s1_ref, s2_ref, head_ref,
):
    place = place_ref[...]
    fourier = fourier_ref[...]
    turns = (
        place[:, 0:1] * fourier[0:1, :]
        + place[:, 1:2] * fourier[1:2, :]
        + place[:, 2:3] * fourier[2:3, :]
    )
    sine, cosine = turn_sin_cos(turns)
    encoded = jnp.concatenate([sine, cosine], axis=1).astype(jnp.bfloat16)
    enc_ref[...] = encoded
    pre_first = jnp.dot(encoded, w1_ref[...], preferred_element_type=jnp.float32) + b1_ref[...]
    gate_first = gate_of(pre_first)
    act_first = (pre_first * gate_first).astype(jnp.bfloat16)
    a1_ref[...] = act_first
    s1_ref[...] = gate_first * (1.0 + pre_first * (1.0 - gate_first))
    pre_second = jnp.dot(act_first, w2_ref[...], preferred_element_type=jnp.float32) + b2_ref[...]
    gate_second = gate_of(pre_second)
    act_second = (pre_second * gate_second).astype(jnp.bfloat16)
    a2_ref[...] = act_second
    s2_ref[...] = gate_second * (1.0 + pre_second * (1.0 - gate_second))
    head_ref[...] = (
        lax.dot_general(
            act_second, wh_ref[...], (((1,), (1,)), ((), ())), preferred_element_type=jnp.float32
        )
        + bh_ref[...]
    )


def backward_kernel(
    enc_ref, a1_ref, a2_ref, s1_ref, s2_ref, raw_ref, w2_ref, wh_ref,
    g1_ref, gb1_ref, g2_ref, gb2_ref, gh_ref,
):
    @pl.when(pl.program_id(0) == 0)
    def _():
        g1_ref[...] = jnp.zeros_like(g1_ref)
        gb1_ref[...] = jnp.zeros_like(gb1_ref)
        g2_ref[...] = jnp.zeros_like(g2_ref)
        gb2_ref[...] = jnp.zeros_like(gb2_ref)
        gh_ref[...] = jnp.zeros_like(gh_ref)

    raw = raw_ref[...]
    back_second = jnp.dot(raw, wh_ref[...], preferred_element_type=jnp.float32)
    delta_second = (back_second * s2_ref[...]).astype(jnp.bfloat16)
    g2_ref[...] += lax.dot_general(
        a1_ref[...], delta_second, (((0,), (0,)), ((), ())), preferred_element_type=jnp.float32
    )
    gb2_ref[...] += jnp.sum(delta_second.astype(jnp.float32), axis=0, keepdims=True)
    back_first = lax.dot_general(
        delta_second, w2_ref[...], (((1,), (1,)), ((), ())), preferred_element_type=jnp.float32
    )
    delta_first = (back_first * s1_ref[...]).astype(jnp.bfloat16)
    g1_ref[...] += lax.dot_general(
        enc_ref[...], delta_first, (((0,), (0,)), ((), ())), preferred_element_type=jnp.float32
    )
    gb1_ref[...] += jnp.sum(delta_first.astype(jnp.float32), axis=0, keepdims=True)
    gh_ref[...] += lax.dot_general(
        raw, a2_ref[...], (((0,), (0,)), ((), ())), preferred_element_type=jnp.float32
    )


BLOCK = 1024


def forward_layers(samples, fourier, params):
    first_weight, first_bias, second_weight, second_bias, head_weight, head_bias = params
    rows = samples.shape[0] * samples.shape[2]
    place = jnp.transpose(samples[:, :3, :], (0, 2, 1)).reshape(rows, 3)
    features, hidden = first_weight.shape
    heads = head_weight.shape[0]
    whole = lambda i: (0, 0)
    by_row = lambda i: (i, 0)
    return pl.pallas_call(
        forward_kernel,
        grid=(rows // BLOCK,),
        in_specs=[
            pl.BlockSpec((BLOCK, 3), by_row),
            pl.BlockSpec(fourier.shape, whole),
            pl.BlockSpec(first_weight.shape, whole),
            pl.BlockSpec((1, hidden), whole),
            pl.BlockSpec(second_weight.shape, whole),
            pl.BlockSpec((1, hidden), whole),
            pl.BlockSpec(head_weight.shape, whole),
            pl.BlockSpec((1, heads), whole),
        ],
        out_specs=[
            pl.BlockSpec((BLOCK, features), by_row),
            pl.BlockSpec((BLOCK, hidden), by_row),
            pl.BlockSpec((BLOCK, hidden), by_row),
            pl.BlockSpec((BLOCK, hidden), by_row),
            pl.BlockSpec((BLOCK, hidden), by_row),
            pl.BlockSpec((BLOCK, heads), by_row),
        ],
        out_shape=[
            jax.ShapeDtypeStruct((rows, features), jnp.bfloat16),
            jax.ShapeDtypeStruct((rows, hidden), jnp.bfloat16),
            jax.ShapeDtypeStruct((rows, hidden), jnp.bfloat16),
            jax.ShapeDtypeStruct((rows, hidden), jnp.float32),
            jax.ShapeDtypeStruct((rows, hidden), jnp.float32),
            jax.ShapeDtypeStruct((rows, heads), jnp.float32),
        ],
        compiler_params=pltpu.CompilerParams(dimension_semantics=("arbitrary",)),
    )(
        place,
        fourier,
        first_weight,
        first_bias.reshape(1, hidden),
        second_weight,
        second_bias.reshape(1, hidden),
        head_weight,
        head_bias.reshape(1, heads),
    )


def network(samples, fourier, params):
    seg_count, length = (samples.shape[0], samples.shape[2])
    encoded, act_first, act_second, slope_first, slope_second, head_raw = forward_layers(
        samples, fourier, params
    )
    head_raw = head_raw.reshape(seg_count, length, 4)
    density = jax.nn.softplus(head_raw[..., 0])
    colour = jax.nn.sigmoid(head_raw[..., 1:])
    optical = density * samples[:, 3, :]
    inclusive = jnp.cumsum(optical, axis=1)
    enter_light = jnp.exp(optical - inclusive)
    leave_light = jnp.exp(-inclusive)
    weight = enter_light - leave_light
    seg_colour = jnp.sum(weight[..., None] * colour, axis=1)
    seg_log = -inclusive[:, -1]
    saved = (
        encoded, act_first, act_second, slope_first, slope_second,
        head_raw, colour, weight, leave_light,
    )
    return (seg_colour, seg_log, saved)


def backward(samples, fourier, params, saved, up_colour, up_log):
    first_weight, first_bias, second_weight, second_bias, head_weight, head_bias = params
    encoded, act_first, act_second, slope_first, slope_second = saved[:5]
    head_raw, colour, weight, leave_light = saved[5:]
    energy = jnp.sum(colour * up_colour[:, None, :], axis=-1)
    spent = weight * energy
    remaining = jnp.sum(spent, axis=1, keepdims=True) - jnp.cumsum(spent, axis=1)
    grad_optical = leave_light * energy - remaining - up_log[:, None]
    grad_density = grad_optical * samples[:, 3, :] * jax.nn.sigmoid(head_raw[..., 0])
    grad_tint = weight[..., None] * up_colour[:, None, :] * colour * (1.0 - colour)
    grad_raw = (
        jnp.concatenate([grad_density[..., None], grad_tint], axis=-1)
        .reshape(-1, 4)
        .astype(jnp.bfloat16)
    )
    grad_head_bias = jnp.sum(grad_raw.astype(jnp.float32), axis=0)
    rows = grad_raw.shape[0]
    features, hidden = first_weight.shape
    whole = lambda i: (0, 0)
    by_row = lambda i: (i, 0)
    outs = pl.pallas_call(
        backward_kernel,
        grid=(rows // BLOCK,),
        in_specs=[
            pl.BlockSpec((BLOCK, features), by_row),
            pl.BlockSpec((BLOCK, hidden), by_row),
            pl.BlockSpec((BLOCK, hidden), by_row),
            pl.BlockSpec((BLOCK, hidden), by_row),
            pl.BlockSpec((BLOCK, hidden), by_row),
            pl.BlockSpec((BLOCK, 4), by_row),
            pl.BlockSpec(second_weight.shape, whole),
            pl.BlockSpec(head_weight.shape, whole),
        ],
        out_specs=[
            pl.BlockSpec((features, hidden), whole),
            pl.BlockSpec((1, hidden), whole),
            pl.BlockSpec((hidden, hidden), whole),
            pl.BlockSpec((1, hidden), whole),
            pl.BlockSpec((4, hidden), whole),
        ],
        out_shape=[
            jax.ShapeDtypeStruct((features, hidden), jnp.float32),
            jax.ShapeDtypeStruct((1, hidden), jnp.float32),
            jax.ShapeDtypeStruct((hidden, hidden), jnp.float32),
            jax.ShapeDtypeStruct((1, hidden), jnp.float32),
            jax.ShapeDtypeStruct((4, hidden), jnp.float32),
        ],
        compiler_params=pltpu.CompilerParams(dimension_semantics=("arbitrary",)),
    )(
        encoded, act_first, act_second, slope_first, slope_second, grad_raw,
        second_weight, head_weight,
    )
    grad_first, bias_first, grad_second, bias_second, grad_head = outs
    return (grad_first, grad_second, grad_head, bias_first[0], bias_second[0], grad_head_bias)


def composite(seg_colour, seg_log, depth_rank, pixel_rows):
    before = (depth_rank[:, None, :] < depth_rank[:, :, None]).astype(jnp.float32)
    prefix = jnp.exp(jnp.sum(before * seg_log[:, None, :], axis=2))
    up_colour = prefix[..., None] * pixel_rows[:, None, :]
    shaded = prefix * jnp.sum(seg_colour * pixel_rows[:, None, :], axis=2)
    up_log = jnp.sum(before * shaded[:, :, None], axis=1)
    return (up_colour, up_log)


def per_device(
    positions,
    spacing,
    assign,
    depth_rank,
    pixel_grad,
    fourier,
    first_weight,
    first_bias,
    second_weight,
    second_bias,
    head_weight,
    head_bias,
):
    groups = lax.axis_size("space")
    ray_count = positions.shape[1]
    total = ray_count * SEGS
    capacity = 3 * total // (2 * groups)
    slot_count = capacity * groups
    owner = assign.reshape(total)
    member = (owner[:, None] == jnp.arange(groups, dtype=jnp.int32)[None, :]).astype(jnp.int32)
    earlier = jnp.cumsum(member, axis=0) - member
    within = jnp.sum(earlier * member, axis=1)
    target = owner * capacity + within
    dispatch = (target[:, None] == jnp.arange(slot_count, dtype=jnp.int32)[None, :]).astype(
        jnp.float32
    )
    seg_pos = jnp.transpose(positions.reshape(3, total, SEG_LEN), (1, 0, 2))
    seg_gap = spacing.reshape(total, 1, SEG_LEN)
    segments = jnp.concatenate([seg_pos, seg_gap], axis=1).reshape(total, 4 * SEG_LEN)
    outgoing = lax.dot_general(
        dispatch,
        segments,
        (((0,), (0,)), ((), ())),
        precision=lax.Precision.HIGHEST,
        preferred_element_type=jnp.float32,
    )
    outgoing = outgoing.reshape(groups, capacity, 4 * SEG_LEN)
    arrived = lax.all_to_all(outgoing, "space", split_axis=0, concat_axis=0, tiled=True)
    samples = arrived.reshape(slot_count, 4, SEG_LEN)
    params = tuple(
        (
            item[0]
            for item in (
                first_weight,
                first_bias,
                second_weight,
                second_bias,
                head_weight,
                head_bias,
            )
        )
    )
    seg_colour, seg_log, saved = network(samples, fourier, params)
    partials = jnp.concatenate([seg_colour.T, seg_log[None, :]], axis=0).reshape(
        4, groups, capacity
    )
    returned = lax.all_to_all(partials, "space", split_axis=1, concat_axis=1, tiled=True).reshape(
        4, slot_count
    )
    mine = lax.dot_general(
        dispatch,
        returned,
        (((1,), (1,)), ((), ())),
        precision=lax.Precision.HIGHEST,
        preferred_element_type=jnp.float32,
    )
    up_colour, up_log = composite(
        mine[:, :3].reshape(ray_count, SEGS, 3),
        mine[:, 3].reshape(ray_count, SEGS),
        depth_rank,
        pixel_grad.T,
    )
    upstream = jnp.concatenate([up_colour.reshape(total, 3), up_log.reshape(total, 1)], axis=1)
    sendback = lax.dot_general(
        upstream,
        dispatch,
        (((0,), (0,)), ((), ())),
        precision=lax.Precision.HIGHEST,
        preferred_element_type=jnp.float32,
    )
    sendback = sendback.reshape(4, groups, capacity)
    received = lax.all_to_all(sendback, "space", split_axis=1, concat_axis=1, tiled=True)
    received = received.reshape(4, slot_count).T
    totals = backward(samples, fourier, params, saved, received[:, :3], received[:, 3])
    grad_first, grad_second, grad_head, bias_first, bias_second, bias_head = totals
    replicas = lax.axis_size("ray")
    small = jnp.concatenate(
        [grad_head.reshape(-1), bias_first, bias_second, bias_head], axis=0
    )
    if replicas == 2:
        position = lax.axis_index("ray")
        got_first, got_second, got_small = lax.ppermute(
            (grad_first, grad_second, small), "ray", [(0, 1), (1, 0)]
        )
        rows_first = grad_first.shape[0] // 2
        rows_second = grad_second.shape[0] // 2
        part_first = lax.dynamic_slice_in_dim(
            grad_first + got_first, position * rows_first, rows_first, 0
        )
        part_second = lax.dynamic_slice_in_dim(
            grad_second + got_second, position * rows_second, rows_second, 0
        )
        small = small + got_small
    elif replicas & (replicas - 1) == 0:
        position = lax.axis_index("ray")
        part_first, part_second = grad_first, grad_second
        distance = replicas // 2
        while distance >= 1:
            pairs = [(i, i ^ distance) for i in range(replicas)]
            half = part_first.shape[0] // 2
            upper = (position // distance) % 2
            keep_first = lax.dynamic_slice_in_dim(part_first, upper * half, half, 0)
            send_first = lax.dynamic_slice_in_dim(part_first, (1 - upper) * half, half, 0)
            keep_second = lax.dynamic_slice_in_dim(part_second, upper * half, half, 0)
            send_second = lax.dynamic_slice_in_dim(part_second, (1 - upper) * half, half, 0)
            got_first, got_second, got_small = lax.ppermute(
                (send_first, send_second, small), "ray", pairs
            )
            part_first = keep_first + got_first
            part_second = keep_second + got_second
            small = small + got_small
            distance //= 2
    else:
        part_first = lax.psum_scatter(grad_first, "ray", scatter_dimension=0, tiled=True)
        part_second = lax.psum_scatter(grad_second, "ray", scatter_dimension=0, tiled=True)
        small = lax.psum(small, "ray")
    heads = grad_head.size
    hidden = bias_first.shape[0]
    small_sums = (
        small[:heads].reshape(grad_head.shape),
        small[heads : heads + hidden],
        small[heads + hidden : heads + 2 * hidden],
        small[heads + 2 * hidden :],
    )
    return (
        part_first[None],
        part_second[None],
        small_sums[0][None],
        small_sums[1][None],
        small_sums[2][None],
        small_sums[3][None],
    )


def solution(mesh):
    placed = (
        P(None, ("space", "ray"), None),
        P(("space", "ray"), None),
        P(("space", "ray"), None, None),
        P(("space", "ray"), None),
        P(None, ("space", "ray")),
        P(),
        P("space", None, None),
        P("space", None),
        P("space", None, None),
        P("space", None),
        P("space", None, None),
        P("space", None),
    )
    return jax.shard_map(
        per_device,
        mesh=mesh,
        in_specs=placed,
        out_specs=(
            P("space", "ray", None),
            P("space", "ray", None),
            P("space", None, None),
            P("space", None),
            P("space", None),
            P("space", None),
        ),
        check_vma=False,
    )
```

```python
import jax
import jax.numpy as jnp
from jax import lax
from jax.sharding import PartitionSpec as P
from jax.experimental import pallas as pl
from jax.experimental.pallas import tpu as pltpu

SEG_LEN = 32
SEGS = 8


two_pi = 6.283185307179586


def gate_of(value):
    return 0.5 * jnp.tanh(0.5 * value) + 0.5


def silu_slope(value):
    gate = gate_of(value)
    return gate * (1.0 + value * (1.0 - gate))


def turn_sin_cos(turns):
    quarter = jnp.floor(turns * 4.0 + 0.5)
    angle = (turns - quarter * 0.25) * two_pi
    square = angle * angle
    sine = angle * (
        1.0
        + square
        * (
            -1.0 / 6.0
            + square * (1.0 / 120.0 + square * (-1.0 / 5040.0 + square * (1.0 / 362880.0)))
        )
    )
    cosine = 1.0 + square * (
        -0.5
        + square
        * (
            1.0 / 24.0
            + square * (-1.0 / 720.0 + square * (1.0 / 40320.0 + square * (-1.0 / 3628800.0)))
        )
    )
    step = quarter - 4.0 * jnp.floor(quarter * 0.25)
    flip = step >= 2.0
    odd = (step == 1.0) | (step == 3.0)
    sin_out = jnp.where(odd, cosine, sine)
    cos_out = jnp.where(odd, sine, cosine)
    sin_out = jnp.where(flip, -sin_out, sin_out)
    cos_out = jnp.where(flip != odd, -cos_out, cos_out)
    return sin_out, cos_out


def encode(samples, fourier):
    turns = (
        samples[:, 0, :, None] * fourier[0]
        + samples[:, 1, :, None] * fourier[1]
        + samples[:, 2, :, None] * fourier[2]
    )
    sine, cosine = turn_sin_cos(turns)
    joined = jnp.concatenate([sine, cosine], axis=-1)
    return joined.astype(jnp.bfloat16).reshape(-1, joined.shape[-1])


def forward_kernel(
    place_ref, fourier_ref, w1_ref, b1_ref, w2_ref, b2_ref, wh_ref, bh_ref,
    enc_ref, a1_ref, a2_ref, s1_ref, s2_ref, head_ref,
):
    place = place_ref[...]
    fourier = fourier_ref[...]
    turns = (
        fourier[:, 0:1] * place[0:1, :]
        + fourier[:, 1:2] * place[1:2, :]
        + fourier[:, 2:3] * place[2:3, :]
    )
    sine, cosine = turn_sin_cos(turns)
    encoded = jnp.concatenate([sine, cosine], axis=0).astype(jnp.bfloat16)
    enc_ref[...] = encoded
    pre_first = (
        lax.dot_general(
            encoded, w1_ref[...], (((0,), (0,)), ((), ())), preferred_element_type=jnp.float32
        )
        + b1_ref[...]
    )
    gate_first = gate_of(pre_first)
    act_first = (pre_first * gate_first).astype(jnp.bfloat16)
    a1_ref[...] = act_first
    s1_ref[...] = gate_first * (1.0 + pre_first * (1.0 - gate_first))
    pre_second = jnp.dot(act_first, w2_ref[...], preferred_element_type=jnp.float32) + b2_ref[...]
    gate_second = gate_of(pre_second)
    act_second = (pre_second * gate_second).astype(jnp.bfloat16)
    a2_ref[...] = act_second
    s2_ref[...] = gate_second * (1.0 + pre_second * (1.0 - gate_second))
    head_ref[...] = (
        lax.dot_general(
            wh_ref[...], act_second, (((1,), (1,)), ((), ())), preferred_element_type=jnp.float32
        )
        + bh_ref[...]
    )


def backward_kernel(
    enc_ref, a1_ref, a2_ref, s1_ref, s2_ref, raw_ref, w2_ref, wh_ref,
    g1_ref, gb1_ref, g2_ref, gb2_ref, gh_ref,
):
    @pl.when(pl.program_id(0) == 0)
    def _():
        g1_ref[...] = jnp.zeros_like(g1_ref)
        gb1_ref[...] = jnp.zeros_like(gb1_ref)
        g2_ref[...] = jnp.zeros_like(g2_ref)
        gb2_ref[...] = jnp.zeros_like(gb2_ref)
        gh_ref[...] = jnp.zeros_like(gh_ref)

    raw = raw_ref[...]
    back_second = jnp.dot(raw, wh_ref[...], preferred_element_type=jnp.float32)
    delta_second = (back_second * s2_ref[...]).astype(jnp.bfloat16)
    g2_ref[...] += lax.dot_general(
        a1_ref[...], delta_second, (((0,), (0,)), ((), ())), preferred_element_type=jnp.float32
    )
    gb2_ref[...] += jnp.sum(delta_second.astype(jnp.float32), axis=0, keepdims=True)
    back_first = lax.dot_general(
        delta_second, w2_ref[...], (((1,), (1,)), ((), ())), preferred_element_type=jnp.float32
    )
    delta_first = (back_first * s1_ref[...]).astype(jnp.bfloat16)
    g1_ref[...] += jnp.dot(enc_ref[...], delta_first, preferred_element_type=jnp.float32)
    gb1_ref[...] += jnp.sum(delta_first.astype(jnp.float32), axis=0, keepdims=True)
    gh_ref[...] += lax.dot_general(
        raw, a2_ref[...], (((0,), (0,)), ((), ())), preferred_element_type=jnp.float32
    )


BLOCK = 1024


def forward_layers(samples, fourier, params):
    first_weight, first_bias, second_weight, second_bias, head_weight, head_bias = params
    rows = samples.shape[0] * samples.shape[2]
    place = jnp.transpose(samples, (1, 0, 2)).reshape(4, rows)
    features, hidden = first_weight.shape
    heads = head_weight.shape[0]
    whole = lambda i: (0, 0)
    by_row = lambda i: (i, 0)
    by_column = lambda i: (0, i)
    return pl.pallas_call(
        forward_kernel,
        grid=(rows // BLOCK,),
        in_specs=[
            pl.BlockSpec((4, BLOCK), by_column),
            pl.BlockSpec((fourier.shape[1], fourier.shape[0]), whole),
            pl.BlockSpec(first_weight.shape, whole),
            pl.BlockSpec((1, hidden), whole),
            pl.BlockSpec(second_weight.shape, whole),
            pl.BlockSpec((1, hidden), whole),
            pl.BlockSpec(head_weight.shape, whole),
            pl.BlockSpec((heads, 1), whole),
        ],
        out_specs=[
            pl.BlockSpec((features, BLOCK), by_column),
            pl.BlockSpec((BLOCK, hidden), by_row),
            pl.BlockSpec((BLOCK, hidden), by_row),
            pl.BlockSpec((BLOCK, hidden), by_row),
            pl.BlockSpec((BLOCK, hidden), by_row),
            pl.BlockSpec((heads, BLOCK), by_column),
        ],
        out_shape=[
            jax.ShapeDtypeStruct((features, rows), jnp.bfloat16),
            jax.ShapeDtypeStruct((rows, hidden), jnp.bfloat16),
            jax.ShapeDtypeStruct((rows, hidden), jnp.bfloat16),
            jax.ShapeDtypeStruct((rows, hidden), jnp.float32),
            jax.ShapeDtypeStruct((rows, hidden), jnp.float32),
            jax.ShapeDtypeStruct((heads, rows), jnp.float32),
        ],
        compiler_params=pltpu.CompilerParams(dimension_semantics=("arbitrary",)),
    )(
        place,
        fourier.T,
        first_weight,
        first_bias.reshape(1, hidden),
        second_weight,
        second_bias.reshape(1, hidden),
        head_weight,
        head_bias.reshape(heads, 1),
    )


def network(samples, fourier, params):
    seg_count, length = (samples.shape[0], samples.shape[2])
    encoded, act_first, act_second, slope_first, slope_second, head_raw = forward_layers(
        samples, fourier, params
    )
    head_raw = head_raw.reshape(4, seg_count, length)
    density = jax.nn.softplus(head_raw[0])
    colour = jax.nn.sigmoid(head_raw[1:])
    optical = density * samples[:, 3, :]
    inclusive = jnp.cumsum(optical, axis=1)
    enter_light = jnp.exp(optical - inclusive)
    leave_light = jnp.exp(-inclusive)
    weight = enter_light - leave_light
    seg_colour = jnp.sum(weight[None] * colour, axis=2)
    seg_log = -inclusive[:, -1]
    saved = (
        encoded, act_first, act_second, slope_first, slope_second,
        head_raw, colour, weight, leave_light,
    )
    return (seg_colour, seg_log, saved)


def backward(samples, fourier, params, saved, up_colour, up_log):
    first_weight, first_bias, second_weight, second_bias, head_weight, head_bias = params
    encoded, act_first, act_second, slope_first, slope_second = saved[:5]
    head_raw, colour, weight, leave_light = saved[5:]
    up_rows = up_colour.T[:, :, None]
    energy = jnp.sum(colour * up_rows, axis=0)
    spent = weight * energy
    remaining = jnp.sum(spent, axis=1, keepdims=True) - jnp.cumsum(spent, axis=1)
    grad_optical = leave_light * energy - remaining - up_log[:, None]
    grad_density = grad_optical * samples[:, 3, :] * jax.nn.sigmoid(head_raw[0])
    grad_tint = weight[None] * up_rows * colour * (1.0 - colour)
    grad_raw = (
        jnp.concatenate([grad_density[None], grad_tint], axis=0)
        .reshape(4, -1)
        .T.astype(jnp.bfloat16)
    )
    grad_head_bias = jnp.sum(grad_raw.astype(jnp.float32), axis=0)
    rows = grad_raw.shape[0]
    features, hidden = first_weight.shape
    whole = lambda i: (0, 0)
    by_row = lambda i: (i, 0)
    outs = pl.pallas_call(
        backward_kernel,
        grid=(rows // BLOCK,),
        in_specs=[
            pl.BlockSpec((features, BLOCK), lambda i: (0, i)),
            pl.BlockSpec((BLOCK, hidden), by_row),
            pl.BlockSpec((BLOCK, hidden), by_row),
            pl.BlockSpec((BLOCK, hidden), by_row),
            pl.BlockSpec((BLOCK, hidden), by_row),
            pl.BlockSpec((BLOCK, 4), by_row),
            pl.BlockSpec(second_weight.shape, whole),
            pl.BlockSpec(head_weight.shape, whole),
        ],
        out_specs=[
            pl.BlockSpec((features, hidden), whole),
            pl.BlockSpec((1, hidden), whole),
            pl.BlockSpec((hidden, hidden), whole),
            pl.BlockSpec((1, hidden), whole),
            pl.BlockSpec((4, hidden), whole),
        ],
        out_shape=[
            jax.ShapeDtypeStruct((features, hidden), jnp.float32),
            jax.ShapeDtypeStruct((1, hidden), jnp.float32),
            jax.ShapeDtypeStruct((hidden, hidden), jnp.float32),
            jax.ShapeDtypeStruct((1, hidden), jnp.float32),
            jax.ShapeDtypeStruct((4, hidden), jnp.float32),
        ],
        compiler_params=pltpu.CompilerParams(dimension_semantics=("arbitrary",)),
    )(
        encoded, act_first, act_second, slope_first, slope_second, grad_raw,
        second_weight, head_weight,
    )
    grad_first, bias_first, grad_second, bias_second, grad_head = outs
    return (grad_first, grad_second, grad_head, bias_first[0], bias_second[0], grad_head_bias)


def composite(seg_colour, seg_log, depth_rank, pixel_rows):
    before = (depth_rank[:, None, :] < depth_rank[:, :, None]).astype(jnp.float32)
    prefix = jnp.exp(jnp.sum(before * seg_log[:, None, :], axis=2))
    up_colour = prefix[..., None] * pixel_rows[:, None, :]
    shaded = prefix * jnp.sum(seg_colour * pixel_rows[:, None, :], axis=2)
    up_log = jnp.sum(before * shaded[:, :, None], axis=1)
    return (up_colour, up_log)


def per_device(
    positions,
    spacing,
    assign,
    depth_rank,
    pixel_grad,
    fourier,
    first_weight,
    first_bias,
    second_weight,
    second_bias,
    head_weight,
    head_bias,
):
    groups = lax.axis_size("space")
    ray_count = positions.shape[1]
    total = ray_count * SEGS
    capacity = 3 * total // (2 * groups)
    slot_count = capacity * groups
    owner = assign.reshape(total)
    member = (owner[:, None] == jnp.arange(groups, dtype=jnp.int32)[None, :]).astype(jnp.int32)
    earlier = jnp.cumsum(member, axis=0) - member
    within = jnp.sum(earlier * member, axis=1)
    target = owner * capacity + within
    dispatch = (target[:, None] == jnp.arange(slot_count, dtype=jnp.int32)[None, :]).astype(
        jnp.float32
    )
    seg_pos = jnp.transpose(positions.reshape(3, total, SEG_LEN), (1, 0, 2))
    seg_gap = spacing.reshape(total, 1, SEG_LEN)
    segments = jnp.concatenate([seg_pos, seg_gap], axis=1).reshape(total, 4 * SEG_LEN)
    outgoing = lax.dot_general(
        dispatch,
        segments,
        (((0,), (0,)), ((), ())),
        precision=lax.Precision.HIGHEST,
        preferred_element_type=jnp.float32,
    )
    outgoing = outgoing.reshape(groups, capacity, 4 * SEG_LEN)
    arrived = lax.all_to_all(outgoing, "space", split_axis=0, concat_axis=0, tiled=True)
    samples = arrived.reshape(slot_count, 4, SEG_LEN)
    params = tuple(
        (
            item[0]
            for item in (
                first_weight,
                first_bias,
                second_weight,
                second_bias,
                head_weight,
                head_bias,
            )
        )
    )
    seg_colour, seg_log, saved = network(samples, fourier, params)
    partials = jnp.concatenate([seg_colour, seg_log[None, :]], axis=0).reshape(
        4, groups, capacity
    )
    returned = lax.all_to_all(partials, "space", split_axis=1, concat_axis=1, tiled=True).reshape(
        4, slot_count
    )
    mine = lax.dot_general(
        dispatch,
        returned,
        (((1,), (1,)), ((), ())),
        precision=lax.Precision.HIGHEST,
        preferred_element_type=jnp.float32,
    )
    up_colour, up_log = composite(
        mine[:, :3].reshape(ray_count, SEGS, 3),
        mine[:, 3].reshape(ray_count, SEGS),
        depth_rank,
        pixel_grad.T,
    )
    upstream = jnp.concatenate([up_colour.reshape(total, 3), up_log.reshape(total, 1)], axis=1)
    sendback = lax.dot_general(
        upstream,
        dispatch,
        (((0,), (0,)), ((), ())),
        precision=lax.Precision.HIGHEST,
        preferred_element_type=jnp.float32,
    )
    sendback = sendback.reshape(4, groups, capacity)
    received = lax.all_to_all(sendback, "space", split_axis=1, concat_axis=1, tiled=True)
    received = received.reshape(4, slot_count).T
    totals = backward(samples, fourier, params, saved, received[:, :3], received[:, 3])
    grad_first, grad_second, grad_head, bias_first, bias_second, bias_head = totals
    replicas = lax.axis_size("ray")
    small = jnp.concatenate(
        [grad_head.reshape(-1), bias_first, bias_second, bias_head], axis=0
    )
    if replicas == 2:
        position = lax.axis_index("ray")
        got_first, got_second, got_small = lax.ppermute(
            (grad_first, grad_second, small), "ray", [(0, 1), (1, 0)]
        )
        rows_first = grad_first.shape[0] // 2
        rows_second = grad_second.shape[0] // 2
        part_first = lax.dynamic_slice_in_dim(
            grad_first + got_first, position * rows_first, rows_first, 0
        )
        part_second = lax.dynamic_slice_in_dim(
            grad_second + got_second, position * rows_second, rows_second, 0
        )
        small = small + got_small
    elif replicas & (replicas - 1) == 0:
        position = lax.axis_index("ray")
        part_first, part_second = grad_first, grad_second
        distance = replicas // 2
        while distance >= 1:
            pairs = [(i, i ^ distance) for i in range(replicas)]
            half = part_first.shape[0] // 2
            upper = (position // distance) % 2
            keep_first = lax.dynamic_slice_in_dim(part_first, upper * half, half, 0)
            send_first = lax.dynamic_slice_in_dim(part_first, (1 - upper) * half, half, 0)
            keep_second = lax.dynamic_slice_in_dim(part_second, upper * half, half, 0)
            send_second = lax.dynamic_slice_in_dim(part_second, (1 - upper) * half, half, 0)
            got_first, got_second, got_small = lax.ppermute(
                (send_first, send_second, small), "ray", pairs
            )
            part_first = keep_first + got_first
            part_second = keep_second + got_second
            small = small + got_small
            distance //= 2
    else:
        part_first = lax.psum_scatter(grad_first, "ray", scatter_dimension=0, tiled=True)
        part_second = lax.psum_scatter(grad_second, "ray", scatter_dimension=0, tiled=True)
        small = lax.psum(small, "ray")
    heads = grad_head.size
    hidden = bias_first.shape[0]
    small_sums = (
        small[:heads].reshape(grad_head.shape),
        small[heads : heads + hidden],
        small[heads + hidden : heads + 2 * hidden],
        small[heads + 2 * hidden :],
    )
    return (
        part_first[None],
        part_second[None],
        small_sums[0][None],
        small_sums[1][None],
        small_sums[2][None],
        small_sums[3][None],
    )


def solution(mesh):
    placed = (
        P(None, ("space", "ray"), None),
        P(("space", "ray"), None),
        P(("space", "ray"), None, None),
        P(("space", "ray"), None),
        P(None, ("space", "ray")),
        P(),
        P("space", None, None),
        P("space", None),
        P("space", None, None),
        P("space", None),
        P("space", None, None),
        P("space", None),
    )
    return jax.shard_map(
        per_device,
        mesh=mesh,
        in_specs=placed,
        out_specs=(
            P("space", "ray", None),
            P("space", "ray", None),
            P("space", None, None),
            P("space", None),
            P("space", None),
            P("space", None),
        ),
        check_vma=False,
    )
```

```python
import jax
import jax.numpy as jnp
from jax import lax
from jax.sharding import PartitionSpec as P
from jax.experimental import pallas as pl
from jax.experimental.pallas import tpu as pltpu

SEG_LEN = 32
SEGS = 8


two_pi = 6.283185307179586


def gate_of(value):
    return 0.5 * jnp.tanh(0.5 * value) + 0.5


def silu_slope(value):
    gate = gate_of(value)
    return gate * (1.0 + value * (1.0 - gate))


def turn_sin_cos(turns):
    quarter = jnp.floor(turns * 4.0 + 0.5)
    angle = (turns - quarter * 0.25) * two_pi
    square = angle * angle
    sine = angle * (
        1.0
        + square
        * (
            -1.0 / 6.0
            + square * (1.0 / 120.0 + square * (-1.0 / 5040.0 + square * (1.0 / 362880.0)))
        )
    )
    cosine = 1.0 + square * (
        -0.5
        + square
        * (
            1.0 / 24.0
            + square * (-1.0 / 720.0 + square * (1.0 / 40320.0 + square * (-1.0 / 3628800.0)))
        )
    )
    step = quarter - 4.0 * jnp.floor(quarter * 0.25)
    flip = step >= 2.0
    odd = (step == 1.0) | (step == 3.0)
    sin_out = jnp.where(odd, cosine, sine)
    cos_out = jnp.where(odd, sine, cosine)
    sin_out = jnp.where(flip, -sin_out, sin_out)
    cos_out = jnp.where(flip != odd, -cos_out, cos_out)
    return sin_out, cos_out


def encode(samples, fourier):
    turns = (
        samples[:, 0, :, None] * fourier[0]
        + samples[:, 1, :, None] * fourier[1]
        + samples[:, 2, :, None] * fourier[2]
    )
    sine, cosine = turn_sin_cos(turns)
    joined = jnp.concatenate([sine, cosine], axis=-1)
    return joined.astype(jnp.bfloat16).reshape(-1, joined.shape[-1])


def forward_kernel(
    place_ref, fourier_ref, w1_ref, b1_ref, w2_ref, b2_ref, wh_ref, bh_ref,
    enc_ref, a1_ref, a2_ref, s1_ref, s2_ref, head_ref,
):
    place = place_ref[...]
    fourier = fourier_ref[...]
    turns = (
        fourier[:, 0:1] * place[0:1, :]
        + fourier[:, 1:2] * place[1:2, :]
        + fourier[:, 2:3] * place[2:3, :]
    )
    sine, cosine = turn_sin_cos(turns)
    encoded = jnp.concatenate([sine, cosine], axis=0).astype(jnp.bfloat16)
    enc_ref[...] = encoded
    pre_first = jnp.dot(w1_ref[...], encoded, preferred_element_type=jnp.float32) + b1_ref[...]
    gate_first = gate_of(pre_first)
    act_first = (pre_first * gate_first).astype(jnp.bfloat16)
    a1_ref[...] = act_first
    s1_ref[...] = (gate_first * (1.0 + pre_first * (1.0 - gate_first))).astype(s1_ref.dtype)
    pre_second = jnp.dot(w2_ref[...], act_first, preferred_element_type=jnp.float32) + b2_ref[...]
    gate_second = gate_of(pre_second)
    act_second = (pre_second * gate_second).astype(jnp.bfloat16)
    a2_ref[...] = act_second
    s2_ref[...] = (gate_second * (1.0 + pre_second * (1.0 - gate_second))).astype(s2_ref.dtype)
    head_ref[...] = (
        jnp.dot(wh_ref[...], act_second, preferred_element_type=jnp.float32) + bh_ref[...]
    )


def backward_kernel(
    enc_ref, a1_ref, a2_ref, s1_ref, s2_ref, raw_ref, w2_ref, wh_ref,
    g1_ref, gb1_ref, g2_ref, gb2_ref, gh_ref,
):
    @pl.when(pl.program_id(0) == 0)
    def _():
        g1_ref[...] = jnp.zeros_like(g1_ref)
        gb1_ref[...] = jnp.zeros_like(gb1_ref)
        g2_ref[...] = jnp.zeros_like(g2_ref)
        gb2_ref[...] = jnp.zeros_like(gb2_ref)
        gh_ref[...] = jnp.zeros_like(gh_ref)

    across = (((1,), (1,)), ((), ()))
    raw = raw_ref[...]
    back_second = jnp.dot(wh_ref[...], raw, preferred_element_type=jnp.float32)
    delta_second = (back_second * s2_ref[...].astype(jnp.float32)).astype(jnp.bfloat16)
    g2_ref[...] += lax.dot_general(
        a1_ref[...], delta_second, across, preferred_element_type=jnp.float32
    )
    gb2_ref[...] += jnp.sum(delta_second.astype(jnp.float32), axis=1, keepdims=True)
    back_first = jnp.dot(w2_ref[...], delta_second, preferred_element_type=jnp.float32)
    delta_first = (back_first * s1_ref[...].astype(jnp.float32)).astype(jnp.bfloat16)
    g1_ref[...] += lax.dot_general(
        enc_ref[...], delta_first, across, preferred_element_type=jnp.float32
    )
    gb1_ref[...] += jnp.sum(delta_first.astype(jnp.float32), axis=1, keepdims=True)
    gh_ref[...] += lax.dot_general(raw, a2_ref[...], across, preferred_element_type=jnp.float32)


SLOPE_TYPE = jnp.float32
BLOCK = 1024


def forward_layers(samples, fourier, params):
    first_weight, first_bias, second_weight, second_bias, head_weight, head_bias = params
    rows = samples.shape[0] * samples.shape[2]
    place = jnp.transpose(samples, (1, 0, 2)).reshape(4, rows)
    features, hidden = first_weight.shape
    heads = head_weight.shape[0]
    whole = lambda i: (0, 0)
    by_column = lambda i: (0, i)
    return pl.pallas_call(
        forward_kernel,
        grid=(rows // BLOCK,),
        in_specs=[
            pl.BlockSpec((4, BLOCK), by_column),
            pl.BlockSpec((fourier.shape[1], fourier.shape[0]), whole),
            pl.BlockSpec((hidden, features), whole),
            pl.BlockSpec((hidden, 1), whole),
            pl.BlockSpec((hidden, hidden), whole),
            pl.BlockSpec((hidden, 1), whole),
            pl.BlockSpec(head_weight.shape, whole),
            pl.BlockSpec((heads, 1), whole),
        ],
        out_specs=[
            pl.BlockSpec((features, BLOCK), by_column),
            pl.BlockSpec((hidden, BLOCK), by_column),
            pl.BlockSpec((hidden, BLOCK), by_column),
            pl.BlockSpec((hidden, BLOCK), by_column),
            pl.BlockSpec((hidden, BLOCK), by_column),
            pl.BlockSpec((heads, BLOCK), by_column),
        ],
        out_shape=[
            jax.ShapeDtypeStruct((features, rows), jnp.bfloat16),
            jax.ShapeDtypeStruct((hidden, rows), jnp.bfloat16),
            jax.ShapeDtypeStruct((hidden, rows), jnp.bfloat16),
            jax.ShapeDtypeStruct((hidden, rows), SLOPE_TYPE),
            jax.ShapeDtypeStruct((hidden, rows), SLOPE_TYPE),
            jax.ShapeDtypeStruct((heads, rows), jnp.float32),
        ],
        compiler_params=pltpu.CompilerParams(dimension_semantics=("arbitrary",)),
    )(
        place,
        fourier.T,
        first_weight.T,
        first_bias.reshape(hidden, 1),
        second_weight.T,
        second_bias.reshape(hidden, 1),
        head_weight,
        head_bias.reshape(heads, 1),
    )


def network(samples, fourier, params):
    seg_count, length = (samples.shape[0], samples.shape[2])
    encoded, act_first, act_second, slope_first, slope_second, head_raw = forward_layers(
        samples, fourier, params
    )
    head_raw = head_raw.reshape(4, seg_count, length)
    density = jax.nn.softplus(head_raw[0])
    colour = jax.nn.sigmoid(head_raw[1:])
    optical = density * samples[:, 3, :]
    inclusive = jnp.cumsum(optical, axis=1)
    enter_light = jnp.exp(optical - inclusive)
    leave_light = jnp.exp(-inclusive)
    weight = enter_light - leave_light
    seg_colour = jnp.sum(weight[None] * colour, axis=2)
    seg_log = -inclusive[:, -1]
    saved = (
        encoded, act_first, act_second, slope_first, slope_second,
        head_raw, colour, weight, leave_light,
    )
    return (seg_colour, seg_log, saved)


def backward(samples, fourier, params, saved, up_colour, up_log):
    first_weight, first_bias, second_weight, second_bias, head_weight, head_bias = params
    encoded, act_first, act_second, slope_first, slope_second = saved[:5]
    head_raw, colour, weight, leave_light = saved[5:]
    up_rows = up_colour.T[:, :, None]
    energy = jnp.sum(colour * up_rows, axis=0)
    spent = weight * energy
    remaining = jnp.sum(spent, axis=1, keepdims=True) - jnp.cumsum(spent, axis=1)
    grad_optical = leave_light * energy - remaining - up_log[:, None]
    grad_density = grad_optical * samples[:, 3, :] * jax.nn.sigmoid(head_raw[0])
    grad_tint = weight[None] * up_rows * colour * (1.0 - colour)
    grad_raw = (
        jnp.concatenate([grad_density[None], grad_tint], axis=0)
        .reshape(4, -1)
        .astype(jnp.bfloat16)
    )
    grad_head_bias = jnp.sum(grad_raw.astype(jnp.float32), axis=1)
    rows = grad_raw.shape[1]
    features, hidden = first_weight.shape
    whole = lambda i: (0, 0)
    by_column = lambda i: (0, i)
    outs = pl.pallas_call(
        backward_kernel,
        grid=(rows // BLOCK,),
        in_specs=[
            pl.BlockSpec((features, BLOCK), by_column),
            pl.BlockSpec((hidden, BLOCK), by_column),
            pl.BlockSpec((hidden, BLOCK), by_column),
            pl.BlockSpec((hidden, BLOCK), by_column),
            pl.BlockSpec((hidden, BLOCK), by_column),
            pl.BlockSpec((4, BLOCK), by_column),
            pl.BlockSpec(second_weight.shape, whole),
            pl.BlockSpec((hidden, 4), whole),
        ],
        out_specs=[
            pl.BlockSpec((features, hidden), whole),
            pl.BlockSpec((hidden, 1), whole),
            pl.BlockSpec((hidden, hidden), whole),
            pl.BlockSpec((hidden, 1), whole),
            pl.BlockSpec((4, hidden), whole),
        ],
        out_shape=[
            jax.ShapeDtypeStruct((features, hidden), jnp.float32),
            jax.ShapeDtypeStruct((hidden, 1), jnp.float32),
            jax.ShapeDtypeStruct((hidden, hidden), jnp.float32),
            jax.ShapeDtypeStruct((hidden, 1), jnp.float32),
            jax.ShapeDtypeStruct((4, hidden), jnp.float32),
        ],
        compiler_params=pltpu.CompilerParams(dimension_semantics=("arbitrary",)),
    )(
        encoded, act_first, act_second, slope_first, slope_second, grad_raw,
        second_weight, head_weight.T,
    )
    grad_first, bias_first, grad_second, bias_second, grad_head = outs
    return (grad_first, grad_second, grad_head, bias_first[:, 0], bias_second[:, 0], grad_head_bias)


def composite(seg_colour, seg_log, depth_rank, pixel_rows):
    before = (depth_rank[:, None, :] < depth_rank[:, :, None]).astype(jnp.float32)
    prefix = jnp.exp(jnp.sum(before * seg_log[:, None, :], axis=2))
    up_colour = prefix[..., None] * pixel_rows[:, None, :]
    shaded = prefix * jnp.sum(seg_colour * pixel_rows[:, None, :], axis=2)
    up_log = jnp.sum(before * shaded[:, :, None], axis=1)
    return (up_colour, up_log)


def per_device(
    positions,
    spacing,
    assign,
    depth_rank,
    pixel_grad,
    fourier,
    first_weight,
    first_bias,
    second_weight,
    second_bias,
    head_weight,
    head_bias,
):
    groups = lax.axis_size("space")
    ray_count = positions.shape[1]
    total = ray_count * SEGS
    capacity = 3 * total // (2 * groups)
    slot_count = capacity * groups
    owner = assign.reshape(total)
    member = (owner[:, None] == jnp.arange(groups, dtype=jnp.int32)[None, :]).astype(jnp.int32)
    earlier = jnp.cumsum(member, axis=0) - member
    within = jnp.sum(earlier * member, axis=1)
    target = owner * capacity + within
    dispatch = (target[:, None] == jnp.arange(slot_count, dtype=jnp.int32)[None, :]).astype(
        jnp.float32
    )
    seg_pos = jnp.transpose(positions.reshape(3, total, SEG_LEN), (1, 0, 2))
    seg_gap = spacing.reshape(total, 1, SEG_LEN)
    segments = jnp.concatenate([seg_pos, seg_gap], axis=1).reshape(total, 4 * SEG_LEN)
    outgoing = lax.dot_general(
        dispatch,
        segments,
        (((0,), (0,)), ((), ())),
        precision=lax.Precision.HIGHEST,
        preferred_element_type=jnp.float32,
    )
    outgoing = outgoing.reshape(groups, capacity, 4 * SEG_LEN)
    arrived = lax.all_to_all(outgoing, "space", split_axis=0, concat_axis=0, tiled=True)
    samples = arrived.reshape(slot_count, 4, SEG_LEN)
    params = tuple(
        (
            item[0]
            for item in (
                first_weight,
                first_bias,
                second_weight,
                second_bias,
                head_weight,
                head_bias,
            )
        )
    )
    seg_colour, seg_log, saved = network(samples, fourier, params)
    partials = jnp.concatenate([seg_colour, seg_log[None, :]], axis=0).reshape(
        4, groups, capacity
    )
    returned = lax.all_to_all(partials, "space", split_axis=1, concat_axis=1, tiled=True).reshape(
        4, slot_count
    )
    mine = lax.dot_general(
        dispatch,
        returned,
        (((1,), (1,)), ((), ())),
        precision=lax.Precision.HIGHEST,
        preferred_element_type=jnp.float32,
    )
    up_colour, up_log = composite(
        mine[:, :3].reshape(ray_count, SEGS, 3),
        mine[:, 3].reshape(ray_count, SEGS),
        depth_rank,
        pixel_grad.T,
    )
    upstream = jnp.concatenate([up_colour.reshape(total, 3), up_log.reshape(total, 1)], axis=1)
    sendback = lax.dot_general(
        upstream,
        dispatch,
        (((0,), (0,)), ((), ())),
        precision=lax.Precision.HIGHEST,
        preferred_element_type=jnp.float32,
    )
    sendback = sendback.reshape(4, groups, capacity)
    received = lax.all_to_all(sendback, "space", split_axis=1, concat_axis=1, tiled=True)
    received = received.reshape(4, slot_count).T
    totals = backward(samples, fourier, params, saved, received[:, :3], received[:, 3])
    grad_first, grad_second, grad_head, bias_first, bias_second, bias_head = totals
    replicas = lax.axis_size("ray")
    small = jnp.concatenate(
        [grad_head.reshape(-1), bias_first, bias_second, bias_head], axis=0
    )
    if replicas == 2:
        position = lax.axis_index("ray")
        got_first, got_second, got_small = lax.ppermute(
            (grad_first, grad_second, small), "ray", [(0, 1), (1, 0)]
        )
        rows_first = grad_first.shape[0] // 2
        rows_second = grad_second.shape[0] // 2
        part_first = lax.dynamic_slice_in_dim(
            grad_first + got_first, position * rows_first, rows_first, 0
        )
        part_second = lax.dynamic_slice_in_dim(
            grad_second + got_second, position * rows_second, rows_second, 0
        )
        small = small + got_small
    elif replicas & (replicas - 1) == 0:
        position = lax.axis_index("ray")
        part_first, part_second = grad_first, grad_second
        distance = replicas // 2
        while distance >= 1:
            pairs = [(i, i ^ distance) for i in range(replicas)]
            half = part_first.shape[0] // 2
            upper = (position // distance) % 2
            keep_first = lax.dynamic_slice_in_dim(part_first, upper * half, half, 0)
            send_first = lax.dynamic_slice_in_dim(part_first, (1 - upper) * half, half, 0)
            keep_second = lax.dynamic_slice_in_dim(part_second, upper * half, half, 0)
            send_second = lax.dynamic_slice_in_dim(part_second, (1 - upper) * half, half, 0)
            got_first, got_second, got_small = lax.ppermute(
                (send_first, send_second, small), "ray", pairs
            )
            part_first = keep_first + got_first
            part_second = keep_second + got_second
            small = small + got_small
            distance //= 2
    else:
        part_first = lax.psum_scatter(grad_first, "ray", scatter_dimension=0, tiled=True)
        part_second = lax.psum_scatter(grad_second, "ray", scatter_dimension=0, tiled=True)
        small = lax.psum(small, "ray")
    heads = grad_head.size
    hidden = bias_first.shape[0]
    small_sums = (
        small[:heads].reshape(grad_head.shape),
        small[heads : heads + hidden],
        small[heads + hidden : heads + 2 * hidden],
        small[heads + 2 * hidden :],
    )
    return (
        part_first[None],
        part_second[None],
        small_sums[0][None],
        small_sums[1][None],
        small_sums[2][None],
        small_sums[3][None],
    )


def solution(mesh):
    placed = (
        P(None, ("space", "ray"), None),
        P(("space", "ray"), None),
        P(("space", "ray"), None, None),
        P(("space", "ray"), None),
        P(None, ("space", "ray")),
        P(),
        P("space", None, None),
        P("space", None),
        P("space", None, None),
        P("space", None),
        P("space", None, None),
        P("space", None),
    )
    return jax.shard_map(
        per_device,
        mesh=mesh,
        in_specs=placed,
        out_specs=(
            P("space", "ray", None),
            P("space", "ray", None),
            P("space", None, None),
            P("space", None),
            P("space", None),
            P("space", None),
        ),
        check_vma=False,
    )
```

```python
import jax
import jax.numpy as jnp
from jax import lax
from jax.sharding import PartitionSpec as P
from jax.experimental import pallas as pl
from jax.experimental.pallas import tpu as pltpu

SEG_LEN = 32
SEGS = 8


two_pi = 6.283185307179586


def gate_of(value):
    return 0.5 * jnp.tanh(0.5 * value) + 0.5


def silu_slope(value):
    gate = gate_of(value)
    return gate * (1.0 + value * (1.0 - gate))


def turn_sin_cos(turns):
    quarter = jnp.floor(turns * 4.0 + 0.5)
    angle = (turns - quarter * 0.25) * two_pi
    square = angle * angle
    sine = angle * (
        1.0
        + square
        * (
            -1.0 / 6.0
            + square * (1.0 / 120.0 + square * (-1.0 / 5040.0 + square * (1.0 / 362880.0)))
        )
    )
    cosine = 1.0 + square * (
        -0.5
        + square
        * (
            1.0 / 24.0
            + square * (-1.0 / 720.0 + square * (1.0 / 40320.0 + square * (-1.0 / 3628800.0)))
        )
    )
    step = quarter - 4.0 * jnp.floor(quarter * 0.25)
    flip = step >= 2.0
    odd = (step == 1.0) | (step == 3.0)
    sin_out = jnp.where(odd, cosine, sine)
    cos_out = jnp.where(odd, sine, cosine)
    sin_out = jnp.where(flip, -sin_out, sin_out)
    cos_out = jnp.where(flip != odd, -cos_out, cos_out)
    return sin_out, cos_out


def encode(samples, fourier):
    turns = (
        samples[:, 0, :, None] * fourier[0]
        + samples[:, 1, :, None] * fourier[1]
        + samples[:, 2, :, None] * fourier[2]
    )
    sine, cosine = turn_sin_cos(turns)
    joined = jnp.concatenate([sine, cosine], axis=-1)
    return joined.astype(jnp.bfloat16).reshape(-1, joined.shape[-1])


def forward_kernel(
    place_ref, fourier_ref, w1_ref, b1_ref, w2_ref, b2_ref, wh_ref, bh_ref,
    enc_ref, a1_ref, a2_ref, s1_ref, s2_ref, head_ref,
):
    place = place_ref[...]
    fourier = fourier_ref[...]
    turns = (
        fourier[:, 0:1] * place[0:1, :]
        + fourier[:, 1:2] * place[1:2, :]
        + fourier[:, 2:3] * place[2:3, :]
    )
    sine, cosine = turn_sin_cos(turns)
    encoded = jnp.concatenate([sine, cosine], axis=0).astype(jnp.bfloat16)
    enc_ref[...] = encoded
    pre_first = (
        lax.dot_general(
            encoded, w1_ref[...], (((0,), (0,)), ((), ())), preferred_element_type=jnp.float32
        )
        + b1_ref[...]
    )
    gate_first = gate_of(pre_first)
    act_first = (pre_first * gate_first).astype(jnp.bfloat16)
    a1_ref[...] = act_first
    s1_ref[...] = gate_first * (1.0 + pre_first * (1.0 - gate_first))
    pre_second = jnp.dot(act_first, w2_ref[...], preferred_element_type=jnp.float32) + b2_ref[...]
    gate_second = gate_of(pre_second)
    act_second = (pre_second * gate_second).astype(jnp.bfloat16)
    a2_ref[...] = act_second
    s2_ref[...] = gate_second * (1.0 + pre_second * (1.0 - gate_second))
    head_ref[...] = (
        lax.dot_general(
            wh_ref[...], act_second, (((1,), (1,)), ((), ())), preferred_element_type=jnp.float32
        )
        + bh_ref[...]
    )


def backward_kernel(
    enc_ref, a1_ref, a2_ref, s1_ref, s2_ref, raw_ref, w2_ref, wh_ref,
    g1_ref, gb1_ref, g2_ref, gb2_ref, gh_ref,
):
    @pl.when(pl.program_id(0) == 0)
    def _():
        g1_ref[...] = jnp.zeros_like(g1_ref)
        gb1_ref[...] = jnp.zeros_like(gb1_ref)
        g2_ref[...] = jnp.zeros_like(g2_ref)
        gb2_ref[...] = jnp.zeros_like(gb2_ref)
        gh_ref[...] = jnp.zeros_like(gh_ref)

    raw = raw_ref[...]
    back_second = jnp.dot(raw, wh_ref[...], preferred_element_type=jnp.float32)
    delta_second = (back_second * s2_ref[...]).astype(jnp.bfloat16)
    g2_ref[...] += lax.dot_general(
        a1_ref[...], delta_second, (((0,), (0,)), ((), ())), preferred_element_type=jnp.float32
    )
    gb2_ref[...] += jnp.sum(delta_second.astype(jnp.float32), axis=0, keepdims=True)
    back_first = lax.dot_general(
        delta_second, w2_ref[...], (((1,), (1,)), ((), ())), preferred_element_type=jnp.float32
    )
    delta_first = (back_first * s1_ref[...]).astype(jnp.bfloat16)
    g1_ref[...] += jnp.dot(enc_ref[...], delta_first, preferred_element_type=jnp.float32)
    gb1_ref[...] += jnp.sum(delta_first.astype(jnp.float32), axis=0, keepdims=True)
    gh_ref[...] += lax.dot_general(
        raw, a2_ref[...], (((0,), (0,)), ((), ())), preferred_element_type=jnp.float32
    )


BLOCK = 1024


def forward_layers(samples, fourier, params):
    first_weight, first_bias, second_weight, second_bias, head_weight, head_bias = params
    rows = samples.shape[0] * samples.shape[2]
    place = jnp.transpose(samples, (1, 0, 2)).reshape(4, rows)
    features, hidden = first_weight.shape
    heads = head_weight.shape[0]
    whole = lambda i: (0, 0)
    by_row = lambda i: (i, 0)
    by_column = lambda i: (0, i)
    return pl.pallas_call(
        forward_kernel,
        grid=(rows // BLOCK,),
        in_specs=[
            pl.BlockSpec((4, BLOCK), by_column),
            pl.BlockSpec((fourier.shape[1], fourier.shape[0]), whole),
            pl.BlockSpec(first_weight.shape, whole),
            pl.BlockSpec((1, hidden), whole),
            pl.BlockSpec(second_weight.shape, whole),
            pl.BlockSpec((1, hidden), whole),
            pl.BlockSpec(head_weight.shape, whole),
            pl.BlockSpec((heads, 1), whole),
        ],
        out_specs=[
            pl.BlockSpec((features, BLOCK), by_column),
            pl.BlockSpec((BLOCK, hidden), by_row),
            pl.BlockSpec((BLOCK, hidden), by_row),
            pl.BlockSpec((BLOCK, hidden), by_row),
            pl.BlockSpec((BLOCK, hidden), by_row),
            pl.BlockSpec((heads, BLOCK), by_column),
        ],
        out_shape=[
            jax.ShapeDtypeStruct((features, rows), jnp.bfloat16),
            jax.ShapeDtypeStruct((rows, hidden), jnp.bfloat16),
            jax.ShapeDtypeStruct((rows, hidden), jnp.bfloat16),
            jax.ShapeDtypeStruct((rows, hidden), jnp.float32),
            jax.ShapeDtypeStruct((rows, hidden), jnp.float32),
            jax.ShapeDtypeStruct((heads, rows), jnp.float32),
        ],
        compiler_params=pltpu.CompilerParams(dimension_semantics=("arbitrary",)),
    )(
        place,
        fourier.T,
        first_weight,
        first_bias.reshape(1, hidden),
        second_weight,
        second_bias.reshape(1, hidden),
        head_weight,
        head_bias.reshape(heads, 1),
    )


def network(samples, fourier, params):
    seg_count, length = (samples.shape[0], samples.shape[2])
    encoded, act_first, act_second, slope_first, slope_second, head_raw = forward_layers(
        samples, fourier, params
    )
    head_raw = head_raw.reshape(4, seg_count, length)
    density = jax.nn.softplus(head_raw[0])
    colour = jax.nn.sigmoid(head_raw[1:])
    optical = density * samples[:, 3, :]
    inclusive = jnp.cumsum(optical, axis=1)
    enter_light = jnp.exp(optical - inclusive)
    leave_light = jnp.exp(-inclusive)
    weight = enter_light - leave_light
    seg_colour = jnp.sum(weight[None] * colour, axis=2)
    seg_log = -inclusive[:, -1]
    saved = (
        encoded, act_first, act_second, slope_first, slope_second,
        head_raw, colour, weight, leave_light,
    )
    return (seg_colour, seg_log, saved)


def backward(samples, fourier, params, saved, up_colour, up_log):
    first_weight, first_bias, second_weight, second_bias, head_weight, head_bias = params
    encoded, act_first, act_second, slope_first, slope_second = saved[:5]
    head_raw, colour, weight, leave_light = saved[5:]
    up_rows = up_colour.T[:, :, None]
    energy = jnp.sum(colour * up_rows, axis=0)
    spent = weight * energy
    remaining = jnp.sum(spent, axis=1, keepdims=True) - jnp.cumsum(spent, axis=1)
    grad_optical = leave_light * energy - remaining - up_log[:, None]
    grad_density = grad_optical * samples[:, 3, :] * jax.nn.sigmoid(head_raw[0])
    grad_tint = weight[None] * up_rows * colour * (1.0 - colour)
    grad_raw = (
        jnp.concatenate([grad_density[None], grad_tint], axis=0)
        .reshape(4, -1)
        .T.astype(jnp.bfloat16)
    )
    grad_head_bias = jnp.sum(grad_raw.astype(jnp.float32), axis=0)
    rows = grad_raw.shape[0]
    features, hidden = first_weight.shape
    whole = lambda i: (0, 0)
    by_row = lambda i: (i, 0)
    outs = pl.pallas_call(
        backward_kernel,
        grid=(rows // BLOCK,),
        in_specs=[
            pl.BlockSpec((features, BLOCK), lambda i: (0, i)),
            pl.BlockSpec((BLOCK, hidden), by_row),
            pl.BlockSpec((BLOCK, hidden), by_row),
            pl.BlockSpec((BLOCK, hidden), by_row),
            pl.BlockSpec((BLOCK, hidden), by_row),
            pl.BlockSpec((BLOCK, 4), by_row),
            pl.BlockSpec(second_weight.shape, whole),
            pl.BlockSpec(head_weight.shape, whole),
        ],
        out_specs=[
            pl.BlockSpec((features, hidden), whole),
            pl.BlockSpec((1, hidden), whole),
            pl.BlockSpec((hidden, hidden), whole),
            pl.BlockSpec((1, hidden), whole),
            pl.BlockSpec((4, hidden), whole),
        ],
        out_shape=[
            jax.ShapeDtypeStruct((features, hidden), jnp.float32),
            jax.ShapeDtypeStruct((1, hidden), jnp.float32),
            jax.ShapeDtypeStruct((hidden, hidden), jnp.float32),
            jax.ShapeDtypeStruct((1, hidden), jnp.float32),
            jax.ShapeDtypeStruct((4, hidden), jnp.float32),
        ],
        compiler_params=pltpu.CompilerParams(dimension_semantics=("arbitrary",)),
    )(
        encoded, act_first, act_second, slope_first, slope_second, grad_raw,
        second_weight, head_weight,
    )
    grad_first, bias_first, grad_second, bias_second, grad_head = outs
    return (grad_first, grad_second, grad_head, bias_first[0], bias_second[0], grad_head_bias)


def composite(seg_colour, seg_log, depth_rank, pixel_rows):
    before = (depth_rank[:, None, :] < depth_rank[:, :, None]).astype(jnp.float32)
    prefix = jnp.exp(jnp.sum(before * seg_log[:, None, :], axis=2))
    up_colour = prefix[..., None] * pixel_rows[:, None, :]
    shaded = prefix * jnp.sum(seg_colour * pixel_rows[:, None, :], axis=2)
    up_log = jnp.sum(before * shaded[:, :, None], axis=1)
    return (up_colour, up_log)


def per_device(
    positions,
    spacing,
    assign,
    depth_rank,
    pixel_grad,
    fourier,
    first_weight,
    first_bias,
    second_weight,
    second_bias,
    head_weight,
    head_bias,
):
    groups = lax.axis_size("space")
    ray_count = positions.shape[1]
    total = ray_count * SEGS
    capacity = 3 * total // (2 * groups)
    slot_count = capacity * groups
    owner = assign.reshape(total)
    member = (owner[:, None] == jnp.arange(groups, dtype=jnp.int32)[None, :]).astype(jnp.int32)
    earlier = jnp.cumsum(member, axis=0) - member
    within = jnp.sum(earlier * member, axis=1)
    target = owner * capacity + within
    dispatch = (target[:, None] == jnp.arange(slot_count, dtype=jnp.int32)[None, :]).astype(
        jnp.float32
    )
    seg_pos = jnp.transpose(positions.reshape(3, total, SEG_LEN), (1, 0, 2))
    seg_gap = spacing.reshape(total, 1, SEG_LEN)
    segments = jnp.concatenate([seg_pos, seg_gap], axis=1).reshape(total, 4 * SEG_LEN)
    outgoing = lax.dot_general(
        dispatch,
        segments,
        (((0,), (0,)), ((), ())),
        precision=lax.Precision.HIGHEST,
        preferred_element_type=jnp.float32,
    )
    outgoing = outgoing.reshape(groups, capacity, 4 * SEG_LEN)
    arrived = lax.all_to_all(outgoing, "space", split_axis=0, concat_axis=0, tiled=True)
    samples = arrived.reshape(slot_count, 4, SEG_LEN)
    params = tuple(
        (
            item[0]
            for item in (
                first_weight,
                first_bias,
                second_weight,
                second_bias,
                head_weight,
                head_bias,
            )
        )
    )
    seg_colour, seg_log, saved = network(samples, fourier, params)
    partials = jnp.concatenate([seg_colour, seg_log[None, :]], axis=0).reshape(
        4, groups, capacity
    )
    returned = lax.all_to_all(partials, "space", split_axis=1, concat_axis=1, tiled=True).reshape(
        4, slot_count
    )
    mine = lax.dot_general(
        dispatch,
        returned,
        (((1,), (1,)), ((), ())),
        precision=lax.Precision.HIGHEST,
        preferred_element_type=jnp.float32,
    )
    up_colour, up_log = composite(
        mine[:, :3].reshape(ray_count, SEGS, 3),
        mine[:, 3].reshape(ray_count, SEGS),
        depth_rank,
        pixel_grad.T,
    )
    upstream = jnp.concatenate([up_colour.reshape(total, 3), up_log.reshape(total, 1)], axis=1)
    sendback = lax.dot_general(
        upstream,
        dispatch,
        (((0,), (0,)), ((), ())),
        precision=lax.Precision.HIGHEST,
        preferred_element_type=jnp.float32,
    )
    sendback = sendback.reshape(4, groups, capacity)
    received = lax.all_to_all(sendback, "space", split_axis=1, concat_axis=1, tiled=True)
    received = received.reshape(4, slot_count).T
    totals = backward(samples, fourier, params, saved, received[:, :3], received[:, 3])
    grad_first, grad_second, grad_head, bias_first, bias_second, bias_head = totals
    replicas = lax.axis_size("ray")
    hidden = bias_first.shape[0]
    heads = grad_head.shape[0]
    small = jnp.concatenate(
        [
            grad_head,
            bias_first[None],
            bias_second[None],
            jnp.pad(bias_head, (0, hidden - heads))[None],
        ],
        axis=0,
    )
    if replicas == 2:
        position = lax.axis_index("ray")
        got_first, got_second, got_small = lax.ppermute(
            (grad_first, grad_second, small), "ray", [(0, 1), (1, 0)]
        )
        rows_first = grad_first.shape[0] // 2
        rows_second = grad_second.shape[0] // 2
        part_first = lax.dynamic_slice_in_dim(
            grad_first + got_first, position * rows_first, rows_first, 0
        )
        part_second = lax.dynamic_slice_in_dim(
            grad_second + got_second, position * rows_second, rows_second, 0
        )
        small = small + got_small
    elif replicas & (replicas - 1) == 0:
        position = lax.axis_index("ray")
        part_first, part_second = grad_first, grad_second
        distance = replicas // 2
        while distance >= 1:
            pairs = [(i, i ^ distance) for i in range(replicas)]
            half = part_first.shape[0] // 2
            upper = (position // distance) % 2
            keep_first = lax.dynamic_slice_in_dim(part_first, upper * half, half, 0)
            send_first = lax.dynamic_slice_in_dim(part_first, (1 - upper) * half, half, 0)
            keep_second = lax.dynamic_slice_in_dim(part_second, upper * half, half, 0)
            send_second = lax.dynamic_slice_in_dim(part_second, (1 - upper) * half, half, 0)
            got_first, got_second, got_small = lax.ppermute(
                (send_first, send_second, small), "ray", pairs
            )
            part_first = keep_first + got_first
            part_second = keep_second + got_second
            small = small + got_small
            distance //= 2
    else:
        part_first = lax.psum_scatter(grad_first, "ray", scatter_dimension=0, tiled=True)
        part_second = lax.psum_scatter(grad_second, "ray", scatter_dimension=0, tiled=True)
        small = lax.psum(small, "ray")
    small_sums = (small[:heads], small[heads], small[heads + 1], small[heads + 2, :heads])
    return (
        part_first[None],
        part_second[None],
        small_sums[0][None],
        small_sums[1][None],
        small_sums[2][None],
        small_sums[3][None],
    )


def solution(mesh):
    placed = (
        P(None, ("space", "ray"), None),
        P(("space", "ray"), None),
        P(("space", "ray"), None, None),
        P(("space", "ray"), None),
        P(None, ("space", "ray")),
        P(),
        P("space", None, None),
        P("space", None),
        P("space", None, None),
        P("space", None),
        P("space", None, None),
        P("space", None),
    )
    return jax.shard_map(
        per_device,
        mesh=mesh,
        in_specs=placed,
        out_specs=(
            P("space", "ray", None),
            P("space", "ray", None),
            P("space", None, None),
            P("space", None),
            P("space", None),
            P("space", None),
        ),
        check_vma=False,
    )
```

```python
import jax
import jax.numpy as jnp
from jax import lax
from jax.sharding import PartitionSpec as P
from jax.experimental import pallas as pl
from jax.experimental.pallas import tpu as pltpu

SEG_LEN = 32
SEGS = 8


two_pi = 6.283185307179586


def gate_of(value):
    return 0.5 * jnp.tanh(0.5 * value) + 0.5


def silu_slope(value):
    gate = gate_of(value)
    return gate * (1.0 + value * (1.0 - gate))


def turn_sin_cos(turns):
    quarter = jnp.floor(turns * 4.0 + 0.5)
    angle = (turns - quarter * 0.25) * two_pi
    square = angle * angle
    sine = angle * (
        1.0
        + square
        * (
            -1.0 / 6.0
            + square * (1.0 / 120.0 + square * (-1.0 / 5040.0 + square * (1.0 / 362880.0)))
        )
    )
    cosine = 1.0 + square * (
        -0.5
        + square
        * (
            1.0 / 24.0
            + square * (-1.0 / 720.0 + square * (1.0 / 40320.0 + square * (-1.0 / 3628800.0)))
        )
    )
    step = quarter - 4.0 * jnp.floor(quarter * 0.25)
    flip = step >= 2.0
    odd = (step == 1.0) | (step == 3.0)
    sin_out = jnp.where(odd, cosine, sine)
    cos_out = jnp.where(odd, sine, cosine)
    sin_out = jnp.where(flip, -sin_out, sin_out)
    cos_out = jnp.where(flip != odd, -cos_out, cos_out)
    return sin_out, cos_out


def encode(samples, fourier):
    turns = (
        samples[:, 0, :, None] * fourier[0]
        + samples[:, 1, :, None] * fourier[1]
        + samples[:, 2, :, None] * fourier[2]
    )
    sine, cosine = turn_sin_cos(turns)
    joined = jnp.concatenate([sine, cosine], axis=-1)
    return joined.astype(jnp.bfloat16).reshape(-1, joined.shape[-1])


def forward_kernel(
    place_ref, fourier_ref, w1_ref, b1_ref, w2_ref, b2_ref, wh_ref, bh_ref,
    enc_ref, a1_ref, a2_ref, s1_ref, s2_ref, head_ref,
):
    place = place_ref[...]
    fourier = fourier_ref[...]
    turns = (
        fourier[:, 0:1] * place[0:1, :]
        + fourier[:, 1:2] * place[1:2, :]
        + fourier[:, 2:3] * place[2:3, :]
    )
    sine, cosine = turn_sin_cos(turns)
    encoded = jnp.concatenate([sine, cosine], axis=0).astype(jnp.bfloat16)
    enc_ref[...] = encoded
    pre_first = (
        lax.dot_general(
            encoded, w1_ref[...], (((0,), (0,)), ((), ())), preferred_element_type=jnp.float32
        )
        + b1_ref[...]
    )
    gate_first = gate_of(pre_first)
    act_first = (pre_first * gate_first).astype(jnp.bfloat16)
    a1_ref[...] = act_first
    s1_ref[...] = gate_first * (1.0 + pre_first * (1.0 - gate_first))
    pre_second = jnp.dot(act_first, w2_ref[...], preferred_element_type=jnp.float32) + b2_ref[...]
    gate_second = gate_of(pre_second)
    act_second = (pre_second * gate_second).astype(jnp.bfloat16)
    a2_ref[...] = act_second
    s2_ref[...] = gate_second * (1.0 + pre_second * (1.0 - gate_second))
    head_ref[...] = (
        lax.dot_general(
            wh_ref[...], act_second, (((1,), (1,)), ((), ())), preferred_element_type=jnp.float32
        )
        + bh_ref[...]
    )


def backward_kernel(
    enc_ref, a1_ref, a2_ref, s1_ref, s2_ref, raw_ref, w2_ref, wh_ref,
    g1_ref, gb1_ref, g2_ref, gb2_ref, gh_ref,
):
    @pl.when(pl.program_id(0) == 0)
    def _():
        g1_ref[...] = jnp.zeros_like(g1_ref)
        gb1_ref[...] = jnp.zeros_like(gb1_ref)
        g2_ref[...] = jnp.zeros_like(g2_ref)
        gb2_ref[...] = jnp.zeros_like(gb2_ref)
        gh_ref[...] = jnp.zeros_like(gh_ref)

    raw = raw_ref[...]
    back_second = jnp.dot(raw, wh_ref[...], preferred_element_type=jnp.float32)
    delta_second = (back_second * s2_ref[...]).astype(jnp.bfloat16)
    g2_ref[...] += lax.dot_general(
        a1_ref[...], delta_second, (((0,), (0,)), ((), ())), preferred_element_type=jnp.float32
    )
    gb2_ref[...] += jnp.sum(delta_second.astype(jnp.float32), axis=0, keepdims=True)
    back_first = lax.dot_general(
        delta_second, w2_ref[...], (((1,), (1,)), ((), ())), preferred_element_type=jnp.float32
    )
    delta_first = (back_first * s1_ref[...]).astype(jnp.bfloat16)
    g1_ref[...] += jnp.dot(enc_ref[...], delta_first, preferred_element_type=jnp.float32)
    gb1_ref[...] += jnp.sum(delta_first.astype(jnp.float32), axis=0, keepdims=True)
    gh_ref[...] += lax.dot_general(
        raw, a2_ref[...], (((0,), (0,)), ((), ())), preferred_element_type=jnp.float32
    )


BLOCK = 2048


def forward_layers(samples, fourier, params):
    first_weight, first_bias, second_weight, second_bias, head_weight, head_bias = params
    rows = samples.shape[0] * samples.shape[2]
    place = jnp.transpose(samples, (1, 0, 2)).reshape(4, rows)
    features, hidden = first_weight.shape
    heads = head_weight.shape[0]
    whole = lambda i: (0, 0)
    by_row = lambda i: (i, 0)
    by_column = lambda i: (0, i)
    return pl.pallas_call(
        forward_kernel,
        grid=(rows // BLOCK,),
        in_specs=[
            pl.BlockSpec((4, BLOCK), by_column),
            pl.BlockSpec((fourier.shape[1], fourier.shape[0]), whole),
            pl.BlockSpec(first_weight.shape, whole),
            pl.BlockSpec((1, hidden), whole),
            pl.BlockSpec(second_weight.shape, whole),
            pl.BlockSpec((1, hidden), whole),
            pl.BlockSpec(head_weight.shape, whole),
            pl.BlockSpec((heads, 1), whole),
        ],
        out_specs=[
            pl.BlockSpec((features, BLOCK), by_column),
            pl.BlockSpec((BLOCK, hidden), by_row),
            pl.BlockSpec((BLOCK, hidden), by_row),
            pl.BlockSpec((BLOCK, hidden), by_row),
            pl.BlockSpec((BLOCK, hidden), by_row),
            pl.BlockSpec((heads, BLOCK), by_column),
        ],
        out_shape=[
            jax.ShapeDtypeStruct((features, rows), jnp.bfloat16),
            jax.ShapeDtypeStruct((rows, hidden), jnp.bfloat16),
            jax.ShapeDtypeStruct((rows, hidden), jnp.bfloat16),
            jax.ShapeDtypeStruct((rows, hidden), jnp.float32),
            jax.ShapeDtypeStruct((rows, hidden), jnp.float32),
            jax.ShapeDtypeStruct((heads, rows), jnp.float32),
        ],
        compiler_params=pltpu.CompilerParams(dimension_semantics=("arbitrary",)),
    )(
        place,
        fourier.T,
        first_weight,
        first_bias.reshape(1, hidden),
        second_weight,
        second_bias.reshape(1, hidden),
        head_weight,
        head_bias.reshape(heads, 1),
    )


def network(samples, fourier, params):
    seg_count, length = (samples.shape[0], samples.shape[2])
    encoded, act_first, act_second, slope_first, slope_second, head_raw = forward_layers(
        samples, fourier, params
    )
    head_raw = head_raw.reshape(4, seg_count, length)
    density = jax.nn.softplus(head_raw[0])
    colour = jax.nn.sigmoid(head_raw[1:])
    optical = density * samples[:, 3, :]
    inclusive = jnp.cumsum(optical, axis=1)
    enter_light = jnp.exp(optical - inclusive)
    leave_light = jnp.exp(-inclusive)
    weight = enter_light - leave_light
    seg_colour = jnp.sum(weight[None] * colour, axis=2)
    seg_log = -inclusive[:, -1]
    saved = (
        encoded, act_first, act_second, slope_first, slope_second,
        head_raw, colour, weight, leave_light,
    )
    return (seg_colour, seg_log, saved)


def backward(samples, fourier, params, saved, up_colour, up_log):
    first_weight, first_bias, second_weight, second_bias, head_weight, head_bias = params
    encoded, act_first, act_second, slope_first, slope_second = saved[:5]
    head_raw, colour, weight, leave_light = saved[5:]
    up_rows = up_colour.T[:, :, None]
    energy = jnp.sum(colour * up_rows, axis=0)
    spent = weight * energy
    remaining = jnp.sum(spent, axis=1, keepdims=True) - jnp.cumsum(spent, axis=1)
    grad_optical = leave_light * energy - remaining - up_log[:, None]
    grad_density = grad_optical * samples[:, 3, :] * jax.nn.sigmoid(head_raw[0])
    grad_tint = weight[None] * up_rows * colour * (1.0 - colour)
    grad_raw = (
        jnp.concatenate([grad_density[None], grad_tint], axis=0)
        .reshape(4, -1)
        .T.astype(jnp.bfloat16)
    )
    grad_head_bias = jnp.sum(grad_raw.astype(jnp.float32), axis=0)
    rows = grad_raw.shape[0]
    features, hidden = first_weight.shape
    whole = lambda i: (0, 0)
    by_row = lambda i: (i, 0)
    outs = pl.pallas_call(
        backward_kernel,
        grid=(rows // BLOCK,),
        in_specs=[
            pl.BlockSpec((features, BLOCK), lambda i: (0, i)),
            pl.BlockSpec((BLOCK, hidden), by_row),
            pl.BlockSpec((BLOCK, hidden), by_row),
            pl.BlockSpec((BLOCK, hidden), by_row),
            pl.BlockSpec((BLOCK, hidden), by_row),
            pl.BlockSpec((BLOCK, 4), by_row),
            pl.BlockSpec(second_weight.shape, whole),
            pl.BlockSpec(head_weight.shape, whole),
        ],
        out_specs=[
            pl.BlockSpec((features, hidden), whole),
            pl.BlockSpec((1, hidden), whole),
            pl.BlockSpec((hidden, hidden), whole),
            pl.BlockSpec((1, hidden), whole),
            pl.BlockSpec((4, hidden), whole),
        ],
        out_shape=[
            jax.ShapeDtypeStruct((features, hidden), jnp.float32),
            jax.ShapeDtypeStruct((1, hidden), jnp.float32),
            jax.ShapeDtypeStruct((hidden, hidden), jnp.float32),
            jax.ShapeDtypeStruct((1, hidden), jnp.float32),
            jax.ShapeDtypeStruct((4, hidden), jnp.float32),
        ],
        compiler_params=pltpu.CompilerParams(dimension_semantics=("arbitrary",)),
    )(
        encoded, act_first, act_second, slope_first, slope_second, grad_raw,
        second_weight, head_weight,
    )
    grad_first, bias_first, grad_second, bias_second, grad_head = outs
    return (grad_first, grad_second, grad_head, bias_first[0], bias_second[0], grad_head_bias)


def composite(seg_colour, seg_log, depth_rank, pixel_rows):
    before = (depth_rank[:, None, :] < depth_rank[:, :, None]).astype(jnp.float32)
    prefix = jnp.exp(jnp.sum(before * seg_log[:, None, :], axis=2))
    up_colour = prefix[..., None] * pixel_rows[:, None, :]
    shaded = prefix * jnp.sum(seg_colour * pixel_rows[:, None, :], axis=2)
    up_log = jnp.sum(before * shaded[:, :, None], axis=1)
    return (up_colour, up_log)


def per_device(
    positions,
    spacing,
    assign,
    depth_rank,
    pixel_grad,
    fourier,
    first_weight,
    first_bias,
    second_weight,
    second_bias,
    head_weight,
    head_bias,
):
    groups = lax.axis_size("space")
    ray_count = positions.shape[1]
    total = ray_count * SEGS
    capacity = 3 * total // (2 * groups)
    slot_count = capacity * groups
    owner = assign.reshape(total)
    member = (owner[:, None] == jnp.arange(groups, dtype=jnp.int32)[None, :]).astype(jnp.int32)
    earlier = jnp.cumsum(member, axis=0) - member
    within = jnp.sum(earlier * member, axis=1)
    target = owner * capacity + within
    dispatch = (target[:, None] == jnp.arange(slot_count, dtype=jnp.int32)[None, :]).astype(
        jnp.float32
    )
    seg_pos = jnp.transpose(positions.reshape(3, total, SEG_LEN), (1, 0, 2))
    seg_gap = spacing.reshape(total, 1, SEG_LEN)
    segments = jnp.concatenate([seg_pos, seg_gap], axis=1).reshape(total, 4 * SEG_LEN)
    outgoing = lax.dot_general(
        dispatch,
        segments,
        (((0,), (0,)), ((), ())),
        precision=lax.Precision.HIGHEST,
        preferred_element_type=jnp.float32,
    )
    outgoing = outgoing.reshape(groups, capacity, 4 * SEG_LEN)
    arrived = lax.all_to_all(outgoing, "space", split_axis=0, concat_axis=0, tiled=True)
    samples = arrived.reshape(slot_count, 4, SEG_LEN)
    params = tuple(
        (
            item[0]
            for item in (
                first_weight,
                first_bias,
                second_weight,
                second_bias,
                head_weight,
                head_bias,
            )
        )
    )
    seg_colour, seg_log, saved = network(samples, fourier, params)
    partials = jnp.concatenate([seg_colour, seg_log[None, :]], axis=0).reshape(
        4, groups, capacity
    )
    returned = lax.all_to_all(partials, "space", split_axis=1, concat_axis=1, tiled=True).reshape(
        4, slot_count
    )
    mine = lax.dot_general(
        dispatch,
        returned,
        (((1,), (1,)), ((), ())),
        precision=lax.Precision.HIGHEST,
        preferred_element_type=jnp.float32,
    )
    up_colour, up_log = composite(
        mine[:, :3].reshape(ray_count, SEGS, 3),
        mine[:, 3].reshape(ray_count, SEGS),
        depth_rank,
        pixel_grad.T,
    )
    upstream = jnp.concatenate([up_colour.reshape(total, 3), up_log.reshape(total, 1)], axis=1)
    sendback = lax.dot_general(
        upstream,
        dispatch,
        (((0,), (0,)), ((), ())),
        precision=lax.Precision.HIGHEST,
        preferred_element_type=jnp.float32,
    )
    sendback = sendback.reshape(4, groups, capacity)
    received = lax.all_to_all(sendback, "space", split_axis=1, concat_axis=1, tiled=True)
    received = received.reshape(4, slot_count).T
    totals = backward(samples, fourier, params, saved, received[:, :3], received[:, 3])
    grad_first, grad_second, grad_head, bias_first, bias_second, bias_head = totals
    replicas = lax.axis_size("ray")
    hidden = bias_first.shape[0]
    heads = grad_head.shape[0]
    small = jnp.concatenate(
        [
            grad_head,
            bias_first[None],
            bias_second[None],
            jnp.pad(bias_head, (0, hidden - heads))[None],
        ],
        axis=0,
    )
    if replicas == 2:
        position = lax.axis_index("ray")
        got_first, got_second, got_small = lax.ppermute(
            (grad_first, grad_second, small), "ray", [(0, 1), (1, 0)]
        )
        rows_first = grad_first.shape[0] // 2
        rows_second = grad_second.shape[0] // 2
        part_first = lax.dynamic_slice_in_dim(
            grad_first + got_first, position * rows_first, rows_first, 0
        )
        part_second = lax.dynamic_slice_in_dim(
            grad_second + got_second, position * rows_second, rows_second, 0
        )
        small = small + got_small
    elif replicas & (replicas - 1) == 0:
        position = lax.axis_index("ray")
        part_first, part_second = grad_first, grad_second
        distance = replicas // 2
        while distance >= 1:
            pairs = [(i, i ^ distance) for i in range(replicas)]
            half = part_first.shape[0] // 2
            upper = (position // distance) % 2
            keep_first = lax.dynamic_slice_in_dim(part_first, upper * half, half, 0)
            send_first = lax.dynamic_slice_in_dim(part_first, (1 - upper) * half, half, 0)
            keep_second = lax.dynamic_slice_in_dim(part_second, upper * half, half, 0)
            send_second = lax.dynamic_slice_in_dim(part_second, (1 - upper) * half, half, 0)
            got_first, got_second, got_small = lax.ppermute(
                (send_first, send_second, small), "ray", pairs
            )
            part_first = keep_first + got_first
            part_second = keep_second + got_second
            small = small + got_small
            distance //= 2
    else:
        part_first = lax.psum_scatter(grad_first, "ray", scatter_dimension=0, tiled=True)
        part_second = lax.psum_scatter(grad_second, "ray", scatter_dimension=0, tiled=True)
        small = lax.psum(small, "ray")
    small_sums = (small[:heads], small[heads], small[heads + 1], small[heads + 2, :heads])
    return (
        part_first[None],
        part_second[None],
        small_sums[0][None],
        small_sums[1][None],
        small_sums[2][None],
        small_sums[3][None],
    )


def solution(mesh):
    placed = (
        P(None, ("space", "ray"), None),
        P(("space", "ray"), None),
        P(("space", "ray"), None, None),
        P(("space", "ray"), None),
        P(None, ("space", "ray")),
        P(),
        P("space", None, None),
        P("space", None),
        P("space", None, None),
        P("space", None),
        P("space", None, None),
        P("space", None),
    )
    return jax.shard_map(
        per_device,
        mesh=mesh,
        in_specs=placed,
        out_specs=(
            P("space", "ray", None),
            P("space", "ray", None),
            P("space", None, None),
            P("space", None),
            P("space", None),
            P("space", None),
        ),
        check_vma=False,
    )
```

```python
import jax
import jax.numpy as jnp
from jax import lax
from jax.sharding import PartitionSpec as P
from jax.experimental import pallas as pl
from jax.experimental.pallas import tpu as pltpu

SEG_LEN = 32
SEGS = 8


two_pi = 6.283185307179586


def gate_of(value):
    return 0.5 * jnp.tanh(0.5 * value) + 0.5


def silu_slope(value):
    gate = gate_of(value)
    return gate * (1.0 + value * (1.0 - gate))


def turn_sin_cos(turns):
    quarter = jnp.floor(turns * 4.0 + 0.5)
    angle = (turns - quarter * 0.25) * two_pi
    square = angle * angle
    sine = angle * (
        1.0 + square * (-1.0 / 6.0 + square * (1.0 / 120.0 + square * (-1.0 / 5040.0)))
    )
    cosine = 1.0 + square * (
        -0.5 + square * (1.0 / 24.0 + square * (-1.0 / 720.0 + square * (1.0 / 40320.0)))
    )
    step = quarter - 4.0 * jnp.floor(quarter * 0.25)
    flip = step >= 2.0
    odd = (step == 1.0) | (step == 3.0)
    sin_out = jnp.where(odd, cosine, sine)
    cos_out = jnp.where(odd, sine, cosine)
    sin_out = jnp.where(flip, -sin_out, sin_out)
    cos_out = jnp.where(flip != odd, -cos_out, cos_out)
    return sin_out, cos_out


def encode(samples, fourier):
    turns = (
        samples[:, 0, :, None] * fourier[0]
        + samples[:, 1, :, None] * fourier[1]
        + samples[:, 2, :, None] * fourier[2]
    )
    sine, cosine = turn_sin_cos(turns)
    joined = jnp.concatenate([sine, cosine], axis=-1)
    return joined.astype(jnp.bfloat16).reshape(-1, joined.shape[-1])


def forward_kernel(
    place_ref, fourier_ref, w1_ref, b1_ref, w2_ref, b2_ref, wh_ref, bh_ref,
    enc_ref, a1_ref, a2_ref, s1_ref, s2_ref, head_ref,
):
    place = place_ref[...]
    fourier = fourier_ref[...]
    turns = (
        fourier[:, 0:1] * place[0:1, :]
        + fourier[:, 1:2] * place[1:2, :]
        + fourier[:, 2:3] * place[2:3, :]
    )
    sine, cosine = turn_sin_cos(turns)
    encoded = jnp.concatenate([sine, cosine], axis=0).astype(jnp.bfloat16)
    enc_ref[...] = encoded
    pre_first = (
        lax.dot_general(
            encoded, w1_ref[...], (((0,), (0,)), ((), ())), preferred_element_type=jnp.float32
        )
        + b1_ref[...]
    )
    gate_first = gate_of(pre_first)
    act_first = (pre_first * gate_first).astype(jnp.bfloat16)
    a1_ref[...] = act_first
    s1_ref[...] = gate_first * (1.0 + pre_first * (1.0 - gate_first))
    pre_second = jnp.dot(act_first, w2_ref[...], preferred_element_type=jnp.float32) + b2_ref[...]
    gate_second = gate_of(pre_second)
    act_second = (pre_second * gate_second).astype(jnp.bfloat16)
    a2_ref[...] = act_second
    s2_ref[...] = gate_second * (1.0 + pre_second * (1.0 - gate_second))
    head_ref[...] = (
        lax.dot_general(
            wh_ref[...], act_second, (((1,), (1,)), ((), ())), preferred_element_type=jnp.float32
        )
        + bh_ref[...]
    )


def backward_kernel(
    enc_ref, a1_ref, a2_ref, s1_ref, s2_ref, raw_ref, w2_ref, wh_ref,
    g1_ref, gb1_ref, g2_ref, gb2_ref, gh_ref,
):
    @pl.when(pl.program_id(0) == 0)
    def _():
        g1_ref[...] = jnp.zeros_like(g1_ref)
        gb1_ref[...] = jnp.zeros_like(gb1_ref)
        g2_ref[...] = jnp.zeros_like(g2_ref)
        gb2_ref[...] = jnp.zeros_like(gb2_ref)
        gh_ref[...] = jnp.zeros_like(gh_ref)

    raw = raw_ref[...]
    back_second = jnp.dot(raw, wh_ref[...], preferred_element_type=jnp.float32)
    delta_second = (back_second * s2_ref[...]).astype(jnp.bfloat16)
    g2_ref[...] += lax.dot_general(
        a1_ref[...], delta_second, (((0,), (0,)), ((), ())), preferred_element_type=jnp.float32
    )
    gb2_ref[...] += jnp.sum(delta_second.astype(jnp.float32), axis=0, keepdims=True)
    back_first = lax.dot_general(
        delta_second, w2_ref[...], (((1,), (1,)), ((), ())), preferred_element_type=jnp.float32
    )
    delta_first = (back_first * s1_ref[...]).astype(jnp.bfloat16)
    g1_ref[...] += jnp.dot(enc_ref[...], delta_first, preferred_element_type=jnp.float32)
    gb1_ref[...] += jnp.sum(delta_first.astype(jnp.float32), axis=0, keepdims=True)
    gh_ref[...] += lax.dot_general(
        raw, a2_ref[...], (((0,), (0,)), ((), ())), preferred_element_type=jnp.float32
    )


BLOCK = 3072


def forward_layers(samples, fourier, params):
    first_weight, first_bias, second_weight, second_bias, head_weight, head_bias = params
    rows = samples.shape[0] * samples.shape[2]
    place = jnp.transpose(samples, (1, 0, 2)).reshape(4, rows)
    features, hidden = first_weight.shape
    heads = head_weight.shape[0]
    whole = lambda i: (0, 0)
    by_row = lambda i: (i, 0)
    by_column = lambda i: (0, i)
    return pl.pallas_call(
        forward_kernel,
        grid=(rows // BLOCK,),
        in_specs=[
            pl.BlockSpec((4, BLOCK), by_column),
            pl.BlockSpec((fourier.shape[1], fourier.shape[0]), whole),
            pl.BlockSpec(first_weight.shape, whole),
            pl.BlockSpec((1, hidden), whole),
            pl.BlockSpec(second_weight.shape, whole),
            pl.BlockSpec((1, hidden), whole),
            pl.BlockSpec(head_weight.shape, whole),
            pl.BlockSpec((heads, 1), whole),
        ],
        out_specs=[
            pl.BlockSpec((features, BLOCK), by_column),
            pl.BlockSpec((BLOCK, hidden), by_row),
            pl.BlockSpec((BLOCK, hidden), by_row),
            pl.BlockSpec((BLOCK, hidden), by_row),
            pl.BlockSpec((BLOCK, hidden), by_row),
            pl.BlockSpec((heads, BLOCK), by_column),
        ],
        out_shape=[
            jax.ShapeDtypeStruct((features, rows), jnp.bfloat16),
            jax.ShapeDtypeStruct((rows, hidden), jnp.bfloat16),
            jax.ShapeDtypeStruct((rows, hidden), jnp.bfloat16),
            jax.ShapeDtypeStruct((rows, hidden), jnp.float32),
            jax.ShapeDtypeStruct((rows, hidden), jnp.float32),
            jax.ShapeDtypeStruct((heads, rows), jnp.float32),
        ],
        compiler_params=pltpu.CompilerParams(dimension_semantics=("arbitrary",)),
    )(
        place,
        fourier.T,
        first_weight,
        first_bias.reshape(1, hidden),
        second_weight,
        second_bias.reshape(1, hidden),
        head_weight,
        head_bias.reshape(heads, 1),
    )


def network(samples, fourier, params):
    seg_count, length = (samples.shape[0], samples.shape[2])
    encoded, act_first, act_second, slope_first, slope_second, head_raw = forward_layers(
        samples, fourier, params
    )
    head_raw = head_raw.reshape(4, seg_count, length)
    density = jax.nn.softplus(head_raw[0])
    colour = jax.nn.sigmoid(head_raw[1:])
    optical = density * samples[:, 3, :]
    inclusive = jnp.cumsum(optical, axis=1)
    enter_light = jnp.exp(optical - inclusive)
    leave_light = jnp.exp(-inclusive)
    weight = enter_light - leave_light
    seg_colour = jnp.sum(weight[None] * colour, axis=2)
    seg_log = -inclusive[:, -1]
    saved = (
        encoded, act_first, act_second, slope_first, slope_second,
        head_raw, colour, weight, leave_light,
    )
    return (seg_colour, seg_log, saved)


def backward(samples, fourier, params, saved, up_colour, up_log):
    first_weight, first_bias, second_weight, second_bias, head_weight, head_bias = params
    encoded, act_first, act_second, slope_first, slope_second = saved[:5]
    head_raw, colour, weight, leave_light = saved[5:]
    up_rows = up_colour.T[:, :, None]
    energy = jnp.sum(colour * up_rows, axis=0)
    spent = weight * energy
    remaining = jnp.sum(spent, axis=1, keepdims=True) - jnp.cumsum(spent, axis=1)
    grad_optical = leave_light * energy - remaining - up_log[:, None]
    grad_density = grad_optical * samples[:, 3, :] * jax.nn.sigmoid(head_raw[0])
    grad_tint = weight[None] * up_rows * colour * (1.0 - colour)
    grad_raw = (
        jnp.concatenate([grad_density[None], grad_tint], axis=0)
        .reshape(4, -1)
        .T.astype(jnp.bfloat16)
    )
    grad_head_bias = jnp.sum(grad_raw.astype(jnp.float32), axis=0)
    rows = grad_raw.shape[0]
    features, hidden = first_weight.shape
    whole = lambda i: (0, 0)
    by_row = lambda i: (i, 0)
    outs = pl.pallas_call(
        backward_kernel,
        grid=(rows // BLOCK,),
        in_specs=[
            pl.BlockSpec((features, BLOCK), lambda i: (0, i)),
            pl.BlockSpec((BLOCK, hidden), by_row),
            pl.BlockSpec((BLOCK, hidden), by_row),
            pl.BlockSpec((BLOCK, hidden), by_row),
            pl.BlockSpec((BLOCK, hidden), by_row),
            pl.BlockSpec((BLOCK, 4), by_row),
            pl.BlockSpec(second_weight.shape, whole),
            pl.BlockSpec(head_weight.shape, whole),
        ],
        out_specs=[
            pl.BlockSpec((features, hidden), whole),
            pl.BlockSpec((1, hidden), whole),
            pl.BlockSpec((hidden, hidden), whole),
            pl.BlockSpec((1, hidden), whole),
            pl.BlockSpec((4, hidden), whole),
        ],
        out_shape=[
            jax.ShapeDtypeStruct((features, hidden), jnp.float32),
            jax.ShapeDtypeStruct((1, hidden), jnp.float32),
            jax.ShapeDtypeStruct((hidden, hidden), jnp.float32),
            jax.ShapeDtypeStruct((1, hidden), jnp.float32),
            jax.ShapeDtypeStruct((4, hidden), jnp.float32),
        ],
        compiler_params=pltpu.CompilerParams(dimension_semantics=("arbitrary",)),
    )(
        encoded, act_first, act_second, slope_first, slope_second, grad_raw,
        second_weight, head_weight,
    )
    grad_first, bias_first, grad_second, bias_second, grad_head = outs
    return (grad_first, grad_second, grad_head, bias_first[0], bias_second[0], grad_head_bias)


def composite(seg_colour, seg_log, depth_rank, pixel_rows):
    before = (depth_rank[:, None, :] < depth_rank[:, :, None]).astype(jnp.float32)
    prefix = jnp.exp(jnp.sum(before * seg_log[:, None, :], axis=2))
    up_colour = prefix[..., None] * pixel_rows[:, None, :]
    shaded = prefix * jnp.sum(seg_colour * pixel_rows[:, None, :], axis=2)
    up_log = jnp.sum(before * shaded[:, :, None], axis=1)
    return (up_colour, up_log)


def per_device(
    positions,
    spacing,
    assign,
    depth_rank,
    pixel_grad,
    fourier,
    first_weight,
    first_bias,
    second_weight,
    second_bias,
    head_weight,
    head_bias,
):
    groups = lax.axis_size("space")
    ray_count = positions.shape[1]
    total = ray_count * SEGS
    capacity = 3 * total // (2 * groups)
    slot_count = capacity * groups
    owner = assign.reshape(total)
    member = (owner[:, None] == jnp.arange(groups, dtype=jnp.int32)[None, :]).astype(jnp.int32)
    earlier = jnp.cumsum(member, axis=0) - member
    within = jnp.sum(earlier * member, axis=1)
    target = owner * capacity + within
    dispatch = (target[:, None] == jnp.arange(slot_count, dtype=jnp.int32)[None, :]).astype(
        jnp.float32
    )
    seg_pos = jnp.transpose(positions.reshape(3, total, SEG_LEN), (1, 0, 2))
    seg_gap = spacing.reshape(total, 1, SEG_LEN)
    segments = jnp.concatenate([seg_pos, seg_gap], axis=1).reshape(total, 4 * SEG_LEN)
    outgoing = lax.dot_general(
        dispatch,
        segments,
        (((0,), (0,)), ((), ())),
        precision=lax.Precision.HIGHEST,
        preferred_element_type=jnp.float32,
    )
    outgoing = outgoing.reshape(groups, capacity, 4 * SEG_LEN)
    arrived = lax.all_to_all(outgoing, "space", split_axis=0, concat_axis=0, tiled=True)
    samples = arrived.reshape(slot_count, 4, SEG_LEN)
    params = tuple(
        (
            item[0]
            for item in (
                first_weight,
                first_bias,
                second_weight,
                second_bias,
                head_weight,
                head_bias,
            )
        )
    )
    seg_colour, seg_log, saved = network(samples, fourier, params)
    partials = jnp.concatenate([seg_colour, seg_log[None, :]], axis=0).reshape(
        4, groups, capacity
    )
    returned = lax.all_to_all(partials, "space", split_axis=1, concat_axis=1, tiled=True).reshape(
        4, slot_count
    )
    mine = lax.dot_general(
        dispatch,
        returned,
        (((1,), (1,)), ((), ())),
        precision=lax.Precision.HIGHEST,
        preferred_element_type=jnp.float32,
    )
    up_colour, up_log = composite(
        mine[:, :3].reshape(ray_count, SEGS, 3),
        mine[:, 3].reshape(ray_count, SEGS),
        depth_rank,
        pixel_grad.T,
    )
    upstream = jnp.concatenate([up_colour.reshape(total, 3), up_log.reshape(total, 1)], axis=1)
    sendback = lax.dot_general(
        upstream,
        dispatch,
        (((0,), (0,)), ((), ())),
        precision=lax.Precision.HIGHEST,
        preferred_element_type=jnp.float32,
    )
    sendback = sendback.reshape(4, groups, capacity)
    received = lax.all_to_all(sendback, "space", split_axis=1, concat_axis=1, tiled=True)
    received = received.reshape(4, slot_count).T
    totals = backward(samples, fourier, params, saved, received[:, :3], received[:, 3])
    grad_first, grad_second, grad_head, bias_first, bias_second, bias_head = totals
    replicas = lax.axis_size("ray")
    hidden = bias_first.shape[0]
    heads = grad_head.shape[0]
    small = jnp.concatenate(
        [
            grad_head,
            bias_first[None],
            bias_second[None],
            jnp.pad(bias_head, (0, hidden - heads))[None],
        ],
        axis=0,
    )
    if replicas == 2:
        position = lax.axis_index("ray")
        got_first, got_second, got_small = lax.ppermute(
            (grad_first, grad_second, small), "ray", [(0, 1), (1, 0)]
        )
        rows_first = grad_first.shape[0] // 2
        rows_second = grad_second.shape[0] // 2
        part_first = lax.dynamic_slice_in_dim(
            grad_first + got_first, position * rows_first, rows_first, 0
        )
        part_second = lax.dynamic_slice_in_dim(
            grad_second + got_second, position * rows_second, rows_second, 0
        )
        small = small + got_small
    elif replicas & (replicas - 1) == 0:
        position = lax.axis_index("ray")
        part_first, part_second = grad_first, grad_second
        distance = replicas // 2
        while distance >= 1:
            pairs = [(i, i ^ distance) for i in range(replicas)]
            half = part_first.shape[0] // 2
            upper = (position // distance) % 2
            keep_first = lax.dynamic_slice_in_dim(part_first, upper * half, half, 0)
            send_first = lax.dynamic_slice_in_dim(part_first, (1 - upper) * half, half, 0)
            keep_second = lax.dynamic_slice_in_dim(part_second, upper * half, half, 0)
            send_second = lax.dynamic_slice_in_dim(part_second, (1 - upper) * half, half, 0)
            got_first, got_second, got_small = lax.ppermute(
                (send_first, send_second, small), "ray", pairs
            )
            part_first = keep_first + got_first
            part_second = keep_second + got_second
            small = small + got_small
            distance //= 2
    else:
        part_first = lax.psum_scatter(grad_first, "ray", scatter_dimension=0, tiled=True)
        part_second = lax.psum_scatter(grad_second, "ray", scatter_dimension=0, tiled=True)
        small = lax.psum(small, "ray")
    small_sums = (small[:heads], small[heads], small[heads + 1], small[heads + 2, :heads])
    return (
        part_first[None],
        part_second[None],
        small_sums[0][None],
        small_sums[1][None],
        small_sums[2][None],
        small_sums[3][None],
    )


def solution(mesh):
    placed = (
        P(None, ("space", "ray"), None),
        P(("space", "ray"), None),
        P(("space", "ray"), None, None),
        P(("space", "ray"), None),
        P(None, ("space", "ray")),
        P(),
        P("space", None, None),
        P("space", None),
        P("space", None, None),
        P("space", None),
        P("space", None, None),
        P("space", None),
    )
    return jax.shard_map(
        per_device,
        mesh=mesh,
        in_specs=placed,
        out_specs=(
            P("space", "ray", None),
            P("space", "ray", None),
            P("space", None, None),
            P("space", None),
            P("space", None),
            P("space", None),
        ),
        check_vma=False,
    )
```

```python
import jax
import jax.numpy as jnp
from jax import lax
from jax.sharding import PartitionSpec as P
from jax.experimental import pallas as pl
from jax.experimental.pallas import tpu as pltpu

SEG_LEN = 32
SEGS = 8


two_pi = 6.283185307179586


def gate_of(value):
    return 0.5 * jnp.tanh(0.5 * value) + 0.5


def silu_slope(value):
    gate = gate_of(value)
    return gate * (1.0 + value * (1.0 - gate))


def turn_sin_cos(turns):
    quarter = jnp.floor(turns * 4.0 + 0.5)
    angle = (turns - quarter * 0.25) * two_pi
    square = angle * angle
    sine = angle * (
        1.0 + square * (-1.0 / 6.0 + square * (1.0 / 120.0 + square * (-1.0 / 5040.0)))
    )
    cosine = 1.0 + square * (
        -0.5 + square * (1.0 / 24.0 + square * (-1.0 / 720.0 + square * (1.0 / 40320.0)))
    )
    step = quarter - 4.0 * jnp.floor(quarter * 0.25)
    flip = step >= 2.0
    odd = (step == 1.0) | (step == 3.0)
    sin_out = jnp.where(odd, cosine, sine)
    cos_out = jnp.where(odd, sine, cosine)
    sin_out = jnp.where(flip, -sin_out, sin_out)
    cos_out = jnp.where(flip != odd, -cos_out, cos_out)
    return sin_out, cos_out


def encode(samples, fourier):
    turns = (
        samples[:, 0, :, None] * fourier[0]
        + samples[:, 1, :, None] * fourier[1]
        + samples[:, 2, :, None] * fourier[2]
    )
    sine, cosine = turn_sin_cos(turns)
    joined = jnp.concatenate([sine, cosine], axis=-1)
    return joined.astype(jnp.bfloat16).reshape(-1, joined.shape[-1])


def forward_kernel(
    place_ref, fourier_ref, w1_ref, b1_ref, w2_ref, b2_ref, wh_ref, bh_ref,
    enc_ref, a1_ref, a2_ref, s1_ref, s2_ref, head_ref,
):
    place = place_ref[...]
    fourier = fourier_ref[...]
    turns = (
        fourier[:, 0:1] * place[0:1, :]
        + fourier[:, 1:2] * place[1:2, :]
        + fourier[:, 2:3] * place[2:3, :]
    )
    sine, cosine = turn_sin_cos(turns)
    encoded = jnp.concatenate([sine, cosine], axis=0).astype(jnp.bfloat16)
    enc_ref[...] = encoded
    pre_first = (
        lax.dot_general(
            encoded, w1_ref[...], (((0,), (0,)), ((), ())), preferred_element_type=jnp.float32
        )
        + b1_ref[...]
    )
    gate_first = gate_of(pre_first)
    act_first = (pre_first * gate_first).astype(jnp.bfloat16)
    a1_ref[...] = act_first
    s1_ref[...] = gate_first * (1.0 + pre_first * (1.0 - gate_first))
    pre_second = jnp.dot(act_first, w2_ref[...], preferred_element_type=jnp.float32) + b2_ref[...]
    gate_second = gate_of(pre_second)
    act_second = (pre_second * gate_second).astype(jnp.bfloat16)
    a2_ref[...] = act_second
    s2_ref[...] = gate_second * (1.0 + pre_second * (1.0 - gate_second))
    head_ref[...] = (
        lax.dot_general(
            wh_ref[...], act_second, (((1,), (1,)), ((), ())), preferred_element_type=jnp.float32
        )
        + bh_ref[...]
    )


def backward_kernel(
    enc_ref, a1_ref, a2_ref, s1_ref, s2_ref, raw_ref, w2_ref, wh_ref,
    g1_ref, gb1_ref, g2_ref, gb2_ref, gh_ref,
):
    @pl.when(pl.program_id(0) == 0)
    def _():
        g1_ref[...] = jnp.zeros_like(g1_ref)
        gb1_ref[...] = jnp.zeros_like(gb1_ref)
        g2_ref[...] = jnp.zeros_like(g2_ref)
        gb2_ref[...] = jnp.zeros_like(gb2_ref)
        gh_ref[...] = jnp.zeros_like(gh_ref)

    raw = raw_ref[...]
    back_second = jnp.dot(raw, wh_ref[...], preferred_element_type=jnp.float32)
    delta_second = (back_second * s2_ref[...]).astype(jnp.bfloat16)
    g2_ref[...] += lax.dot_general(
        a1_ref[...], delta_second, (((0,), (0,)), ((), ())), preferred_element_type=jnp.float32
    )
    gb2_ref[...] += jnp.sum(delta_second.astype(jnp.float32), axis=0, keepdims=True)
    back_first = lax.dot_general(
        delta_second, w2_ref[...], (((1,), (1,)), ((), ())), preferred_element_type=jnp.float32
    )
    delta_first = (back_first * s1_ref[...]).astype(jnp.bfloat16)
    g1_ref[...] += jnp.dot(enc_ref[...], delta_first, preferred_element_type=jnp.float32)
    gb1_ref[...] += jnp.sum(delta_first.astype(jnp.float32), axis=0, keepdims=True)
    gh_ref[...] += lax.dot_general(
        raw, a2_ref[...], (((0,), (0,)), ((), ())), preferred_element_type=jnp.float32
    )


BLOCK = 3072
FORWARD_BLOCK = 1024


def forward_layers(samples, fourier, params):
    first_weight, first_bias, second_weight, second_bias, head_weight, head_bias = params
    rows = samples.shape[0] * samples.shape[2]
    place = jnp.transpose(samples, (1, 0, 2)).reshape(4, rows)
    features, hidden = first_weight.shape
    heads = head_weight.shape[0]
    whole = lambda i: (0, 0)
    by_row = lambda i: (i, 0)
    by_column = lambda i: (0, i)
    return pl.pallas_call(
        forward_kernel,
        grid=(rows // FORWARD_BLOCK,),
        in_specs=[
            pl.BlockSpec((4, FORWARD_BLOCK), by_column),
            pl.BlockSpec((fourier.shape[1], fourier.shape[0]), whole),
            pl.BlockSpec(first_weight.shape, whole),
            pl.BlockSpec((1, hidden), whole),
            pl.BlockSpec(second_weight.shape, whole),
            pl.BlockSpec((1, hidden), whole),
            pl.BlockSpec(head_weight.shape, whole),
            pl.BlockSpec((heads, 1), whole),
        ],
        out_specs=[
            pl.BlockSpec((features, FORWARD_BLOCK), by_column),
            pl.BlockSpec((FORWARD_BLOCK, hidden), by_row),
            pl.BlockSpec((FORWARD_BLOCK, hidden), by_row),
            pl.BlockSpec((FORWARD_BLOCK, hidden), by_row),
            pl.BlockSpec((FORWARD_BLOCK, hidden), by_row),
            pl.BlockSpec((heads, FORWARD_BLOCK), by_column),
        ],
        out_shape=[
            jax.ShapeDtypeStruct((features, rows), jnp.bfloat16),
            jax.ShapeDtypeStruct((rows, hidden), jnp.bfloat16),
            jax.ShapeDtypeStruct((rows, hidden), jnp.bfloat16),
            jax.ShapeDtypeStruct((rows, hidden), jnp.float32),
            jax.ShapeDtypeStruct((rows, hidden), jnp.float32),
            jax.ShapeDtypeStruct((heads, rows), jnp.float32),
        ],
        compiler_params=pltpu.CompilerParams(dimension_semantics=("arbitrary",)),
    )(
        place,
        fourier.T,
        first_weight,
        first_bias.reshape(1, hidden),
        second_weight,
        second_bias.reshape(1, hidden),
        head_weight,
        head_bias.reshape(heads, 1),
    )


def network(samples, fourier, params):
    seg_count, length = (samples.shape[0], samples.shape[2])
    encoded, act_first, act_second, slope_first, slope_second, head_raw = forward_layers(
        samples, fourier, params
    )
    head_raw = head_raw.reshape(4, seg_count, length)
    density = jax.nn.softplus(head_raw[0])
    colour = jax.nn.sigmoid(head_raw[1:])
    optical = density * samples[:, 3, :]
    inclusive = jnp.cumsum(optical, axis=1)
    enter_light = jnp.exp(optical - inclusive)
    leave_light = jnp.exp(-inclusive)
    weight = enter_light - leave_light
    seg_colour = jnp.sum(weight[None] * colour, axis=2)
    seg_log = -inclusive[:, -1]
    saved = (
        encoded, act_first, act_second, slope_first, slope_second,
        head_raw, colour, weight, leave_light,
    )
    return (seg_colour, seg_log, saved)


def backward(samples, fourier, params, saved, up_colour, up_log):
    first_weight, first_bias, second_weight, second_bias, head_weight, head_bias = params
    encoded, act_first, act_second, slope_first, slope_second = saved[:5]
    head_raw, colour, weight, leave_light = saved[5:]
    up_rows = up_colour.T[:, :, None]
    energy = jnp.sum(colour * up_rows, axis=0)
    spent = weight * energy
    remaining = jnp.sum(spent, axis=1, keepdims=True) - jnp.cumsum(spent, axis=1)
    grad_optical = leave_light * energy - remaining - up_log[:, None]
    grad_density = grad_optical * samples[:, 3, :] * jax.nn.sigmoid(head_raw[0])
    grad_tint = weight[None] * up_rows * colour * (1.0 - colour)
    grad_raw = (
        jnp.concatenate([grad_density[None], grad_tint], axis=0)
        .reshape(4, -1)
        .T.astype(jnp.bfloat16)
    )
    grad_head_bias = jnp.sum(grad_raw.astype(jnp.float32), axis=0)
    rows = grad_raw.shape[0]
    features, hidden = first_weight.shape
    whole = lambda i: (0, 0)
    by_row = lambda i: (i, 0)
    outs = pl.pallas_call(
        backward_kernel,
        grid=(rows // BLOCK,),
        in_specs=[
            pl.BlockSpec((features, BLOCK), lambda i: (0, i)),
            pl.BlockSpec((BLOCK, hidden), by_row),
            pl.BlockSpec((BLOCK, hidden), by_row),
            pl.BlockSpec((BLOCK, hidden), by_row),
            pl.BlockSpec((BLOCK, hidden), by_row),
            pl.BlockSpec((BLOCK, 4), by_row),
            pl.BlockSpec(second_weight.shape, whole),
            pl.BlockSpec(head_weight.shape, whole),
        ],
        out_specs=[
            pl.BlockSpec((features, hidden), whole),
            pl.BlockSpec((1, hidden), whole),
            pl.BlockSpec((hidden, hidden), whole),
            pl.BlockSpec((1, hidden), whole),
            pl.BlockSpec((4, hidden), whole),
        ],
        out_shape=[
            jax.ShapeDtypeStruct((features, hidden), jnp.float32),
            jax.ShapeDtypeStruct((1, hidden), jnp.float32),
            jax.ShapeDtypeStruct((hidden, hidden), jnp.float32),
            jax.ShapeDtypeStruct((1, hidden), jnp.float32),
            jax.ShapeDtypeStruct((4, hidden), jnp.float32),
        ],
        compiler_params=pltpu.CompilerParams(dimension_semantics=("arbitrary",)),
    )(
        encoded, act_first, act_second, slope_first, slope_second, grad_raw,
        second_weight, head_weight,
    )
    grad_first, bias_first, grad_second, bias_second, grad_head = outs
    return (grad_first, grad_second, grad_head, bias_first[0], bias_second[0], grad_head_bias)


def composite(seg_colour, seg_log, depth_rank, pixel_rows):
    before = (depth_rank[:, None, :] < depth_rank[:, :, None]).astype(jnp.float32)
    prefix = jnp.exp(jnp.sum(before * seg_log[:, None, :], axis=2))
    up_colour = prefix[..., None] * pixel_rows[:, None, :]
    shaded = prefix * jnp.sum(seg_colour * pixel_rows[:, None, :], axis=2)
    up_log = jnp.sum(before * shaded[:, :, None], axis=1)
    return (up_colour, up_log)


def per_device(
    positions,
    spacing,
    assign,
    depth_rank,
    pixel_grad,
    fourier,
    first_weight,
    first_bias,
    second_weight,
    second_bias,
    head_weight,
    head_bias,
):
    groups = lax.axis_size("space")
    ray_count = positions.shape[1]
    total = ray_count * SEGS
    capacity = 3 * total // (2 * groups)
    slot_count = capacity * groups
    owner = assign.reshape(total)
    member = (owner[:, None] == jnp.arange(groups, dtype=jnp.int32)[None, :]).astype(jnp.int32)
    earlier = jnp.cumsum(member, axis=0) - member
    within = jnp.sum(earlier * member, axis=1)
    target = owner * capacity + within
    dispatch = (target[:, None] == jnp.arange(slot_count, dtype=jnp.int32)[None, :]).astype(
        jnp.float32
    )
    seg_pos = jnp.transpose(positions.reshape(3, total, SEG_LEN), (1, 0, 2))
    seg_gap = spacing.reshape(total, 1, SEG_LEN)
    segments = jnp.concatenate([seg_pos, seg_gap], axis=1).reshape(total, 4 * SEG_LEN)
    outgoing = lax.dot_general(
        dispatch,
        segments,
        (((0,), (0,)), ((), ())),
        precision=lax.Precision.HIGHEST,
        preferred_element_type=jnp.float32,
    )
    outgoing = outgoing.reshape(groups, capacity, 4 * SEG_LEN)
    arrived = lax.all_to_all(outgoing, "space", split_axis=0, concat_axis=0, tiled=True)
    samples = arrived.reshape(slot_count, 4, SEG_LEN)
    params = tuple(
        (
            item[0]
            for item in (
                first_weight,
                first_bias,
                second_weight,
                second_bias,
                head_weight,
                head_bias,
            )
        )
    )
    seg_colour, seg_log, saved = network(samples, fourier, params)
    partials = jnp.concatenate([seg_colour, seg_log[None, :]], axis=0).reshape(
        4, groups, capacity
    )
    returned = lax.all_to_all(partials, "space", split_axis=1, concat_axis=1, tiled=True).reshape(
        4, slot_count
    )
    mine = lax.dot_general(
        dispatch,
        returned,
        (((1,), (1,)), ((), ())),
        precision=lax.Precision.HIGHEST,
        preferred_element_type=jnp.float32,
    )
    up_colour, up_log = composite(
        mine[:, :3].reshape(ray_count, SEGS, 3),
        mine[:, 3].reshape(ray_count, SEGS),
        depth_rank,
        pixel_grad.T,
    )
    upstream = jnp.concatenate([up_colour.reshape(total, 3), up_log.reshape(total, 1)], axis=1)
    sendback = lax.dot_general(
        upstream,
        dispatch,
        (((0,), (0,)), ((), ())),
        precision=lax.Precision.HIGHEST,
        preferred_element_type=jnp.float32,
    )
    sendback = sendback.reshape(4, groups, capacity)
    received = lax.all_to_all(sendback, "space", split_axis=1, concat_axis=1, tiled=True)
    received = received.reshape(4, slot_count).T
    totals = backward(samples, fourier, params, saved, received[:, :3], received[:, 3])
    grad_first, grad_second, grad_head, bias_first, bias_second, bias_head = totals
    replicas = lax.axis_size("ray")
    hidden = bias_first.shape[0]
    heads = grad_head.shape[0]
    small = jnp.concatenate(
        [
            grad_head,
            bias_first[None],
            bias_second[None],
            jnp.pad(bias_head, (0, hidden - heads))[None],
        ],
        axis=0,
    )
    if replicas == 2:
        position = lax.axis_index("ray")
        got_first, got_second, got_small = lax.ppermute(
            (grad_first, grad_second, small), "ray", [(0, 1), (1, 0)]
        )
        rows_first = grad_first.shape[0] // 2
        rows_second = grad_second.shape[0] // 2
        part_first = lax.dynamic_slice_in_dim(
            grad_first + got_first, position * rows_first, rows_first, 0
        )
        part_second = lax.dynamic_slice_in_dim(
            grad_second + got_second, position * rows_second, rows_second, 0
        )
        small = small + got_small
    elif replicas & (replicas - 1) == 0:
        position = lax.axis_index("ray")
        part_first, part_second = grad_first, grad_second
        distance = replicas // 2
        while distance >= 1:
            pairs = [(i, i ^ distance) for i in range(replicas)]
            half = part_first.shape[0] // 2
            upper = (position // distance) % 2
            keep_first = lax.dynamic_slice_in_dim(part_first, upper * half, half, 0)
            send_first = lax.dynamic_slice_in_dim(part_first, (1 - upper) * half, half, 0)
            keep_second = lax.dynamic_slice_in_dim(part_second, upper * half, half, 0)
            send_second = lax.dynamic_slice_in_dim(part_second, (1 - upper) * half, half, 0)
            got_first, got_second, got_small = lax.ppermute(
                (send_first, send_second, small), "ray", pairs
            )
            part_first = keep_first + got_first
            part_second = keep_second + got_second
            small = small + got_small
            distance //= 2
    else:
        part_first = lax.psum_scatter(grad_first, "ray", scatter_dimension=0, tiled=True)
        part_second = lax.psum_scatter(grad_second, "ray", scatter_dimension=0, tiled=True)
        small = lax.psum(small, "ray")
    small_sums = (small[:heads], small[heads], small[heads + 1], small[heads + 2, :heads])
    return (
        part_first[None],
        part_second[None],
        small_sums[0][None],
        small_sums[1][None],
        small_sums[2][None],
        small_sums[3][None],
    )


def solution(mesh):
    placed = (
        P(None, ("space", "ray"), None),
        P(("space", "ray"), None),
        P(("space", "ray"), None, None),
        P(("space", "ray"), None),
        P(None, ("space", "ray")),
        P(),
        P("space", None, None),
        P("space", None),
        P("space", None, None),
        P("space", None),
        P("space", None, None),
        P("space", None),
    )
    return jax.shard_map(
        per_device,
        mesh=mesh,
        in_specs=placed,
        out_specs=(
            P("space", "ray", None),
            P("space", "ray", None),
            P("space", None, None),
            P("space", None),
            P("space", None),
            P("space", None),
        ),
        check_vma=False,
    )
```

```python
import jax
import jax.numpy as jnp
from jax import lax
from jax.sharding import PartitionSpec as P
from jax.experimental import pallas as pl
from jax.experimental.pallas import tpu as pltpu

SEG_LEN = 32
SEGS = 8


two_pi = 6.283185307179586


def gate_of(value):
    return 0.5 * jnp.tanh(0.5 * value) + 0.5


def silu_slope(value):
    gate = gate_of(value)
    return gate * (1.0 + value * (1.0 - gate))


def turn_sin_cos(turns):
    quarter = jnp.floor(turns * 4.0 + 0.5)
    angle = (turns - quarter * 0.25) * two_pi
    square = angle * angle
    sine = angle * (
        1.0 + square * (-1.0 / 6.0 + square * (1.0 / 120.0 + square * (-1.0 / 5040.0)))
    )
    cosine = 1.0 + square * (
        -0.5 + square * (1.0 / 24.0 + square * (-1.0 / 720.0 + square * (1.0 / 40320.0)))
    )
    step = quarter - 4.0 * jnp.floor(quarter * 0.25)
    flip = step >= 2.0
    odd = (step == 1.0) | (step == 3.0)
    sin_out = jnp.where(odd, cosine, sine)
    cos_out = jnp.where(odd, sine, cosine)
    sin_out = jnp.where(flip, -sin_out, sin_out)
    cos_out = jnp.where(flip != odd, -cos_out, cos_out)
    return sin_out, cos_out


def encode(samples, fourier):
    turns = (
        samples[:, 0, :, None] * fourier[0]
        + samples[:, 1, :, None] * fourier[1]
        + samples[:, 2, :, None] * fourier[2]
    )
    sine, cosine = turn_sin_cos(turns)
    joined = jnp.concatenate([sine, cosine], axis=-1)
    return joined.astype(jnp.bfloat16).reshape(-1, joined.shape[-1])


def forward_kernel(
    place_ref, fourier_ref, w1_ref, b1_ref, w2_ref, b2_ref, wh_ref, bh_ref,
    enc_ref, a1_ref, a2_ref, s1_ref, s2_ref, head_ref,
):
    place = place_ref[...]
    fourier = fourier_ref[...]
    turns = (
        fourier[:, 0:1] * place[0:1, :]
        + fourier[:, 1:2] * place[1:2, :]
        + fourier[:, 2:3] * place[2:3, :]
    )
    sine, cosine = turn_sin_cos(turns)
    encoded = jnp.concatenate([sine, cosine], axis=0).astype(jnp.bfloat16)
    enc_ref[...] = encoded
    pre_first = (
        lax.dot_general(
            encoded, w1_ref[...], (((0,), (0,)), ((), ())), preferred_element_type=jnp.float32
        )
        + b1_ref[...]
    )
    gate_first = gate_of(pre_first)
    act_first = (pre_first * gate_first).astype(jnp.bfloat16)
    a1_ref[...] = act_first
    s1_ref[...] = gate_first * (1.0 + pre_first * (1.0 - gate_first))
    pre_second = jnp.dot(act_first, w2_ref[...], preferred_element_type=jnp.float32) + b2_ref[...]
    gate_second = gate_of(pre_second)
    act_second = (pre_second * gate_second).astype(jnp.bfloat16)
    a2_ref[...] = act_second
    s2_ref[...] = gate_second * (1.0 + pre_second * (1.0 - gate_second))
    head_ref[...] = (
        lax.dot_general(
            wh_ref[...], act_second, (((1,), (1,)), ((), ())), preferred_element_type=jnp.float32
        )
        + bh_ref[...]
    )


def backward_kernel(
    enc_ref, a1_ref, a2_ref, s1_ref, s2_ref, raw_ref, w2_ref, wh_ref,
    g1_ref, gb1_ref, g2_ref, gb2_ref, gh_ref,
):
    @pl.when(pl.program_id(0) == 0)
    def _():
        g1_ref[...] = jnp.zeros_like(g1_ref)
        gb1_ref[...] = jnp.zeros_like(gb1_ref)
        g2_ref[...] = jnp.zeros_like(g2_ref)
        gb2_ref[...] = jnp.zeros_like(gb2_ref)
        gh_ref[...] = jnp.zeros_like(gh_ref)

    raw = raw_ref[...]
    back_second = jnp.dot(raw, wh_ref[...], preferred_element_type=jnp.float32)
    delta_second = (back_second * s2_ref[...]).astype(jnp.bfloat16)
    g2_ref[...] += lax.dot_general(
        a1_ref[...], delta_second, (((0,), (0,)), ((), ())), preferred_element_type=jnp.float32
    )
    gb2_ref[...] += jnp.sum(delta_second.astype(jnp.float32), axis=0, keepdims=True)
    back_first = lax.dot_general(
        delta_second, w2_ref[...], (((1,), (1,)), ((), ())), preferred_element_type=jnp.float32
    )
    delta_first = (back_first * s1_ref[...]).astype(jnp.bfloat16)
    g1_ref[...] += jnp.dot(enc_ref[...], delta_first, preferred_element_type=jnp.float32)
    gb1_ref[...] += jnp.sum(delta_first.astype(jnp.float32), axis=0, keepdims=True)
    gh_ref[...] += lax.dot_general(
        raw, a2_ref[...], (((0,), (0,)), ((), ())), preferred_element_type=jnp.float32
    )


BLOCK = 3072
FORWARD_BLOCK = 512


def forward_layers(samples, fourier, params):
    first_weight, first_bias, second_weight, second_bias, head_weight, head_bias = params
    rows = samples.shape[0] * samples.shape[2]
    place = jnp.transpose(samples, (1, 0, 2)).reshape(4, rows)
    features, hidden = first_weight.shape
    heads = head_weight.shape[0]
    whole = lambda i: (0, 0)
    by_row = lambda i: (i, 0)
    by_column = lambda i: (0, i)
    return pl.pallas_call(
        forward_kernel,
        grid=(rows // FORWARD_BLOCK,),
        in_specs=[
            pl.BlockSpec((4, FORWARD_BLOCK), by_column),
            pl.BlockSpec((fourier.shape[1], fourier.shape[0]), whole),
            pl.BlockSpec(first_weight.shape, whole),
            pl.BlockSpec((1, hidden), whole),
            pl.BlockSpec(second_weight.shape, whole),
            pl.BlockSpec((1, hidden), whole),
            pl.BlockSpec(head_weight.shape, whole),
            pl.BlockSpec((heads, 1), whole),
        ],
        out_specs=[
            pl.BlockSpec((features, FORWARD_BLOCK), by_column),
            pl.BlockSpec((FORWARD_BLOCK, hidden), by_row),
            pl.BlockSpec((FORWARD_BLOCK, hidden), by_row),
            pl.BlockSpec((FORWARD_BLOCK, hidden), by_row),
            pl.BlockSpec((FORWARD_BLOCK, hidden), by_row),
            pl.BlockSpec((heads, FORWARD_BLOCK), by_column),
        ],
        out_shape=[
            jax.ShapeDtypeStruct((features, rows), jnp.bfloat16),
            jax.ShapeDtypeStruct((rows, hidden), jnp.bfloat16),
            jax.ShapeDtypeStruct((rows, hidden), jnp.bfloat16),
            jax.ShapeDtypeStruct((rows, hidden), jnp.float32),
            jax.ShapeDtypeStruct((rows, hidden), jnp.float32),
            jax.ShapeDtypeStruct((heads, rows), jnp.float32),
        ],
        compiler_params=pltpu.CompilerParams(dimension_semantics=("arbitrary",)),
    )(
        place,
        fourier.T,
        first_weight,
        first_bias.reshape(1, hidden),
        second_weight,
        second_bias.reshape(1, hidden),
        head_weight,
        head_bias.reshape(heads, 1),
    )


def network(samples, fourier, params):
    seg_count, length = (samples.shape[0], samples.shape[2])
    encoded, act_first, act_second, slope_first, slope_second, head_raw = forward_layers(
        samples, fourier, params
    )
    head_raw = head_raw.reshape(4, seg_count, length)
    density = jax.nn.softplus(head_raw[0])
    colour = jax.nn.sigmoid(head_raw[1:])
    optical = density * samples[:, 3, :]
    inclusive = jnp.cumsum(optical, axis=1)
    enter_light = jnp.exp(optical - inclusive)
    leave_light = jnp.exp(-inclusive)
    weight = enter_light - leave_light
    seg_colour = jnp.sum(weight[None] * colour, axis=2)
    seg_log = -inclusive[:, -1]
    saved = (
        encoded, act_first, act_second, slope_first, slope_second,
        head_raw, colour, weight, leave_light,
    )
    return (seg_colour, seg_log, saved)


def backward(samples, fourier, params, saved, up_colour, up_log):
    first_weight, first_bias, second_weight, second_bias, head_weight, head_bias = params
    encoded, act_first, act_second, slope_first, slope_second = saved[:5]
    head_raw, colour, weight, leave_light = saved[5:]
    up_rows = up_colour.T[:, :, None]
    energy = jnp.sum(colour * up_rows, axis=0)
    spent = weight * energy
    remaining = jnp.sum(spent, axis=1, keepdims=True) - jnp.cumsum(spent, axis=1)
    grad_optical = leave_light * energy - remaining - up_log[:, None]
    grad_density = grad_optical * samples[:, 3, :] * jax.nn.sigmoid(head_raw[0])
    grad_tint = weight[None] * up_rows * colour * (1.0 - colour)
    grad_raw = (
        jnp.concatenate([grad_density[None], grad_tint], axis=0)
        .reshape(4, -1)
        .T.astype(jnp.bfloat16)
    )
    grad_head_bias = jnp.sum(grad_raw.astype(jnp.float32), axis=0)
    rows = grad_raw.shape[0]
    features, hidden = first_weight.shape
    whole = lambda i: (0, 0)
    by_row = lambda i: (i, 0)
    outs = pl.pallas_call(
        backward_kernel,
        grid=(rows // BLOCK,),
        in_specs=[
            pl.BlockSpec((features, BLOCK), lambda i: (0, i)),
            pl.BlockSpec((BLOCK, hidden), by_row),
            pl.BlockSpec((BLOCK, hidden), by_row),
            pl.BlockSpec((BLOCK, hidden), by_row),
            pl.BlockSpec((BLOCK, hidden), by_row),
            pl.BlockSpec((BLOCK, 4), by_row),
            pl.BlockSpec(second_weight.shape, whole),
            pl.BlockSpec(head_weight.shape, whole),
        ],
        out_specs=[
            pl.BlockSpec((features, hidden), whole),
            pl.BlockSpec((1, hidden), whole),
            pl.BlockSpec((hidden, hidden), whole),
            pl.BlockSpec((1, hidden), whole),
            pl.BlockSpec((4, hidden), whole),
        ],
        out_shape=[
            jax.ShapeDtypeStruct((features, hidden), jnp.float32),
            jax.ShapeDtypeStruct((1, hidden), jnp.float32),
            jax.ShapeDtypeStruct((hidden, hidden), jnp.float32),
            jax.ShapeDtypeStruct((1, hidden), jnp.float32),
            jax.ShapeDtypeStruct((4, hidden), jnp.float32),
        ],
        compiler_params=pltpu.CompilerParams(dimension_semantics=("arbitrary",)),
    )(
        encoded, act_first, act_second, slope_first, slope_second, grad_raw,
        second_weight, head_weight,
    )
    grad_first, bias_first, grad_second, bias_second, grad_head = outs
    return (grad_first, grad_second, grad_head, bias_first[0], bias_second[0], grad_head_bias)


def composite(seg_colour, seg_log, depth_rank, pixel_rows):
    before = (depth_rank[:, None, :] < depth_rank[:, :, None]).astype(jnp.float32)
    prefix = jnp.exp(jnp.sum(before * seg_log[:, None, :], axis=2))
    up_colour = prefix[..., None] * pixel_rows[:, None, :]
    shaded = prefix * jnp.sum(seg_colour * pixel_rows[:, None, :], axis=2)
    up_log = jnp.sum(before * shaded[:, :, None], axis=1)
    return (up_colour, up_log)


def per_device(
    positions,
    spacing,
    assign,
    depth_rank,
    pixel_grad,
    fourier,
    first_weight,
    first_bias,
    second_weight,
    second_bias,
    head_weight,
    head_bias,
):
    groups = lax.axis_size("space")
    ray_count = positions.shape[1]
    total = ray_count * SEGS
    capacity = 3 * total // (2 * groups)
    slot_count = capacity * groups
    owner = assign.reshape(total)
    member = (owner[:, None] == jnp.arange(groups, dtype=jnp.int32)[None, :]).astype(jnp.int32)
    earlier = jnp.cumsum(member, axis=0) - member
    within = jnp.sum(earlier * member, axis=1)
    target = owner * capacity + within
    dispatch = (target[:, None] == jnp.arange(slot_count, dtype=jnp.int32)[None, :]).astype(
        jnp.float32
    )
    seg_pos = jnp.transpose(positions.reshape(3, total, SEG_LEN), (1, 0, 2))
    seg_gap = spacing.reshape(total, 1, SEG_LEN)
    segments = jnp.concatenate([seg_pos, seg_gap], axis=1).reshape(total, 4 * SEG_LEN)
    outgoing = lax.dot_general(
        dispatch,
        segments,
        (((0,), (0,)), ((), ())),
        precision=lax.Precision.HIGHEST,
        preferred_element_type=jnp.float32,
    )
    outgoing = outgoing.reshape(groups, capacity, 4 * SEG_LEN)
    arrived = lax.all_to_all(outgoing, "space", split_axis=0, concat_axis=0, tiled=True)
    samples = arrived.reshape(slot_count, 4, SEG_LEN)
    params = tuple(
        (
            item[0]
            for item in (
                first_weight,
                first_bias,
                second_weight,
                second_bias,
                head_weight,
                head_bias,
            )
        )
    )
    seg_colour, seg_log, saved = network(samples, fourier, params)
    partials = jnp.concatenate([seg_colour, seg_log[None, :]], axis=0).reshape(
        4, groups, capacity
    )
    returned = lax.all_to_all(partials, "space", split_axis=1, concat_axis=1, tiled=True).reshape(
        4, slot_count
    )
    mine = lax.dot_general(
        dispatch,
        returned,
        (((1,), (1,)), ((), ())),
        precision=lax.Precision.HIGHEST,
        preferred_element_type=jnp.float32,
    )
    up_colour, up_log = composite(
        mine[:, :3].reshape(ray_count, SEGS, 3),
        mine[:, 3].reshape(ray_count, SEGS),
        depth_rank,
        pixel_grad.T,
    )
    upstream = jnp.concatenate([up_colour.reshape(total, 3), up_log.reshape(total, 1)], axis=1)
    sendback = lax.dot_general(
        upstream,
        dispatch,
        (((0,), (0,)), ((), ())),
        precision=lax.Precision.HIGHEST,
        preferred_element_type=jnp.float32,
    )
    sendback = sendback.reshape(4, groups, capacity)
    received = lax.all_to_all(sendback, "space", split_axis=1, concat_axis=1, tiled=True)
    received = received.reshape(4, slot_count).T
    totals = backward(samples, fourier, params, saved, received[:, :3], received[:, 3])
    grad_first, grad_second, grad_head, bias_first, bias_second, bias_head = totals
    replicas = lax.axis_size("ray")
    hidden = bias_first.shape[0]
    heads = grad_head.shape[0]
    small = jnp.concatenate(
        [
            grad_head,
            bias_first[None],
            bias_second[None],
            jnp.pad(bias_head, (0, hidden - heads))[None],
        ],
        axis=0,
    )
    if replicas == 2:
        position = lax.axis_index("ray")
        got_first, got_second, got_small = lax.ppermute(
            (grad_first, grad_second, small), "ray", [(0, 1), (1, 0)]
        )
        rows_first = grad_first.shape[0] // 2
        rows_second = grad_second.shape[0] // 2
        part_first = lax.dynamic_slice_in_dim(
            grad_first + got_first, position * rows_first, rows_first, 0
        )
        part_second = lax.dynamic_slice_in_dim(
            grad_second + got_second, position * rows_second, rows_second, 0
        )
        small = small + got_small
    elif replicas & (replicas - 1) == 0:
        position = lax.axis_index("ray")
        part_first, part_second = grad_first, grad_second
        distance = replicas // 2
        while distance >= 1:
            pairs = [(i, i ^ distance) for i in range(replicas)]
            half = part_first.shape[0] // 2
            upper = (position // distance) % 2
            keep_first = lax.dynamic_slice_in_dim(part_first, upper * half, half, 0)
            send_first = lax.dynamic_slice_in_dim(part_first, (1 - upper) * half, half, 0)
            keep_second = lax.dynamic_slice_in_dim(part_second, upper * half, half, 0)
            send_second = lax.dynamic_slice_in_dim(part_second, (1 - upper) * half, half, 0)
            got_first, got_second, got_small = lax.ppermute(
                (send_first, send_second, small), "ray", pairs
            )
            part_first = keep_first + got_first
            part_second = keep_second + got_second
            small = small + got_small
            distance //= 2
    else:
        part_first = lax.psum_scatter(grad_first, "ray", scatter_dimension=0, tiled=True)
        part_second = lax.psum_scatter(grad_second, "ray", scatter_dimension=0, tiled=True)
        small = lax.psum(small, "ray")
    small_sums = (small[:heads], small[heads], small[heads + 1], small[heads + 2, :heads])
    return (
        part_first[None],
        part_second[None],
        small_sums[0][None],
        small_sums[1][None],
        small_sums[2][None],
        small_sums[3][None],
    )


def solution(mesh):
    placed = (
        P(None, ("space", "ray"), None),
        P(("space", "ray"), None),
        P(("space", "ray"), None, None),
        P(("space", "ray"), None),
        P(None, ("space", "ray")),
        P(),
        P("space", None, None),
        P("space", None),
        P("space", None, None),
        P("space", None),
        P("space", None, None),
        P("space", None),
    )
    return jax.shard_map(
        per_device,
        mesh=mesh,
        in_specs=placed,
        out_specs=(
            P("space", "ray", None),
            P("space", "ray", None),
            P("space", None, None),
            P("space", None),
            P("space", None),
            P("space", None),
        ),
        check_vma=False,
    )
```

```python
import jax
import jax.numpy as jnp
from jax import lax
from jax.sharding import PartitionSpec as P
from jax.experimental import pallas as pl
from jax.experimental.pallas import tpu as pltpu

SEG_LEN = 32
SEGS = 8


two_pi = 6.283185307179586


def gate_of(value):
    return 0.5 * jnp.tanh(0.5 * value) + 0.5


def silu_slope(value):
    gate = gate_of(value)
    return gate * (1.0 + value * (1.0 - gate))


def turn_sin_cos(turns):
    quarter = jnp.floor(turns * 4.0 + 0.5)
    angle = (turns - quarter * 0.25) * two_pi
    square = angle * angle
    sine = angle * (
        1.0 + square * (-1.0 / 6.0 + square * (1.0 / 120.0 + square * (-1.0 / 5040.0)))
    )
    cosine = 1.0 + square * (
        -0.5 + square * (1.0 / 24.0 + square * (-1.0 / 720.0 + square * (1.0 / 40320.0)))
    )
    step = quarter - 4.0 * jnp.floor(quarter * 0.25)
    flip = step >= 2.0
    odd = (step == 1.0) | (step == 3.0)
    sin_out = jnp.where(odd, cosine, sine)
    cos_out = jnp.where(odd, sine, cosine)
    sin_out = jnp.where(flip, -sin_out, sin_out)
    cos_out = jnp.where(flip != odd, -cos_out, cos_out)
    return sin_out, cos_out


def encode(samples, fourier):
    turns = (
        samples[:, 0, :, None] * fourier[0]
        + samples[:, 1, :, None] * fourier[1]
        + samples[:, 2, :, None] * fourier[2]
    )
    sine, cosine = turn_sin_cos(turns)
    joined = jnp.concatenate([sine, cosine], axis=-1)
    return joined.astype(jnp.bfloat16).reshape(-1, joined.shape[-1])


def forward_kernel(
    place_ref, fourier_ref, w1_ref, b1_ref, w2_ref, b2_ref, wh_ref, bh_ref,
    enc_ref, a1_ref, a2_ref, s1_ref, s2_ref, head_ref,
):
    place = place_ref[...]
    fourier = fourier_ref[...]
    turns = (
        fourier[:, 0:1] * place[0:1, :]
        + fourier[:, 1:2] * place[1:2, :]
        + fourier[:, 2:3] * place[2:3, :]
    )
    sine, cosine = turn_sin_cos(turns)
    encoded = jnp.concatenate([sine, cosine], axis=0).astype(jnp.bfloat16)
    enc_ref[...] = encoded
    pre_first = (
        lax.dot_general(
            encoded, w1_ref[...], (((0,), (0,)), ((), ())), preferred_element_type=jnp.float32
        )
        + b1_ref[...]
    )
    gate_first = gate_of(pre_first)
    act_first = (pre_first * gate_first).astype(jnp.bfloat16)
    a1_ref[...] = act_first
    s1_ref[...] = gate_first * (1.0 + pre_first * (1.0 - gate_first))
    pre_second = jnp.dot(act_first, w2_ref[...], preferred_element_type=jnp.float32) + b2_ref[...]
    gate_second = gate_of(pre_second)
    act_second = (pre_second * gate_second).astype(jnp.bfloat16)
    a2_ref[...] = act_second
    s2_ref[...] = gate_second * (1.0 + pre_second * (1.0 - gate_second))
    head_ref[...] = (
        lax.dot_general(
            wh_ref[...], act_second, (((1,), (1,)), ((), ())), preferred_element_type=jnp.float32
        )
        + bh_ref[...]
    )


def backward_kernel(
    enc_ref, a1_ref, a2_ref, s1_ref, s2_ref, raw_ref, w2_ref, wh_ref,
    g1_ref, gb1_ref, g2_ref, gb2_ref, gh_ref,
):
    @pl.when(pl.program_id(0) == 0)
    def _():
        g1_ref[...] = jnp.zeros_like(g1_ref)
        gb1_ref[...] = jnp.zeros_like(gb1_ref)
        g2_ref[...] = jnp.zeros_like(g2_ref)
        gb2_ref[...] = jnp.zeros_like(gb2_ref)
        gh_ref[...] = jnp.zeros_like(gh_ref)

    raw = raw_ref[...]
    back_second = jnp.dot(raw, wh_ref[...], preferred_element_type=jnp.float32)
    delta_second = (back_second * s2_ref[...]).astype(jnp.bfloat16)
    g2_ref[...] += lax.dot_general(
        a1_ref[...], delta_second, (((0,), (0,)), ((), ())), preferred_element_type=jnp.float32
    )
    gb2_ref[...] += jnp.sum(delta_second.astype(jnp.float32), axis=0, keepdims=True)
    back_first = lax.dot_general(
        delta_second, w2_ref[...], (((1,), (1,)), ((), ())), preferred_element_type=jnp.float32
    )
    delta_first = (back_first * s1_ref[...]).astype(jnp.bfloat16)
    g1_ref[...] += jnp.dot(enc_ref[...], delta_first, preferred_element_type=jnp.float32)
    gb1_ref[...] += jnp.sum(delta_first.astype(jnp.float32), axis=0, keepdims=True)
    gh_ref[...] += lax.dot_general(
        raw, a2_ref[...], (((0,), (0,)), ((), ())), preferred_element_type=jnp.float32
    )


BLOCK = 3072
FORWARD_BLOCK = 1536


def forward_layers(samples, fourier, params):
    first_weight, first_bias, second_weight, second_bias, head_weight, head_bias = params
    rows = samples.shape[0] * samples.shape[2]
    place = jnp.transpose(samples, (1, 0, 2)).reshape(4, rows)
    features, hidden = first_weight.shape
    heads = head_weight.shape[0]
    whole = lambda i: (0, 0)
    by_row = lambda i: (i, 0)
    by_column = lambda i: (0, i)
    return pl.pallas_call(
        forward_kernel,
        grid=(rows // FORWARD_BLOCK,),
        in_specs=[
            pl.BlockSpec((4, FORWARD_BLOCK), by_column),
            pl.BlockSpec((fourier.shape[1], fourier.shape[0]), whole),
            pl.BlockSpec(first_weight.shape, whole),
            pl.BlockSpec((1, hidden), whole),
            pl.BlockSpec(second_weight.shape, whole),
            pl.BlockSpec((1, hidden), whole),
            pl.BlockSpec(head_weight.shape, whole),
            pl.BlockSpec((heads, 1), whole),
        ],
        out_specs=[
            pl.BlockSpec((features, FORWARD_BLOCK), by_column),
            pl.BlockSpec((FORWARD_BLOCK, hidden), by_row),
            pl.BlockSpec((FORWARD_BLOCK, hidden), by_row),
            pl.BlockSpec((FORWARD_BLOCK, hidden), by_row),
            pl.BlockSpec((FORWARD_BLOCK, hidden), by_row),
            pl.BlockSpec((heads, FORWARD_BLOCK), by_column),
        ],
        out_shape=[
            jax.ShapeDtypeStruct((features, rows), jnp.bfloat16),
            jax.ShapeDtypeStruct((rows, hidden), jnp.bfloat16),
            jax.ShapeDtypeStruct((rows, hidden), jnp.bfloat16),
            jax.ShapeDtypeStruct((rows, hidden), jnp.float32),
            jax.ShapeDtypeStruct((rows, hidden), jnp.float32),
            jax.ShapeDtypeStruct((heads, rows), jnp.float32),
        ],
        compiler_params=pltpu.CompilerParams(dimension_semantics=("arbitrary",)),
    )(
        place,
        fourier.T,
        first_weight,
        first_bias.reshape(1, hidden),
        second_weight,
        second_bias.reshape(1, hidden),
        head_weight,
        head_bias.reshape(heads, 1),
    )


def network(samples, fourier, params):
    seg_count, length = (samples.shape[0], samples.shape[2])
    encoded, act_first, act_second, slope_first, slope_second, head_raw = forward_layers(
        samples, fourier, params
    )
    head_raw = head_raw.reshape(4, seg_count, length)
    density = jax.nn.softplus(head_raw[0])
    colour = jax.nn.sigmoid(head_raw[1:])
    optical = density * samples[:, 3, :]
    inclusive = jnp.cumsum(optical, axis=1)
    enter_light = jnp.exp(optical - inclusive)
    leave_light = jnp.exp(-inclusive)
    weight = enter_light - leave_light
    seg_colour = jnp.sum(weight[None] * colour, axis=2)
    seg_log = -inclusive[:, -1]
    saved = (
        encoded, act_first, act_second, slope_first, slope_second,
        head_raw, colour, weight, leave_light,
    )
    return (seg_colour, seg_log, saved)


def backward(samples, fourier, params, saved, up_colour, up_log):
    first_weight, first_bias, second_weight, second_bias, head_weight, head_bias = params
    encoded, act_first, act_second, slope_first, slope_second = saved[:5]
    head_raw, colour, weight, leave_light = saved[5:]
    up_rows = up_colour.T[:, :, None]
    energy = jnp.sum(colour * up_rows, axis=0)
    spent = weight * energy
    remaining = jnp.sum(spent, axis=1, keepdims=True) - jnp.cumsum(spent, axis=1)
    grad_optical = leave_light * energy - remaining - up_log[:, None]
    grad_density = grad_optical * samples[:, 3, :] * jax.nn.sigmoid(head_raw[0])
    grad_tint = weight[None] * up_rows * colour * (1.0 - colour)
    grad_raw = (
        jnp.concatenate([grad_density[None], grad_tint], axis=0)
        .reshape(4, -1)
        .T.astype(jnp.bfloat16)
    )
    grad_head_bias = jnp.sum(grad_raw.astype(jnp.float32), axis=0)
    rows = grad_raw.shape[0]
    features, hidden = first_weight.shape
    whole = lambda i: (0, 0)
    by_row = lambda i: (i, 0)
    outs = pl.pallas_call(
        backward_kernel,
        grid=(rows // BLOCK,),
        in_specs=[
            pl.BlockSpec((features, BLOCK), lambda i: (0, i)),
            pl.BlockSpec((BLOCK, hidden), by_row),
            pl.BlockSpec((BLOCK, hidden), by_row),
            pl.BlockSpec((BLOCK, hidden), by_row),
            pl.BlockSpec((BLOCK, hidden), by_row),
            pl.BlockSpec((BLOCK, 4), by_row),
            pl.BlockSpec(second_weight.shape, whole),
            pl.BlockSpec(head_weight.shape, whole),
        ],
        out_specs=[
            pl.BlockSpec((features, hidden), whole),
            pl.BlockSpec((1, hidden), whole),
            pl.BlockSpec((hidden, hidden), whole),
            pl.BlockSpec((1, hidden), whole),
            pl.BlockSpec((4, hidden), whole),
        ],
        out_shape=[
            jax.ShapeDtypeStruct((features, hidden), jnp.float32),
            jax.ShapeDtypeStruct((1, hidden), jnp.float32),
            jax.ShapeDtypeStruct((hidden, hidden), jnp.float32),
            jax.ShapeDtypeStruct((1, hidden), jnp.float32),
            jax.ShapeDtypeStruct((4, hidden), jnp.float32),
        ],
        compiler_params=pltpu.CompilerParams(dimension_semantics=("arbitrary",)),
    )(
        encoded, act_first, act_second, slope_first, slope_second, grad_raw,
        second_weight, head_weight,
    )
    grad_first, bias_first, grad_second, bias_second, grad_head = outs
    return (grad_first, grad_second, grad_head, bias_first[0], bias_second[0], grad_head_bias)


def composite(seg_colour, seg_log, depth_rank, pixel_rows):
    before = (depth_rank[:, None, :] < depth_rank[:, :, None]).astype(jnp.float32)
    prefix = jnp.exp(jnp.sum(before * seg_log[:, None, :], axis=2))
    up_colour = prefix[..., None] * pixel_rows[:, None, :]
    shaded = prefix * jnp.sum(seg_colour * pixel_rows[:, None, :], axis=2)
    up_log = jnp.sum(before * shaded[:, :, None], axis=1)
    return (up_colour, up_log)


def per_device(
    positions,
    spacing,
    assign,
    depth_rank,
    pixel_grad,
    fourier,
    first_weight,
    first_bias,
    second_weight,
    second_bias,
    head_weight,
    head_bias,
):
    groups = lax.axis_size("space")
    ray_count = positions.shape[1]
    total = ray_count * SEGS
    capacity = 3 * total // (2 * groups)
    slot_count = capacity * groups
    owner = assign.reshape(total)
    member = (owner[:, None] == jnp.arange(groups, dtype=jnp.int32)[None, :]).astype(jnp.int32)
    earlier = jnp.cumsum(member, axis=0) - member
    within = jnp.sum(earlier * member, axis=1)
    target = owner * capacity + within
    dispatch = (target[:, None] == jnp.arange(slot_count, dtype=jnp.int32)[None, :]).astype(
        jnp.float32
    )
    seg_pos = jnp.transpose(positions.reshape(3, total, SEG_LEN), (1, 0, 2))
    seg_gap = spacing.reshape(total, 1, SEG_LEN)
    segments = jnp.concatenate([seg_pos, seg_gap], axis=1).reshape(total, 4 * SEG_LEN)
    outgoing = lax.dot_general(
        dispatch,
        segments,
        (((0,), (0,)), ((), ())),
        precision=lax.Precision.HIGHEST,
        preferred_element_type=jnp.float32,
    )
    outgoing = outgoing.reshape(groups, capacity, 4 * SEG_LEN)
    arrived = lax.all_to_all(outgoing, "space", split_axis=0, concat_axis=0, tiled=True)
    samples = arrived.reshape(slot_count, 4, SEG_LEN)
    params = tuple(
        (
            item[0]
            for item in (
                first_weight,
                first_bias,
                second_weight,
                second_bias,
                head_weight,
                head_bias,
            )
        )
    )
    seg_colour, seg_log, saved = network(samples, fourier, params)
    partials = jnp.concatenate([seg_colour, seg_log[None, :]], axis=0).reshape(
        4, groups, capacity
    )
    returned = lax.all_to_all(partials, "space", split_axis=1, concat_axis=1, tiled=True).reshape(
        4, slot_count
    )
    mine = lax.dot_general(
        dispatch,
        returned,
        (((1,), (1,)), ((), ())),
        precision=lax.Precision.HIGHEST,
        preferred_element_type=jnp.float32,
    )
    up_colour, up_log = composite(
        mine[:, :3].reshape(ray_count, SEGS, 3),
        mine[:, 3].reshape(ray_count, SEGS),
        depth_rank,
        pixel_grad.T,
    )
    upstream = jnp.concatenate([up_colour.reshape(total, 3), up_log.reshape(total, 1)], axis=1)
    sendback = lax.dot_general(
        upstream,
        dispatch,
        (((0,), (0,)), ((), ())),
        precision=lax.Precision.HIGHEST,
        preferred_element_type=jnp.float32,
    )
    sendback = sendback.reshape(4, groups, capacity)
    received = lax.all_to_all(sendback, "space", split_axis=1, concat_axis=1, tiled=True)
    received = received.reshape(4, slot_count).T
    totals = backward(samples, fourier, params, saved, received[:, :3], received[:, 3])
    grad_first, grad_second, grad_head, bias_first, bias_second, bias_head = totals
    replicas = lax.axis_size("ray")
    hidden = bias_first.shape[0]
    heads = grad_head.shape[0]
    small = jnp.concatenate(
        [
            grad_head,
            bias_first[None],
            bias_second[None],
            jnp.pad(bias_head, (0, hidden - heads))[None],
        ],
        axis=0,
    )
    if replicas == 2:
        position = lax.axis_index("ray")
        got_first, got_second, got_small = lax.ppermute(
            (grad_first, grad_second, small), "ray", [(0, 1), (1, 0)]
        )
        rows_first = grad_first.shape[0] // 2
        rows_second = grad_second.shape[0] // 2
        part_first = lax.dynamic_slice_in_dim(
            grad_first + got_first, position * rows_first, rows_first, 0
        )
        part_second = lax.dynamic_slice_in_dim(
            grad_second + got_second, position * rows_second, rows_second, 0
        )
        small = small + got_small
    elif replicas & (replicas - 1) == 0:
        position = lax.axis_index("ray")
        part_first, part_second = grad_first, grad_second
        distance = replicas // 2
        while distance >= 1:
            pairs = [(i, i ^ distance) for i in range(replicas)]
            half = part_first.shape[0] // 2
            upper = (position // distance) % 2
            keep_first = lax.dynamic_slice_in_dim(part_first, upper * half, half, 0)
            send_first = lax.dynamic_slice_in_dim(part_first, (1 - upper) * half, half, 0)
            keep_second = lax.dynamic_slice_in_dim(part_second, upper * half, half, 0)
            send_second = lax.dynamic_slice_in_dim(part_second, (1 - upper) * half, half, 0)
            got_first, got_second, got_small = lax.ppermute(
                (send_first, send_second, small), "ray", pairs
            )
            part_first = keep_first + got_first
            part_second = keep_second + got_second
            small = small + got_small
            distance //= 2
    else:
        part_first = lax.psum_scatter(grad_first, "ray", scatter_dimension=0, tiled=True)
        part_second = lax.psum_scatter(grad_second, "ray", scatter_dimension=0, tiled=True)
        small = lax.psum(small, "ray")
    small_sums = (small[:heads], small[heads], small[heads + 1], small[heads + 2, :heads])
    return (
        part_first[None],
        part_second[None],
        small_sums[0][None],
        small_sums[1][None],
        small_sums[2][None],
        small_sums[3][None],
    )


def solution(mesh):
    placed = (
        P(None, ("space", "ray"), None),
        P(("space", "ray"), None),
        P(("space", "ray"), None, None),
        P(("space", "ray"), None),
        P(None, ("space", "ray")),
        P(),
        P("space", None, None),
        P("space", None),
        P("space", None, None),
        P("space", None),
        P("space", None, None),
        P("space", None),
    )
    return jax.shard_map(
        per_device,
        mesh=mesh,
        in_specs=placed,
        out_specs=(
            P("space", "ray", None),
            P("space", "ray", None),
            P("space", None, None),
            P("space", None),
            P("space", None),
            P("space", None),
        ),
        check_vma=False,
    )
```

```python
import jax
import jax.numpy as jnp
from jax import lax
from jax.sharding import PartitionSpec as P
from jax.experimental import pallas as pl
from jax.experimental.pallas import tpu as pltpu

SEG_LEN = 32
SEGS = 8


two_pi = 6.283185307179586


def gate_of(value):
    return 0.5 * jnp.tanh(0.5 * value) + 0.5


def silu_slope(value):
    gate = gate_of(value)
    return gate * (1.0 + value * (1.0 - gate))


def turn_sin_cos(turns):
    quarter = jnp.floor(turns * 4.0 + 0.5)
    angle = (turns - quarter * 0.25) * two_pi
    square = angle * angle
    sine = angle * (
        1.0 + square * (-1.0 / 6.0 + square * (1.0 / 120.0 + square * (-1.0 / 5040.0)))
    )
    cosine = 1.0 + square * (
        -0.5 + square * (1.0 / 24.0 + square * (-1.0 / 720.0 + square * (1.0 / 40320.0)))
    )
    step = quarter - 4.0 * jnp.floor(quarter * 0.25)
    flip = step >= 2.0
    odd = (step == 1.0) | (step == 3.0)
    sin_out = jnp.where(odd, cosine, sine)
    cos_out = jnp.where(odd, sine, cosine)
    sin_out = jnp.where(flip, -sin_out, sin_out)
    cos_out = jnp.where(flip != odd, -cos_out, cos_out)
    return sin_out, cos_out


def encode(samples, fourier):
    turns = (
        samples[:, 0, :, None] * fourier[0]
        + samples[:, 1, :, None] * fourier[1]
        + samples[:, 2, :, None] * fourier[2]
    )
    sine, cosine = turn_sin_cos(turns)
    joined = jnp.concatenate([sine, cosine], axis=-1)
    return joined.astype(jnp.bfloat16).reshape(-1, joined.shape[-1])


def forward_kernel(
    place_ref, fourier_ref, w1_ref, b1_ref, w2_ref, b2_ref, wh_ref, bh_ref,
    enc_ref, a1_ref, a2_ref, s1_ref, s2_ref, head_ref,
):
    place = place_ref[...]
    fourier = fourier_ref[...]
    turns = (
        fourier[:, 0:1] * place[0:1, :]
        + fourier[:, 1:2] * place[1:2, :]
        + fourier[:, 2:3] * place[2:3, :]
    )
    sine, cosine = turn_sin_cos(turns)
    encoded = jnp.concatenate([sine, cosine], axis=0).astype(jnp.bfloat16)
    enc_ref[...] = encoded
    pre_first = (
        lax.dot_general(
            encoded, w1_ref[...], (((0,), (0,)), ((), ())), preferred_element_type=jnp.float32
        )
        + b1_ref[...]
    )
    gate_first = gate_of(pre_first)
    act_first = (pre_first * gate_first).astype(jnp.bfloat16)
    a1_ref[...] = act_first
    s1_ref[...] = gate_first * (1.0 + pre_first * (1.0 - gate_first))
    pre_second = jnp.dot(act_first, w2_ref[...], preferred_element_type=jnp.float32) + b2_ref[...]
    gate_second = gate_of(pre_second)
    act_second = (pre_second * gate_second).astype(jnp.bfloat16)
    a2_ref[...] = act_second
    s2_ref[...] = gate_second * (1.0 + pre_second * (1.0 - gate_second))
    head_ref[...] = (
        lax.dot_general(
            wh_ref[...], act_second, (((1,), (1,)), ((), ())), preferred_element_type=jnp.float32
        )
        + bh_ref[...]
    )


def backward_kernel(
    enc_ref, a1_ref, a2_ref, s1_ref, s2_ref, raw_ref, w2_ref, wh_ref,
    g1_ref, gb1_ref, g2_ref, gb2_ref, gh_ref,
):
    @pl.when(pl.program_id(0) == 0)
    def _():
        g1_ref[...] = jnp.zeros_like(g1_ref)
        gb1_ref[...] = jnp.zeros_like(gb1_ref)
        g2_ref[...] = jnp.zeros_like(g2_ref)
        gb2_ref[...] = jnp.zeros_like(gb2_ref)
        gh_ref[...] = jnp.zeros_like(gh_ref)

    raw = raw_ref[...]
    back_second = jnp.dot(raw, wh_ref[...], preferred_element_type=jnp.float32)
    delta_second = (back_second * s2_ref[...]).astype(jnp.bfloat16)
    g2_ref[...] += lax.dot_general(
        a1_ref[...], delta_second, (((0,), (0,)), ((), ())), preferred_element_type=jnp.float32
    )
    gb2_ref[...] += jnp.sum(delta_second.astype(jnp.float32), axis=0, keepdims=True)
    back_first = lax.dot_general(
        delta_second, w2_ref[...], (((1,), (1,)), ((), ())), preferred_element_type=jnp.float32
    )
    delta_first = (back_first * s1_ref[...]).astype(jnp.bfloat16)
    g1_ref[...] += jnp.dot(enc_ref[...], delta_first, preferred_element_type=jnp.float32)
    gb1_ref[...] += jnp.sum(delta_first.astype(jnp.float32), axis=0, keepdims=True)
    gh_ref[...] += lax.dot_general(
        raw, a2_ref[...], (((0,), (0,)), ((), ())), preferred_element_type=jnp.float32
    )


BLOCK = 6144
FORWARD_BLOCK = 1024


def forward_layers(samples, fourier, params):
    first_weight, first_bias, second_weight, second_bias, head_weight, head_bias = params
    rows = samples.shape[0] * samples.shape[2]
    place = jnp.transpose(samples, (1, 0, 2)).reshape(4, rows)
    features, hidden = first_weight.shape
    heads = head_weight.shape[0]
    whole = lambda i: (0, 0)
    by_row = lambda i: (i, 0)
    by_column = lambda i: (0, i)
    return pl.pallas_call(
        forward_kernel,
        grid=(rows // FORWARD_BLOCK,),
        in_specs=[
            pl.BlockSpec((4, FORWARD_BLOCK), by_column),
            pl.BlockSpec((fourier.shape[1], fourier.shape[0]), whole),
            pl.BlockSpec(first_weight.shape, whole),
            pl.BlockSpec((1, hidden), whole),
            pl.BlockSpec(second_weight.shape, whole),
            pl.BlockSpec((1, hidden), whole),
            pl.BlockSpec(head_weight.shape, whole),
            pl.BlockSpec((heads, 1), whole),
        ],
        out_specs=[
            pl.BlockSpec((features, FORWARD_BLOCK), by_column),
            pl.BlockSpec((FORWARD_BLOCK, hidden), by_row),
            pl.BlockSpec((FORWARD_BLOCK, hidden), by_row),
            pl.BlockSpec((FORWARD_BLOCK, hidden), by_row),
            pl.BlockSpec((FORWARD_BLOCK, hidden), by_row),
            pl.BlockSpec((heads, FORWARD_BLOCK), by_column),
        ],
        out_shape=[
            jax.ShapeDtypeStruct((features, rows), jnp.bfloat16),
            jax.ShapeDtypeStruct((rows, hidden), jnp.bfloat16),
            jax.ShapeDtypeStruct((rows, hidden), jnp.bfloat16),
            jax.ShapeDtypeStruct((rows, hidden), jnp.float32),
            jax.ShapeDtypeStruct((rows, hidden), jnp.float32),
            jax.ShapeDtypeStruct((heads, rows), jnp.float32),
        ],
        compiler_params=pltpu.CompilerParams(dimension_semantics=("arbitrary",)),
    )(
        place,
        fourier.T,
        first_weight,
        first_bias.reshape(1, hidden),
        second_weight,
        second_bias.reshape(1, hidden),
        head_weight,
        head_bias.reshape(heads, 1),
    )


def network(samples, fourier, params):
    seg_count, length = (samples.shape[0], samples.shape[2])
    encoded, act_first, act_second, slope_first, slope_second, head_raw = forward_layers(
        samples, fourier, params
    )
    head_raw = head_raw.reshape(4, seg_count, length)
    density = jax.nn.softplus(head_raw[0])
    colour = jax.nn.sigmoid(head_raw[1:])
    optical = density * samples[:, 3, :]
    inclusive = jnp.cumsum(optical, axis=1)
    enter_light = jnp.exp(optical - inclusive)
    leave_light = jnp.exp(-inclusive)
    weight = enter_light - leave_light
    seg_colour = jnp.sum(weight[None] * colour, axis=2)
    seg_log = -inclusive[:, -1]
    saved = (
        encoded, act_first, act_second, slope_first, slope_second,
        head_raw, colour, weight, leave_light,
    )
    return (seg_colour, seg_log, saved)


def backward(samples, fourier, params, saved, up_colour, up_log):
    first_weight, first_bias, second_weight, second_bias, head_weight, head_bias = params
    encoded, act_first, act_second, slope_first, slope_second = saved[:5]
    head_raw, colour, weight, leave_light = saved[5:]
    up_rows = up_colour.T[:, :, None]
    energy = jnp.sum(colour * up_rows, axis=0)
    spent = weight * energy
    remaining = jnp.sum(spent, axis=1, keepdims=True) - jnp.cumsum(spent, axis=1)
    grad_optical = leave_light * energy - remaining - up_log[:, None]
    grad_density = grad_optical * samples[:, 3, :] * jax.nn.sigmoid(head_raw[0])
    grad_tint = weight[None] * up_rows * colour * (1.0 - colour)
    grad_raw = (
        jnp.concatenate([grad_density[None], grad_tint], axis=0)
        .reshape(4, -1)
        .T.astype(jnp.bfloat16)
    )
    grad_head_bias = jnp.sum(grad_raw.astype(jnp.float32), axis=0)
    rows = grad_raw.shape[0]
    features, hidden = first_weight.shape
    whole = lambda i: (0, 0)
    by_row = lambda i: (i, 0)
    outs = pl.pallas_call(
        backward_kernel,
        grid=(rows // BLOCK,),
        in_specs=[
            pl.BlockSpec((features, BLOCK), lambda i: (0, i)),
            pl.BlockSpec((BLOCK, hidden), by_row),
            pl.BlockSpec((BLOCK, hidden), by_row),
            pl.BlockSpec((BLOCK, hidden), by_row),
            pl.BlockSpec((BLOCK, hidden), by_row),
            pl.BlockSpec((BLOCK, 4), by_row),
            pl.BlockSpec(second_weight.shape, whole),
            pl.BlockSpec(head_weight.shape, whole),
        ],
        out_specs=[
            pl.BlockSpec((features, hidden), whole),
            pl.BlockSpec((1, hidden), whole),
            pl.BlockSpec((hidden, hidden), whole),
            pl.BlockSpec((1, hidden), whole),
            pl.BlockSpec((4, hidden), whole),
        ],
        out_shape=[
            jax.ShapeDtypeStruct((features, hidden), jnp.float32),
            jax.ShapeDtypeStruct((1, hidden), jnp.float32),
            jax.ShapeDtypeStruct((hidden, hidden), jnp.float32),
            jax.ShapeDtypeStruct((1, hidden), jnp.float32),
            jax.ShapeDtypeStruct((4, hidden), jnp.float32),
        ],
        compiler_params=pltpu.CompilerParams(dimension_semantics=("arbitrary",)),
    )(
        encoded, act_first, act_second, slope_first, slope_second, grad_raw,
        second_weight, head_weight,
    )
    grad_first, bias_first, grad_second, bias_second, grad_head = outs
    return (grad_first, grad_second, grad_head, bias_first[0], bias_second[0], grad_head_bias)


def composite(seg_colour, seg_log, depth_rank, pixel_rows):
    before = (depth_rank[:, None, :] < depth_rank[:, :, None]).astype(jnp.float32)
    prefix = jnp.exp(jnp.sum(before * seg_log[:, None, :], axis=2))
    up_colour = prefix[..., None] * pixel_rows[:, None, :]
    shaded = prefix * jnp.sum(seg_colour * pixel_rows[:, None, :], axis=2)
    up_log = jnp.sum(before * shaded[:, :, None], axis=1)
    return (up_colour, up_log)


def per_device(
    positions,
    spacing,
    assign,
    depth_rank,
    pixel_grad,
    fourier,
    first_weight,
    first_bias,
    second_weight,
    second_bias,
    head_weight,
    head_bias,
):
    groups = lax.axis_size("space")
    ray_count = positions.shape[1]
    total = ray_count * SEGS
    capacity = 3 * total // (2 * groups)
    slot_count = capacity * groups
    owner = assign.reshape(total)
    member = (owner[:, None] == jnp.arange(groups, dtype=jnp.int32)[None, :]).astype(jnp.int32)
    earlier = jnp.cumsum(member, axis=0) - member
    within = jnp.sum(earlier * member, axis=1)
    target = owner * capacity + within
    dispatch = (target[:, None] == jnp.arange(slot_count, dtype=jnp.int32)[None, :]).astype(
        jnp.float32
    )
    seg_pos = jnp.transpose(positions.reshape(3, total, SEG_LEN), (1, 0, 2))
    seg_gap = spacing.reshape(total, 1, SEG_LEN)
    segments = jnp.concatenate([seg_pos, seg_gap], axis=1).reshape(total, 4 * SEG_LEN)
    outgoing = lax.dot_general(
        dispatch,
        segments,
        (((0,), (0,)), ((), ())),
        precision=lax.Precision.HIGHEST,
        preferred_element_type=jnp.float32,
    )
    outgoing = outgoing.reshape(groups, capacity, 4 * SEG_LEN)
    arrived = lax.all_to_all(outgoing, "space", split_axis=0, concat_axis=0, tiled=True)
    samples = arrived.reshape(slot_count, 4, SEG_LEN)
    params = tuple(
        (
            item[0]
            for item in (
                first_weight,
                first_bias,
                second_weight,
                second_bias,
                head_weight,
                head_bias,
            )
        )
    )
    seg_colour, seg_log, saved = network(samples, fourier, params)
    partials = jnp.concatenate([seg_colour, seg_log[None, :]], axis=0).reshape(
        4, groups, capacity
    )
    returned = lax.all_to_all(partials, "space", split_axis=1, concat_axis=1, tiled=True).reshape(
        4, slot_count
    )
    mine = lax.dot_general(
        dispatch,
        returned,
        (((1,), (1,)), ((), ())),
        precision=lax.Precision.HIGHEST,
        preferred_element_type=jnp.float32,
    )
    up_colour, up_log = composite(
        mine[:, :3].reshape(ray_count, SEGS, 3),
        mine[:, 3].reshape(ray_count, SEGS),
        depth_rank,
        pixel_grad.T,
    )
    upstream = jnp.concatenate([up_colour.reshape(total, 3), up_log.reshape(total, 1)], axis=1)
    sendback = lax.dot_general(
        upstream,
        dispatch,
        (((0,), (0,)), ((), ())),
        precision=lax.Precision.HIGHEST,
        preferred_element_type=jnp.float32,
    )
    sendback = sendback.reshape(4, groups, capacity)
    received = lax.all_to_all(sendback, "space", split_axis=1, concat_axis=1, tiled=True)
    received = received.reshape(4, slot_count).T
    totals = backward(samples, fourier, params, saved, received[:, :3], received[:, 3])
    grad_first, grad_second, grad_head, bias_first, bias_second, bias_head = totals
    replicas = lax.axis_size("ray")
    hidden = bias_first.shape[0]
    heads = grad_head.shape[0]
    small = jnp.concatenate(
        [
            grad_head,
            bias_first[None],
            bias_second[None],
            jnp.pad(bias_head, (0, hidden - heads))[None],
        ],
        axis=0,
    )
    if replicas == 2:
        position = lax.axis_index("ray")
        got_first, got_second, got_small = lax.ppermute(
            (grad_first, grad_second, small), "ray", [(0, 1), (1, 0)]
        )
        rows_first = grad_first.shape[0] // 2
        rows_second = grad_second.shape[0] // 2
        part_first = lax.dynamic_slice_in_dim(
            grad_first + got_first, position * rows_first, rows_first, 0
        )
        part_second = lax.dynamic_slice_in_dim(
            grad_second + got_second, position * rows_second, rows_second, 0
        )
        small = small + got_small
    elif replicas & (replicas - 1) == 0:
        position = lax.axis_index("ray")
        part_first, part_second = grad_first, grad_second
        distance = replicas // 2
        while distance >= 1:
            pairs = [(i, i ^ distance) for i in range(replicas)]
            half = part_first.shape[0] // 2
            upper = (position // distance) % 2
            keep_first = lax.dynamic_slice_in_dim(part_first, upper * half, half, 0)
            send_first = lax.dynamic_slice_in_dim(part_first, (1 - upper) * half, half, 0)
            keep_second = lax.dynamic_slice_in_dim(part_second, upper * half, half, 0)
            send_second = lax.dynamic_slice_in_dim(part_second, (1 - upper) * half, half, 0)
            got_first, got_second, got_small = lax.ppermute(
                (send_first, send_second, small), "ray", pairs
            )
            part_first = keep_first + got_first
            part_second = keep_second + got_second
            small = small + got_small
            distance //= 2
    else:
        part_first = lax.psum_scatter(grad_first, "ray", scatter_dimension=0, tiled=True)
        part_second = lax.psum_scatter(grad_second, "ray", scatter_dimension=0, tiled=True)
        small = lax.psum(small, "ray")
    small_sums = (small[:heads], small[heads], small[heads + 1], small[heads + 2, :heads])
    return (
        part_first[None],
        part_second[None],
        small_sums[0][None],
        small_sums[1][None],
        small_sums[2][None],
        small_sums[3][None],
    )


def solution(mesh):
    placed = (
        P(None, ("space", "ray"), None),
        P(("space", "ray"), None),
        P(("space", "ray"), None, None),
        P(("space", "ray"), None),
        P(None, ("space", "ray")),
        P(),
        P("space", None, None),
        P("space", None),
        P("space", None, None),
        P("space", None),
        P("space", None, None),
        P("space", None),
    )
    return jax.shard_map(
        per_device,
        mesh=mesh,
        in_specs=placed,
        out_specs=(
            P("space", "ray", None),
            P("space", "ray", None),
            P("space", None, None),
            P("space", None),
            P("space", None),
            P("space", None),
        ),
        check_vma=False,
    )
```
